32 devices in a mesh: sec: 8 (over z, y), strip: 4 (over x, core).
Axes of the slice: x: 2, y: 2, z: 4, core: 2. Of those that a mesh axis runs over, the one named last changes fastest.
Arguments:
- images: bfloat16 [8, 2048, 2048], P('sec', 'strip'), may hold values from -8 to 8
- offsets: int32 [25, 2], replicated, may hold values from -3 to 3, as said below
- springs: int32 [2, 8, 512, 512], P(None, 'sec', 'strip'), may hold values from 1 to 8
- validity: int32 [8, 512, 512], P('sec', 'strip'), may hold values 0 or 1
Outputs:
- relaxed: float32 [2, 8, 512, 512], P(None, 'sec', 'strip')
The draws below stay inside these ranges and needn't reach their ends.
Inputs may be any that keep to these rules, and one draw needn't show every extreme that they name: `offsets`: 25 distinct displacements; among them (0, 0), (-3, -3) and (3, 3).
All inputs are finite; a program needn't handle non-finite values. No bound on the sum of `validity` on one device may be relied on, other than what follows from the above.
Results may differ from the reference program's by a relative error of at most 0.0015.
Values may be sent and summed in bfloat16 or wider, within the bound.
No kernel may reach another device: no remote copies, remote signals or barrier semaphores. Data moves between devices by JAX's collectives and lax.ppermute only.
A program may use at most 128 MiB of HBM per device.

```python
import jax
import jax.numpy as jnp
import numpy as np
from jax import lax

WIDTH = 2048
RAD = 3
NOFF = 25
ITERS = 8
SECTIONS = 8
HEIGHT = 2048
NODE_ROWS = 512
NODE_COLS = 512


def draw_images(key, part):
    full_shape = (SECTIONS, HEIGHT, WIDTH)
    own_key = jax.random.fold_in(jax.random.fold_in(key, 11), 0)
    own_part = jax.random.normal(own_key, full_shape, jnp.float32)
    return jnp.clip(own_part, -6.0, 6.0).astype(jnp.bfloat16)


def draw_offsets(key, part):
    extent = 2 * RAD + 1
    cells = extent * extent
    anchors = [cells // 2, 0, cells - 1]
    remaining = np.array([entry for entry in range(cells) if entry not in anchors], dtype=np.int32)
    chosen = jax.random.permutation(jax.random.fold_in(key, 23), remaining.shape[0])[:NOFF - 3]
    selected = jnp.concatenate([jnp.array(anchors, jnp.int32), jnp.asarray(remaining)[chosen]])
    return jnp.stack([selected // extent - RAD, selected % extent - RAD], axis=1).astype(jnp.int32)


def place_ends(values, rng, least, high):
    dims = values.shape
    index_at = [jax.random.randint(jax.random.fold_in(rng, axis), (), 0, dims[axis]) for axis in range(len(dims))]
    values = values.at[tuple(index_at)].set(least)
    longest = dims.index(max(dims))
    index_at[longest] = (index_at[longest] + 1) % dims[longest]
    return values.at[tuple(index_at)].set(high)


def setup_inputs(seed: int = 0) -> dict:
    key_of = jax.random.split(jax.random.key(seed), 5)
    images = draw_images(jax.random.fold_in(key_of[4], 71), 0)
    offsets = draw_offsets(jax.random.fold_in(key_of[4], 71), 0)
    springs = place_ends(jax.random.randint(key_of[2], (2, SECTIONS, NODE_ROWS, NODE_COLS), 1, 9), jax.random.fold_in(key_of[2], 1), 1, 8).astype(jnp.int32)
    validity = place_ends((jax.random.randint(key_of[3], (SECTIONS, NODE_ROWS, NODE_COLS), 0, 4) < 3).astype(jnp.int32), jax.random.fold_in(key_of[3], 1), 0, 1)
    return dict(images=images, offsets=offsets, springs=springs, validity=validity)


sharpness = 0.5
relax_rate = 0.8


def section_flow(current, padded, offsets):
    row_count, col_count = current.shape
    current_f = current.astype(jnp.float32)

    def one_offset(offset):
        shifted = lax.dynamic_slice(padded, (RAD + offset[0], RAD + offset[1]), (row_count, col_count)).astype(jnp.float32)
        product = current_f * shifted
        return sharpness * product.reshape(row_count // 4, 4, col_count // 4, 4).sum(axis=(1, 3))

    scores = lax.map(one_offset, offsets)
    highest = jnp.max(scores, axis=0)
    soft_weights = jnp.exp(scores - highest)
    weight_sum = jnp.sum(soft_weights, axis=0)
    shifts = offsets.astype(jnp.float32)
    flow_row = jnp.sum(soft_weights * shifts[:, 0, None, None], axis=0) / weight_sum
    flow_col = jnp.sum(soft_weights * shifts[:, 1, None, None], axis=0) / weight_sum
    return jnp.stack([flow_row, flow_col])


def advance(positions, from_below, from_above, from_right, from_left, row_weight, weight_up, col_weight, weight_left, pull_term, pull_prior, diagonal):
    force = row_weight * (from_below - positions) + weight_up * (from_above - positions)
    force = force + col_weight * (from_right - positions) + weight_left * (from_left - positions)
    force = force + pull_term - pull_prior
    return positions + relax_rate * force / (1.0 + diagonal)


def reference(images, offsets, springs, validity):
    section_count = images.shape[0]
    extended = jnp.concatenate([images, jnp.zeros_like(images[:1])], axis=0)
    extended = jnp.pad(extended, ((0, 0), (RAD, RAD), (RAD, RAD)))

    def per_section(section):
        current = lax.dynamic_index_in_dim(extended, section, 0, keepdims=False)[RAD:-RAD, RAD:-RAD]
        padded = lax.dynamic_index_in_dim(extended, section + 1, 0, keepdims=False)
        return section_flow(current, padded, offsets)

    flows = lax.map(per_section, jnp.arange(section_count, dtype=jnp.int32))
    keep_mask = (jnp.arange(section_count) < section_count - 1).astype(jnp.float32)
    flow_field = jnp.transpose(flows, (1, 0, 2, 3)) * keep_mask[None, :, None, None]
    node_rows, node_cols = flow_field.shape[2], flow_field.shape[3]
    row_keep = (jnp.arange(node_rows) < node_rows - 1).astype(jnp.float32)
    col_keep = (jnp.arange(node_cols) < node_cols - 1).astype(jnp.float32)
    row_weight = 0.25 * springs[0].astype(jnp.float32) * row_keep[None, :, None]
    col_weight = 0.25 * springs[1].astype(jnp.float32) * col_keep[None, None, :]
    match_weight = validity.astype(jnp.float32) * keep_mask[:, None, None]
    weight_up = jnp.pad(row_weight, ((0, 0), (1, 0), (0, 0)))[:, :-1]
    weight_left = jnp.pad(col_weight, ((0, 0), (0, 0), (1, 0)))[:, :, :-1]
    match_prior = jnp.pad(match_weight, ((1, 0), (0, 0), (0, 0)))[:-1]
    diagonal = row_weight + weight_up + col_weight + weight_left + match_weight + match_prior
    positions = jnp.zeros_like(flow_field)
    for iteration in range(ITERS):
        padded = jnp.pad(positions, ((0, 0), (0, 0), (1, 1), (1, 1)))
        following = jnp.pad(positions, ((0, 0), (0, 1), (0, 0), (0, 0)))[:, 1:]
        pull_term = match_weight * (following - positions - flow_field)
        pull_prior = jnp.pad(pull_term, ((0, 0), (1, 0), (0, 0), (0, 0)))[:, :-1]
        positions = advance(positions, padded[:, :, 2:, 1:-1], padded[:, :, :-2, 1:-1], padded[:, :, 1:-1, 2:], padded[:, :, 1:-1, :-2], row_weight, weight_up, col_weight, weight_left, pull_term, pull_prior, diagonal)
    return positions
```

```python
import jax
import jax.numpy as jnp
from jax import lax
from jax.sharding import PartitionSpec as P

RAD = 3
ITERS = 8


sharpness = 0.5
relax_rate = 0.8


def shifted_2(shard, axis, by):
    size = lax.axis_size(axis)
    pairs = [(i, i + by) for i in range(size) if 0 <= i + by < size]
    return lax.ppermute(shard, axis, pairs)


def extended(cells, sides, width):
    for axis, dim in sides:
        count = lax.axis_size(axis)
        ends = count - 1
        head = lax.slice_in_dim(cells, 0, width, axis=dim)
        tail = lax.slice_in_dim(cells, cells.shape[dim] - width, cells.shape[dim], axis=dim)
        cells = jnp.concatenate(
            [
                lax.ppermute(tail, axis, [(i, (i + 1) % count) for i in range(ends)]),
                cells,
                lax.ppermute(head, axis, [((i + 1) % count, i) for i in range(ends)]),
            ],
            axis=dim,
        )
    return cells


def section_flow(current, padded, offsets):
    row_count, col_count = current.shape
    current_f = current.astype(jnp.float32)
    column_ids = jnp.arange(col_count, dtype=jnp.int32)[:, None] // 4
    node_ids = jnp.arange(col_count // 4, dtype=jnp.int32)[None, :]
    pooling = (column_ids == node_ids).astype(jnp.float32)

    def one_offset(offset):
        shifted = lax.dynamic_slice(
            padded, (RAD + offset[0], RAD + offset[1]), (row_count, col_count)
        ).astype(jnp.float32)
        product = current_f * shifted
        row_pooled = product.reshape(row_count // 4, 4, col_count).sum(axis=1)
        return sharpness * jnp.dot(
            row_pooled, pooling, precision=lax.Precision.HIGHEST, preferred_element_type=jnp.float32
        )

    scores = lax.map(one_offset, offsets)
    highest = jnp.max(scores, axis=0)
    soft_weights = jnp.exp(scores - highest)
    weight_sum = jnp.sum(soft_weights, axis=0)
    shifts = offsets.astype(jnp.float32)
    flow_row = jnp.sum(soft_weights * shifts[:, 0, None, None], axis=0) / weight_sum
    flow_col = jnp.sum(soft_weights * shifts[:, 1, None, None], axis=0) / weight_sum
    return jnp.stack([flow_row, flow_col])


def advance(
    positions,
    from_below,
    from_above,
    from_right,
    from_left,
    row_weight,
    weight_up,
    col_weight,
    weight_left,
    pull_term,
    pull_prior,
    diagonal,
):
    force = row_weight * (from_below - positions) + weight_up * (from_above - positions)
    force = force + col_weight * (from_right - positions) + weight_left * (from_left - positions)
    force = force + pull_term - pull_prior
    return positions + relax_rate * force / (1.0 + diagonal)


def shards(images, offsets, springs, validity):
    successor = shifted_2(images, "sec", -1)
    rimmed = extended(successor, (("strip", 1),), RAD)
    padded = jnp.pad(rimmed[0], ((0, 0), (RAD, RAD)))
    flow_field = section_flow(images[0], padded, offsets)
    keep_mask = (lax.axis_index("sec") < lax.axis_size("sec") - 1).astype(jnp.float32)
    flow_field = flow_field * keep_mask
    node_rows, node_cols = (flow_field.shape[1], flow_field.shape[2])
    global_rows = lax.axis_index("strip") * node_rows + jnp.arange(node_rows, dtype=jnp.int32)
    row_keep = (global_rows < node_rows * lax.axis_size("strip") - 1).astype(jnp.float32)
    col_keep = (jnp.arange(node_cols) < node_cols - 1).astype(jnp.float32)
    row_weight = 0.25 * springs[0, 0].astype(jnp.float32) * row_keep[:, None]
    col_weight = 0.25 * springs[1, 0].astype(jnp.float32) * col_keep[None, :]
    match_weight = validity[0].astype(jnp.float32) * keep_mask
    stacked = jnp.stack([flow_field[0], flow_field[1], row_weight, col_weight, match_weight])
    stacked = jnp.transpose(stacked, (0, 2, 1))[:, None]
    tiled = lax.all_to_all(stacked, "sec", split_axis=2, concat_axis=1, tiled=True)
    halo = ITERS
    haloed = extended(tiled, (("sec", 2), ("strip", 3)), halo)
    flow_tiles = haloed[0:2]
    tile_row = haloed[2]
    tile_col = haloed[3]
    tile_match = haloed[4]
    weight_up = jnp.pad(tile_row, ((0, 0), (0, 0), (1, 0)))[:, :, :-1]
    weight_left = jnp.pad(tile_col, ((0, 0), (1, 0), (0, 0)))[:, :-1, :]
    match_prior = jnp.pad(tile_match, ((1, 0), (0, 0), (0, 0)))[:-1]
    diagonal = tile_row + weight_up + tile_col + weight_left + tile_match + match_prior
    positions = jnp.zeros_like(flow_tiles)
    for iteration in range(ITERS):
        padded = jnp.pad(positions, ((0, 0), (0, 0), (1, 1), (1, 1)))
        following = jnp.pad(positions, ((0, 0), (0, 1), (0, 0), (0, 0)))[:, 1:]
        pull_term = tile_match * (following - positions - flow_tiles)
        pull_prior = jnp.pad(pull_term, ((0, 0), (1, 0), (0, 0), (0, 0)))[:, :-1]
        positions = advance(
            positions,
            padded[:, :, 1:-1, 2:],
            padded[:, :, 1:-1, :-2],
            padded[:, :, 2:, 1:-1],
            padded[:, :, :-2, 1:-1],
            tile_row,
            weight_up,
            tile_col,
            weight_left,
            pull_term,
            pull_prior,
            diagonal,
        )
    core = positions[:, :, halo:-halo, halo:-halo]
    returned = lax.all_to_all(core, "sec", split_axis=1, concat_axis=2, tiled=True)
    return jnp.transpose(returned, (0, 1, 3, 2))


def solution(mesh):
    in_specs = (
        P("sec", "strip", None),
        P(),
        P(None, "sec", "strip", None),
        P("sec", "strip", None),
    )
    out_specs = P(None, "sec", "strip", None)
    return jax.shard_map(shards, mesh=mesh, in_specs=in_specs, out_specs=out_specs, check_vma=False)
```

```python
import jax
import jax.numpy as jnp
from jax import lax
from jax.experimental import pallas as pl
from jax.experimental.pallas import tpu as pltpu
from jax.sharding import PartitionSpec as P

RAD = 3
ITERS = 8


sharpness = 0.5
relax_rate = 0.8


def shifted_2(shard, axis, by):
    size = lax.axis_size(axis)
    pairs = [(i, i + by) for i in range(size) if 0 <= i + by < size]
    return lax.ppermute(shard, axis, pairs)


def extended(cells, sides, width):
    for axis, dim in sides:
        count = lax.axis_size(axis)
        ends = count - 1
        head = lax.slice_in_dim(cells, 0, width, axis=dim)
        tail = lax.slice_in_dim(cells, cells.shape[dim] - width, cells.shape[dim], axis=dim)
        cells = jnp.concatenate(
            [
                lax.ppermute(tail, axis, [(i, (i + 1) % count) for i in range(ends)]),
                cells,
                lax.ppermute(head, axis, [((i + 1) % count, i) for i in range(ends)]),
            ],
            axis=dim,
        )
    return cells


def phases(pixels, node_rows, node_cols):
    chunks = node_cols // 128
    source = jnp.arange(512, dtype=jnp.int32)[:, None]
    target = jnp.arange(512, dtype=jnp.int32)[None, :]
    permute = ((source % 4) * 128 + source // 4 == target).astype(pixels.dtype)
    lanes = jnp.einsum(
        "rcl,lm->rcm", pixels.reshape(node_rows * 4, chunks, 512), permute, preferred_element_type=jnp.float32
    )
    split = lanes.reshape(node_rows, 4, chunks, 4, 128)
    return jnp.transpose(split, (1, 3, 0, 2, 4)).reshape(16, node_rows, node_cols)


def flow_kernel(offsets_ref, current_ref, following_ref, flow_ref, shifted_ref, scores_ref):
    tile_rows = current_ref.shape[1]
    node_cols = current_ref.shape[2]
    window = tile_rows + 8
    base = pl.multiple_of(pl.program_id(0) * tile_rows, 8)

    def build(phase, carry):
        block = following_ref[phase, pl.ds(base, window), :]
        width = block.shape[1]
        for col_shift in range(3):
            moved = block if col_shift == 0 else pltpu.roll(block, width - col_shift, 1)
            moved = moved[:, :node_cols]
            for row_shift in range(3):
                rows = moved if row_shift == 0 else pltpu.roll(moved, window - row_shift, 0)
                shifted_ref[(row_shift * 3 + col_shift) * 16 + phase] = rows[:tile_rows]
        return carry

    lax.fori_loop(0, 16, build, 0)
    chunks = tile_rows // 8
    offset_count = scores_ref.shape[0]

    def score(k, carry):
        row_off = offsets_ref[k, 0]
        col_off = offsets_ref[k, 1]
        sources = []
        for q in range(4):
            u = q + row_off + 4
            u_node, u_phase = lax.shift_right_logical(u, 2), u & 3
            for t in range(4):
                v = t + col_off + 4
                v_node, v_phase = lax.shift_right_logical(v, 2), v & 3
                sources.append((u_node * 3 + v_node) * 16 + u_phase * 4 + v_phase)
        for c in range(chunks):
            rows = pl.ds(c * 8, 8)
            acc = current_ref[0, rows, :] * shifted_ref[sources[0], rows, :]
            for p in range(1, 16):
                acc = acc + current_ref[p, rows, :] * shifted_ref[sources[p], rows, :]
            scores_ref[k, rows, :] = sharpness * acc
        return carry

    lax.fori_loop(0, offset_count, score, 0)
    for c in range(chunks):
        rows = pl.ds(c * 8, 8)
        highest = scores_ref[0, rows, :]
        for k in range(1, offset_count):
            highest = jnp.maximum(highest, scores_ref[k, rows, :])
        weight_sum = jnp.zeros_like(highest)
        row_sum = jnp.zeros_like(highest)
        col_sum = jnp.zeros_like(highest)
        for k in range(offset_count):
            weight = jnp.exp(scores_ref[k, rows, :] - highest)
            weight_sum = weight_sum + weight
            row_sum = row_sum + weight * offsets_ref[k, 0].astype(jnp.float32)
            col_sum = col_sum + weight * offsets_ref[k, 1].astype(jnp.float32)
        flow_ref[0, rows, :] = row_sum / weight_sum
        flow_ref[1, rows, :] = col_sum / weight_sum


def section_flow(current, following, offsets, tile_rows=32):
    row_count, col_count = current.shape
    node_rows, node_cols = row_count // 4, col_count // 4
    current_ph = phases(current, node_rows, node_cols)
    lane_nodes = -(-(node_cols + 2) // 128) * 128
    row_nodes = node_rows + 8
    padded = jnp.pad(
        following,
        ((4 - RAD, row_nodes * 4 - following.shape[0] - (4 - RAD)), (4, lane_nodes * 4 - col_count - 4)),
    )
    following_ph = phases(padded, row_nodes, lane_nodes)
    offset_count = offsets.shape[0]
    grid_spec = pltpu.PrefetchScalarGridSpec(
        num_scalar_prefetch=1,
        grid=(node_rows // tile_rows,),
        in_specs=[
            pl.BlockSpec((16, tile_rows, node_cols), lambda g, off: (0, g, 0)),
            pl.BlockSpec((16, row_nodes, lane_nodes), lambda g, off: (0, 0, 0)),
        ],
        out_specs=pl.BlockSpec((2, tile_rows, node_cols), lambda g, off: (0, g, 0)),
        scratch_shapes=[
            pltpu.VMEM((144, tile_rows, node_cols), jnp.float32),
            pltpu.VMEM((offset_count, tile_rows, node_cols), jnp.float32),
        ],
    )
    return pl.pallas_call(
        flow_kernel,
        grid_spec=grid_spec,
        out_shape=jax.ShapeDtypeStruct((2, node_rows, node_cols), jnp.float32),
        compiler_params=pltpu.CompilerParams(
            dimension_semantics=("arbitrary",), vmem_limit_bytes=48 * 1024 * 1024
        ),
    )(offsets, current_ph, following_ph)


def advance(
    positions,
    from_below,
    from_above,
    from_right,
    from_left,
    row_weight,
    weight_up,
    col_weight,
    weight_left,
    pull_term,
    pull_prior,
    diagonal,
):
    force = row_weight * (from_below - positions) + weight_up * (from_above - positions)
    force = force + col_weight * (from_right - positions) + weight_left * (from_left - positions)
    force = force + pull_term - pull_prior
    return positions + relax_rate * force / (1.0 + diagonal)


def shards(images, offsets, springs, validity):
    successor = shifted_2(images, "sec", -1)
    rimmed = extended(successor, (("strip", 1),), RAD)
    flow_field = section_flow(images[0], rimmed[0], offsets)
    keep_mask = (lax.axis_index("sec") < lax.axis_size("sec") - 1).astype(jnp.float32)
    flow_field = flow_field * keep_mask
    node_rows, node_cols = (flow_field.shape[1], flow_field.shape[2])
    global_rows = lax.axis_index("strip") * node_rows + jnp.arange(node_rows, dtype=jnp.int32)
    row_keep = (global_rows < node_rows * lax.axis_size("strip") - 1).astype(jnp.float32)
    col_keep = (jnp.arange(node_cols) < node_cols - 1).astype(jnp.float32)
    row_weight = 0.25 * springs[0, 0].astype(jnp.float32) * row_keep[:, None]
    col_weight = 0.25 * springs[1, 0].astype(jnp.float32) * col_keep[None, :]
    match_weight = validity[0].astype(jnp.float32) * keep_mask
    stacked = jnp.stack([flow_field[0], flow_field[1], row_weight, col_weight, match_weight])
    stacked = jnp.transpose(stacked, (0, 2, 1))[:, None]
    tiled = lax.all_to_all(stacked, "sec", split_axis=2, concat_axis=1, tiled=True)
    halo = ITERS
    haloed = extended(tiled, (("sec", 2), ("strip", 3)), halo)
    flow_tiles = haloed[0:2]
    tile_row = haloed[2]
    tile_col = haloed[3]
    tile_match = haloed[4]
    weight_up = jnp.pad(tile_row, ((0, 0), (0, 0), (1, 0)))[:, :, :-1]
    weight_left = jnp.pad(tile_col, ((0, 0), (1, 0), (0, 0)))[:, :-1, :]
    match_prior = jnp.pad(tile_match, ((1, 0), (0, 0), (0, 0)))[:-1]
    diagonal = tile_row + weight_up + tile_col + weight_left + tile_match + match_prior
    positions = jnp.zeros_like(flow_tiles)
    for iteration in range(ITERS):
        padded = jnp.pad(positions, ((0, 0), (0, 0), (1, 1), (1, 1)))
        following = jnp.pad(positions, ((0, 0), (0, 1), (0, 0), (0, 0)))[:, 1:]
        pull_term = tile_match * (following - positions - flow_tiles)
        pull_prior = jnp.pad(pull_term, ((0, 0), (1, 0), (0, 0), (0, 0)))[:, :-1]
        positions = advance(
            positions,
            padded[:, :, 1:-1, 2:],
            padded[:, :, 1:-1, :-2],
            padded[:, :, 2:, 1:-1],
            padded[:, :, :-2, 1:-1],
            tile_row,
            weight_up,
            tile_col,
            weight_left,
            pull_term,
            pull_prior,
            diagonal,
        )
    core = positions[:, :, halo:-halo, halo:-halo]
    returned = lax.all_to_all(core, "sec", split_axis=1, concat_axis=2, tiled=True)
    return jnp.transpose(returned, (0, 1, 3, 2))


def solution(mesh):
    in_specs = (
        P("sec", "strip", None),
        P(),
        P(None, "sec", "strip", None),
        P("sec", "strip", None),
    )
    out_specs = P(None, "sec", "strip", None)
    return jax.shard_map(shards, mesh=mesh, in_specs=in_specs, out_specs=out_specs, check_vma=False)
```

```python
import jax
import jax.numpy as jnp
from jax import lax
from jax.experimental import pallas as pl
from jax.experimental.pallas import tpu as pltpu
from jax.sharding import PartitionSpec as P

RAD = 3
ITERS = 8


sharpness = 0.5
relax_rate = 0.8


def shifted_2(shard, axis, by):
    size = lax.axis_size(axis)
    pairs = [(i, i + by) for i in range(size) if 0 <= i + by < size]
    return lax.ppermute(shard, axis, pairs)


def extended(cells, sides, width):
    for axis, dim in sides:
        count = lax.axis_size(axis)
        ends = count - 1
        head = lax.slice_in_dim(cells, 0, width, axis=dim)
        tail = lax.slice_in_dim(cells, cells.shape[dim] - width, cells.shape[dim], axis=dim)
        cells = jnp.concatenate(
            [
                lax.ppermute(tail, axis, [(i, (i + 1) % count) for i in range(ends)]),
                cells,
                lax.ppermute(head, axis, [((i + 1) % count, i) for i in range(ends)]),
            ],
            axis=dim,
        )
    return cells


def lane_permutation():
    source = jnp.arange(512, dtype=jnp.int32)[:, None]
    target = jnp.arange(512, dtype=jnp.int32)[None, :]
    return ((source % 4) * 128 + source // 4 == target).astype(jnp.bfloat16)


def split_phases(pixels, permute, lanes_ref, phase_ref, node_rows):
    chunks = pixels.shape[1] // 512
    for c in range(chunks):
        permuted = jnp.dot(pixels[:, c * 512 : (c + 1) * 512], permute, preferred_element_type=jnp.float32)
        for t in range(4):
            lanes_ref[c * 4 + t, 0 : pixels.shape[0], :] = permuted[:, t * 128 : (t + 1) * 128]
    for q in range(4):
        for t in range(4):
            parts = [lanes_ref[pl.ds(c * 4 + t, 1), pl.ds(q, node_rows, stride=4), :][0] for c in range(chunks)]
            phase_ref[q * 4 + t] = jnp.concatenate(parts, axis=1)


def flow_kernel(
    offsets_ref, current_ref, following_ref, permute_ref, flow_ref, current_ph, following_ph, lanes_ref, shifted_ref, scores_ref
):
    tile_rows = current_ph.shape[1]
    node_cols = current_ph.shape[2]
    window = following_ph.shape[1]
    base = pl.multiple_of(pl.program_id(0) * tile_rows * 4, 32)
    permute = permute_ref[...]
    split_phases(current_ref[...], permute, lanes_ref, current_ph, tile_rows)
    split_phases(following_ref[pl.ds(base, window * 4), :], permute, lanes_ref, following_ph, window)
    column = lax.broadcasted_iota(jnp.int32, (window, node_cols), 1)

    def build(phase, carry):
        block = following_ph[phase]
        for col_shift in range(3):
            if col_shift == 1:
                moved = block
            else:
                moved = pltpu.roll(block, (1 - col_shift) % node_cols, 1)
                inside = (column + col_shift - 1 >= 0) & (column + col_shift - 1 < node_cols)
                moved = jnp.where(inside, moved, 0.0)
            for row_shift in range(3):
                rows = moved if row_shift == 0 else pltpu.roll(moved, window - row_shift, 0)
                shifted_ref[(row_shift * 3 + col_shift) * 16 + phase] = rows[:tile_rows]
        return carry

    lax.fori_loop(0, 16, build, 0)
    chunks = tile_rows // 8
    offset_count = scores_ref.shape[0]

    def score(k, carry):
        row_off = offsets_ref[k, 0]
        col_off = offsets_ref[k, 1]
        sources = []
        for q in range(4):
            u = q + row_off + 4
            u_node, u_phase = lax.shift_right_logical(u, 2), u & 3
            for t in range(4):
                v = t + col_off + 4
                v_node, v_phase = lax.shift_right_logical(v, 2), v & 3
                sources.append((u_node * 3 + v_node) * 16 + u_phase * 4 + v_phase)
        for c in range(chunks):
            rows = pl.ds(c * 8, 8)
            acc = current_ph[0, rows, :] * shifted_ref[sources[0], rows, :]
            for p in range(1, 16):
                acc = acc + current_ph[p, rows, :] * shifted_ref[sources[p], rows, :]
            scores_ref[k, rows, :] = sharpness * acc
        return carry

    lax.fori_loop(0, offset_count, score, 0)
    for c in range(chunks):
        rows = pl.ds(c * 8, 8)
        highest = scores_ref[0, rows, :]
        for k in range(1, offset_count):
            highest = jnp.maximum(highest, scores_ref[k, rows, :])
        weight_sum = jnp.zeros_like(highest)
        row_sum = jnp.zeros_like(highest)
        col_sum = jnp.zeros_like(highest)
        for k in range(offset_count):
            weight = jnp.exp(scores_ref[k, rows, :] - highest)
            weight_sum = weight_sum + weight
            row_sum = row_sum + weight * offsets_ref[k, 0].astype(jnp.float32)
            col_sum = col_sum + weight * offsets_ref[k, 1].astype(jnp.float32)
        flow_ref[0, rows, :] = row_sum / weight_sum
        flow_ref[1, rows, :] = col_sum / weight_sum


def section_flow(current, following, offsets, tile_rows=32):
    row_count, col_count = current.shape
    node_rows, node_cols = row_count // 4, col_count // 4
    window = tile_rows + 8
    padded = jnp.pad(following, ((4 - RAD, (node_rows + 8) * 4 - following.shape[0] - (4 - RAD)), (0, 0)))
    offset_count = offsets.shape[0]
    grid_spec = pltpu.PrefetchScalarGridSpec(
        num_scalar_prefetch=1,
        grid=(node_rows // tile_rows,),
        in_specs=[
            pl.BlockSpec((tile_rows * 4, col_count), lambda g, off: (g, 0)),
            pl.BlockSpec(padded.shape, lambda g, off: (0, 0)),
            pl.BlockSpec((512, 512), lambda g, off: (0, 0)),
        ],
        out_specs=pl.BlockSpec((2, tile_rows, node_cols), lambda g, off: (0, g, 0)),
        scratch_shapes=[
            pltpu.VMEM((16, tile_rows, node_cols), jnp.float32),
            pltpu.VMEM((16, window, node_cols), jnp.float32),
            pltpu.VMEM((col_count // 128, window * 4, 128), jnp.float32),
            pltpu.VMEM((144, tile_rows, node_cols), jnp.float32),
            pltpu.VMEM((offset_count, tile_rows, node_cols), jnp.float32),
        ],
    )
    return pl.pallas_call(
        flow_kernel,
        grid_spec=grid_spec,
        out_shape=jax.ShapeDtypeStruct((2, node_rows, node_cols), jnp.float32),
        compiler_params=pltpu.CompilerParams(
            dimension_semantics=("arbitrary",), vmem_limit_bytes=48 * 1024 * 1024
        ),
    )(offsets, current, padded, lane_permutation())


def advance(
    positions,
    from_below,
    from_above,
    from_right,
    from_left,
    row_weight,
    weight_up,
    col_weight,
    weight_left,
    pull_term,
    pull_prior,
    diagonal,
):
    force = row_weight * (from_below - positions) + weight_up * (from_above - positions)
    force = force + col_weight * (from_right - positions) + weight_left * (from_left - positions)
    force = force + pull_term - pull_prior
    return positions + relax_rate * force / (1.0 + diagonal)


def shards(images, offsets, springs, validity):
    successor = shifted_2(images, "sec", -1)
    rimmed = extended(successor, (("strip", 1),), RAD)
    flow_field = section_flow(images[0], rimmed[0], offsets)
    keep_mask = (lax.axis_index("sec") < lax.axis_size("sec") - 1).astype(jnp.float32)
    flow_field = flow_field * keep_mask
    node_rows, node_cols = (flow_field.shape[1], flow_field.shape[2])
    global_rows = lax.axis_index("strip") * node_rows + jnp.arange(node_rows, dtype=jnp.int32)
    row_keep = (global_rows < node_rows * lax.axis_size("strip") - 1).astype(jnp.float32)
    col_keep = (jnp.arange(node_cols) < node_cols - 1).astype(jnp.float32)
    row_weight = 0.25 * springs[0, 0].astype(jnp.float32) * row_keep[:, None]
    col_weight = 0.25 * springs[1, 0].astype(jnp.float32) * col_keep[None, :]
    match_weight = validity[0].astype(jnp.float32) * keep_mask
    stacked = jnp.stack([flow_field[0], flow_field[1], row_weight, col_weight, match_weight])
    stacked = jnp.transpose(stacked, (0, 2, 1))[:, None]
    tiled = lax.all_to_all(stacked, "sec", split_axis=2, concat_axis=1, tiled=True)
    halo = ITERS
    haloed = extended(tiled, (("sec", 2), ("strip", 3)), halo)
    flow_tiles = haloed[0:2]
    tile_row = haloed[2]
    tile_col = haloed[3]
    tile_match = haloed[4]
    weight_up = jnp.pad(tile_row, ((0, 0), (0, 0), (1, 0)))[:, :, :-1]
    weight_left = jnp.pad(tile_col, ((0, 0), (1, 0), (0, 0)))[:, :-1, :]
    match_prior = jnp.pad(tile_match, ((1, 0), (0, 0), (0, 0)))[:-1]
    diagonal = tile_row + weight_up + tile_col + weight_left + tile_match + match_prior
    positions = jnp.zeros_like(flow_tiles)
    for iteration in range(ITERS):
        padded = jnp.pad(positions, ((0, 0), (0, 0), (1, 1), (1, 1)))
        following = jnp.pad(positions, ((0, 0), (0, 1), (0, 0), (0, 0)))[:, 1:]
        pull_term = tile_match * (following - positions - flow_tiles)
        pull_prior = jnp.pad(pull_term, ((0, 0), (1, 0), (0, 0), (0, 0)))[:, :-1]
        positions = advance(
            positions,
            padded[:, :, 1:-1, 2:],
            padded[:, :, 1:-1, :-2],
            padded[:, :, 2:, 1:-1],
            padded[:, :, :-2, 1:-1],
            tile_row,
            weight_up,
            tile_col,
            weight_left,
            pull_term,
            pull_prior,
            diagonal,
        )
    core = positions[:, :, halo:-halo, halo:-halo]
    returned = lax.all_to_all(core, "sec", split_axis=1, concat_axis=2, tiled=True)
    return jnp.transpose(returned, (0, 1, 3, 2))


def solution(mesh):
    in_specs = (
        P("sec", "strip", None),
        P(),
        P(None, "sec", "strip", None),
        P("sec", "strip", None),
    )
    out_specs = P(None, "sec", "strip", None)
    return jax.shard_map(shards, mesh=mesh, in_specs=in_specs, out_specs=out_specs, check_vma=False)
```

```python
import jax
import jax.numpy as jnp
from jax import lax
from jax.experimental import pallas as pl
from jax.experimental.pallas import tpu as pltpu
from jax.sharding import PartitionSpec as P

RAD = 3
ITERS = 8


sharpness = 0.5
relax_rate = 0.8


def shifted_2(shard, axis, by):
    size = lax.axis_size(axis)
    pairs = [(i, i + by) for i in range(size) if 0 <= i + by < size]
    return lax.ppermute(shard, axis, pairs)


def extended(cells, sides, width):
    for axis, dim in sides:
        count = lax.axis_size(axis)
        ends = count - 1
        head = lax.slice_in_dim(cells, 0, width, axis=dim)
        tail = lax.slice_in_dim(cells, cells.shape[dim] - width, cells.shape[dim], axis=dim)
        cells = jnp.concatenate(
            [
                lax.ppermute(tail, axis, [(i, (i + 1) % count) for i in range(ends)]),
                cells,
                lax.ppermute(head, axis, [((i + 1) % count, i) for i in range(ends)]),
            ],
            axis=dim,
        )
    return cells


def lane_permutation():
    source = jnp.arange(512, dtype=jnp.int32)[:, None]
    target = jnp.arange(512, dtype=jnp.int32)[None, :]
    return ((source % 4) * 128 + source // 4 == target).astype(jnp.bfloat16)


def split_phases(pixels, permute, lanes_ref, phase_ref, node_rows):
    chunks = pixels.shape[1] // 512
    for c in range(chunks):
        permuted = jnp.dot(pixels[:, c * 512 : (c + 1) * 512], permute, preferred_element_type=jnp.float32)
        for t in range(4):
            lanes_ref[c * 4 + t, 0 : pixels.shape[0], :] = permuted[:, t * 128 : (t + 1) * 128]
    for q in range(4):
        for t in range(4):
            parts = [lanes_ref[pl.ds(c * 4 + t, 1), pl.ds(q, node_rows, stride=4), :][0] for c in range(chunks)]
            phase_ref[q * 4 + t] = jnp.concatenate(parts, axis=1)


def flow_kernel(
    offsets_ref, current_ref, following_ref, permute_ref, flow_ref, current_ph, following_ph, lanes_ref, shifted_ref, scores_ref
):
    tile_rows = current_ph.shape[1]
    node_cols = current_ph.shape[2]
    window = following_ph.shape[1]
    base = pl.multiple_of(pl.program_id(0) * tile_rows * 4, 32)
    permute = permute_ref[...]
    split_phases(current_ref[...], permute, lanes_ref, current_ph, tile_rows)
    split_phases(following_ref[pl.ds(base, window * 4), :], permute, lanes_ref, following_ph, window)
    column = lax.broadcasted_iota(jnp.int32, (window, node_cols), 1)

    def build(phase, carry):
        block = following_ph[phase]
        for col_shift in range(3):
            if col_shift == 1:
                moved = block
            else:
                moved = pltpu.roll(block, (1 - col_shift) % node_cols, 1)
                inside = (column + col_shift - 1 >= 0) & (column + col_shift - 1 < node_cols)
                moved = jnp.where(inside, moved, 0.0)
            for row_shift in range(3):
                rows = moved if row_shift == 0 else pltpu.roll(moved, window - row_shift, 0)
                shifted_ref[(row_shift * 3 + col_shift) * 16 + phase] = rows[:tile_rows]
        return carry

    lax.fori_loop(0, 16, build, 0)
    chunks = tile_rows // 8
    offset_count = scores_ref.shape[0]

    def score(k, carry):
        row_off = offsets_ref[k, 0]
        col_off = offsets_ref[k, 1]
        sources = []
        for q in range(4):
            u = q + row_off + 4
            u_node, u_phase = lax.shift_right_logical(u, 2), u & 3
            for t in range(4):
                v = t + col_off + 4
                v_node, v_phase = lax.shift_right_logical(v, 2), v & 3
                sources.append((u_node * 3 + v_node) * 16 + u_phase * 4 + v_phase)
        for c in range(chunks):
            rows = pl.ds(c * 8, 8)
            acc = current_ph[0, rows, :] * shifted_ref[sources[0], rows, :]
            for p in range(1, 16):
                acc = acc + current_ph[p, rows, :] * shifted_ref[sources[p], rows, :]
            scores_ref[k, rows, :] = sharpness * acc
        return carry

    lax.fori_loop(0, offset_count, score, 0)
    for c in range(chunks):
        rows = pl.ds(c * 8, 8)
        highest = scores_ref[0, rows, :]
        for k in range(1, offset_count):
            highest = jnp.maximum(highest, scores_ref[k, rows, :])
        weight_sum = jnp.zeros_like(highest)
        row_sum = jnp.zeros_like(highest)
        col_sum = jnp.zeros_like(highest)
        for k in range(offset_count):
            weight = jnp.exp(scores_ref[k, rows, :] - highest)
            weight_sum = weight_sum + weight
            row_sum = row_sum + weight * offsets_ref[k, 0].astype(jnp.float32)
            col_sum = col_sum + weight * offsets_ref[k, 1].astype(jnp.float32)
        flow_ref[0, rows, :] = row_sum / weight_sum
        flow_ref[1, rows, :] = col_sum / weight_sum


def section_flow(current, following, offsets, tile_rows=32):
    row_count, col_count = current.shape
    node_rows, node_cols = row_count // 4, col_count // 4
    window = tile_rows + 8
    padded = jnp.pad(following, ((4 - RAD, (node_rows + 8) * 4 - following.shape[0] - (4 - RAD)), (0, 0)))
    offset_count = offsets.shape[0]
    grid_spec = pltpu.PrefetchScalarGridSpec(
        num_scalar_prefetch=1,
        grid=(node_rows // tile_rows,),
        in_specs=[
            pl.BlockSpec((tile_rows * 4, col_count), lambda g, off: (g, 0)),
            pl.BlockSpec(padded.shape, lambda g, off: (0, 0)),
            pl.BlockSpec((512, 512), lambda g, off: (0, 0)),
        ],
        out_specs=pl.BlockSpec((2, tile_rows, node_cols), lambda g, off: (0, g, 0)),
        scratch_shapes=[
            pltpu.VMEM((16, tile_rows, node_cols), jnp.float32),
            pltpu.VMEM((16, window, node_cols), jnp.float32),
            pltpu.VMEM((col_count // 128, window * 4, 128), jnp.float32),
            pltpu.VMEM((144, tile_rows, node_cols), jnp.float32),
            pltpu.VMEM((offset_count, tile_rows, node_cols), jnp.float32),
        ],
    )
    return pl.pallas_call(
        flow_kernel,
        grid_spec=grid_spec,
        out_shape=jax.ShapeDtypeStruct((2, node_rows, node_cols), jnp.float32),
        compiler_params=pltpu.CompilerParams(
            dimension_semantics=("arbitrary",), vmem_limit_bytes=48 * 1024 * 1024
        ),
    )(offsets, current, padded, lane_permutation())


def advance(
    positions,
    from_below,
    from_above,
    from_right,
    from_left,
    row_weight,
    weight_up,
    col_weight,
    weight_left,
    pull_term,
    pull_prior,
    diagonal,
):
    force = row_weight * (from_below - positions) + weight_up * (from_above - positions)
    force = force + col_weight * (from_right - positions) + weight_left * (from_left - positions)
    force = force + pull_term - pull_prior
    return positions + relax_rate * force / (1.0 + diagonal)


def shards(images, offsets, springs, validity):
    pixels = images[0]
    half = pixels.shape[0] // 2
    sec_count = lax.axis_size("sec")
    strip_count = lax.axis_size("strip")
    successor_top = shifted_2(pixels[: half + RAD], "sec", -1)
    prior_bottom = shifted_2(pixels[half:], "sec", 1)
    corner = lax.ppermute(
        pixels[-RAD:],
        ("sec", "strip"),
        [((s + 1) * strip_count + p - 1, s * strip_count + p) for s in range(sec_count - 1) for p in range(1, strip_count)],
    )
    below = shifted_2(pixels[:RAD], "strip", -1)
    keep_mask = (lax.axis_index("sec") < sec_count - 1).astype(jnp.float32)
    flow_top = section_flow(pixels[:half], jnp.concatenate([corner, successor_top]), offsets) * keep_mask
    flow_bottom = section_flow(prior_bottom, jnp.concatenate([pixels[half - RAD :], below]), offsets)
    flow_field = jnp.concatenate([flow_top, flow_bottom], axis=1)
    node_rows, node_cols = (flow_field.shape[1], flow_field.shape[2])
    global_rows = lax.axis_index("strip") * node_rows + jnp.arange(node_rows, dtype=jnp.int32)
    row_keep = (global_rows < node_rows * lax.axis_size("strip") - 1).astype(jnp.float32)
    col_keep = (jnp.arange(node_cols) < node_cols - 1).astype(jnp.float32)
    row_weight = 0.25 * springs[0, 0].astype(jnp.float32) * row_keep[:, None]
    col_weight = 0.25 * springs[1, 0].astype(jnp.float32) * col_keep[None, :]
    match_weight = validity[0].astype(jnp.float32) * keep_mask
    stacked = jnp.stack([flow_field[0], flow_field[1], row_weight, col_weight, match_weight])
    stacked = jnp.transpose(stacked, (0, 2, 1))[:, None]
    tiled = lax.all_to_all(stacked, "sec", split_axis=2, concat_axis=1, tiled=True)
    node_half = tiled.shape[3] // 2
    bottoms = tiled[0:2, 1:, :, node_half:]
    bottoms = jnp.concatenate([bottoms, jnp.zeros_like(bottoms[:, :1])], axis=1)
    tiled = jnp.concatenate([jnp.concatenate([tiled[0:2, :, :, :node_half], bottoms], axis=3), tiled[2:]])
    halo = ITERS
    haloed = extended(tiled, (("sec", 2), ("strip", 3)), halo)
    flow_tiles = haloed[0:2]
    tile_row = haloed[2]
    tile_col = haloed[3]
    tile_match = haloed[4]
    weight_up = jnp.pad(tile_row, ((0, 0), (0, 0), (1, 0)))[:, :, :-1]
    weight_left = jnp.pad(tile_col, ((0, 0), (1, 0), (0, 0)))[:, :-1, :]
    match_prior = jnp.pad(tile_match, ((1, 0), (0, 0), (0, 0)))[:-1]
    diagonal = tile_row + weight_up + tile_col + weight_left + tile_match + match_prior
    positions = jnp.zeros_like(flow_tiles)
    for iteration in range(ITERS):
        padded = jnp.pad(positions, ((0, 0), (0, 0), (1, 1), (1, 1)))
        following = jnp.pad(positions, ((0, 0), (0, 1), (0, 0), (0, 0)))[:, 1:]
        pull_term = tile_match * (following - positions - flow_tiles)
        pull_prior = jnp.pad(pull_term, ((0, 0), (1, 0), (0, 0), (0, 0)))[:, :-1]
        positions = advance(
            positions,
            padded[:, :, 1:-1, 2:],
            padded[:, :, 1:-1, :-2],
            padded[:, :, 2:, 1:-1],
            padded[:, :, :-2, 1:-1],
            tile_row,
            weight_up,
            tile_col,
            weight_left,
            pull_term,
            pull_prior,
            diagonal,
        )
    core = positions[:, :, halo:-halo, halo:-halo]
    returned = lax.all_to_all(core, "sec", split_axis=1, concat_axis=2, tiled=True)
    return jnp.transpose(returned, (0, 1, 3, 2))


def solution(mesh):
    in_specs = (
        P("sec", "strip", None),
        P(),
        P(None, "sec", "strip", None),
        P("sec", "strip", None),
    )
    out_specs = P(None, "sec", "strip", None)
    return jax.shard_map(shards, mesh=mesh, in_specs=in_specs, out_specs=out_specs, check_vma=False)
```

```python
import jax
import jax.numpy as jnp
from jax import lax
from jax.experimental import pallas as pl
from jax.experimental.pallas import tpu as pltpu
from jax.sharding import PartitionSpec as P

RAD = 3
ITERS = 8


sharpness = 0.5
relax_rate = 0.8


def shifted_2(shard, axis, by):
    size = lax.axis_size(axis)
    pairs = [(i, i + by) for i in range(size) if 0 <= i + by < size]
    return lax.ppermute(shard, axis, pairs)


def extended(cells, sides, width):
    for axis, dim in sides:
        count = lax.axis_size(axis)
        ends = count - 1
        head = lax.slice_in_dim(cells, 0, width, axis=dim)
        tail = lax.slice_in_dim(cells, cells.shape[dim] - width, cells.shape[dim], axis=dim)
        cells = jnp.concatenate(
            [
                lax.ppermute(tail, axis, [(i, (i + 1) % count) for i in range(ends)]),
                cells,
                lax.ppermute(head, axis, [((i + 1) % count, i) for i in range(ends)]),
            ],
            axis=dim,
        )
    return cells


def lane_permutation():
    source = jnp.arange(512, dtype=jnp.int32)[:, None]
    target = jnp.arange(512, dtype=jnp.int32)[None, :]
    return ((source % 4) * 128 + source // 4 == target).astype(jnp.bfloat16)


def split_phases(pixels, permute, lanes_ref, phase_ref, node_rows):
    chunks = pixels.shape[1] // 512
    for c in range(chunks):
        permuted = jnp.dot(pixels[:, c * 512 : (c + 1) * 512], permute, preferred_element_type=jnp.float32)
        for t in range(4):
            lanes_ref[c * 4 + t, 0 : pixels.shape[0], :] = permuted[:, t * 128 : (t + 1) * 128]
    for q in range(4):
        for t in range(4):
            parts = [lanes_ref[pl.ds(c * 4 + t, 1), pl.ds(q, node_rows, stride=4), :][0] for c in range(chunks)]
            phase_ref[q * 4 + t] = jnp.concatenate(parts, axis=1)


def flow_kernel(
    offsets_ref, current_ref, following_ref, permute_ref, flow_ref, current_ph, following_ph, lanes_ref, shifted_ref, scores_ref
):
    tile_rows = current_ph.shape[1]
    node_cols = current_ph.shape[2]
    window = following_ph.shape[1]
    base = pl.multiple_of(pl.program_id(0) * tile_rows * 4, 32)
    permute = permute_ref[...]
    split_phases(current_ref[...], permute, lanes_ref, current_ph, tile_rows)
    split_phases(following_ref[pl.ds(base, window * 4), :], permute, lanes_ref, following_ph, window)
    column = lax.broadcasted_iota(jnp.int32, (window, node_cols), 1)

    def build(phase, carry):
        block = following_ph[phase]
        for col_shift in range(3):
            if col_shift == 1:
                moved = block
            else:
                moved = pltpu.roll(block, (1 - col_shift) % node_cols, 1)
                inside = (column + col_shift - 1 >= 0) & (column + col_shift - 1 < node_cols)
                moved = jnp.where(inside, moved, 0.0)
            for row_shift in range(3):
                rows = moved if row_shift == 0 else pltpu.roll(moved, window - row_shift, 0)
                shifted_ref[(row_shift * 3 + col_shift) * 16 + phase] = rows[:tile_rows]
        return carry

    lax.fori_loop(0, 16, build, 0)
    chunks = tile_rows // 8
    offset_count = scores_ref.shape[0]

    def score(k, carry):
        row_off = offsets_ref[k, 0]
        col_off = offsets_ref[k, 1]
        sources = []
        for q in range(4):
            u = q + row_off + 4
            u_node, u_phase = lax.shift_right_logical(u, 2), u & 3
            for t in range(4):
                v = t + col_off + 4
                v_node, v_phase = lax.shift_right_logical(v, 2), v & 3
                sources.append((u_node * 3 + v_node) * 16 + u_phase * 4 + v_phase)
        for c in range(chunks):
            rows = pl.ds(c * 8, 8)
            acc = current_ph[0, rows, :] * shifted_ref[sources[0], rows, :]
            for p in range(1, 16):
                acc = acc + current_ph[p, rows, :] * shifted_ref[sources[p], rows, :]
            scores_ref[k, rows, :] = sharpness * acc
        return carry

    lax.fori_loop(0, offset_count, score, 0)
    for c in range(chunks):
        rows = pl.ds(c * 8, 8)
        highest = scores_ref[0, rows, :]
        for k in range(1, offset_count):
            highest = jnp.maximum(highest, scores_ref[k, rows, :])
        weight_sum = jnp.zeros_like(highest)
        row_sum = jnp.zeros_like(highest)
        col_sum = jnp.zeros_like(highest)
        for k in range(offset_count):
            weight = jnp.exp(scores_ref[k, rows, :] - highest)
            weight_sum = weight_sum + weight
            row_sum = row_sum + weight * offsets_ref[k, 0].astype(jnp.float32)
            col_sum = col_sum + weight * offsets_ref[k, 1].astype(jnp.float32)
        flow_ref[0, rows, :] = row_sum / weight_sum
        flow_ref[1, rows, :] = col_sum / weight_sum


def section_flow(current, following, offsets, tile_rows=32):
    row_count, col_count = current.shape
    node_rows, node_cols = row_count // 4, col_count // 4
    window = tile_rows + 8
    padded = jnp.pad(following, ((4 - RAD, (node_rows + 8) * 4 - following.shape[0] - (4 - RAD)), (0, 0)))
    offset_count = offsets.shape[0]
    grid_spec = pltpu.PrefetchScalarGridSpec(
        num_scalar_prefetch=1,
        grid=(node_rows // tile_rows,),
        in_specs=[
            pl.BlockSpec((tile_rows * 4, col_count), lambda g, off: (g, 0)),
            pl.BlockSpec(padded.shape, lambda g, off: (0, 0)),
            pl.BlockSpec((512, 512), lambda g, off: (0, 0)),
        ],
        out_specs=pl.BlockSpec((2, tile_rows, node_cols), lambda g, off: (0, g, 0)),
        scratch_shapes=[
            pltpu.VMEM((16, tile_rows, node_cols), jnp.float32),
            pltpu.VMEM((16, window, node_cols), jnp.float32),
            pltpu.VMEM((col_count // 128, window * 4, 128), jnp.float32),
            pltpu.VMEM((144, tile_rows, node_cols), jnp.float32),
            pltpu.VMEM((offset_count, tile_rows, node_cols), jnp.float32),
        ],
    )
    return pl.pallas_call(
        flow_kernel,
        grid_spec=grid_spec,
        out_shape=jax.ShapeDtypeStruct((2, node_rows, node_cols), jnp.float32),
        compiler_params=pltpu.CompilerParams(
            dimension_semantics=("arbitrary",), vmem_limit_bytes=48 * 1024 * 1024
        ),
    )(offsets, current, padded, lane_permutation())


def advance(
    positions,
    from_below,
    from_above,
    from_right,
    from_left,
    row_weight,
    weight_up,
    col_weight,
    weight_left,
    pull_term,
    pull_prior,
    diagonal,
):
    force = row_weight * (from_below - positions) + weight_up * (from_above - positions)
    force = force + col_weight * (from_right - positions) + weight_left * (from_left - positions)
    force = force + pull_term - pull_prior
    return positions + relax_rate * force / (1.0 + diagonal)


def shards(images, offsets, springs, validity):
    pixels = images[0]
    half = pixels.shape[0] // 2
    sec_count = lax.axis_size("sec")
    strip_count = lax.axis_size("strip")
    successor_top = shifted_2(pixels[: half + RAD], "sec", -1)
    prior_bottom = shifted_2(pixels[half:], "sec", 1)
    corner = lax.ppermute(
        pixels[-RAD:],
        ("sec", "strip"),
        [((s + 1) * strip_count + p - 1, s * strip_count + p) for s in range(sec_count - 1) for p in range(1, strip_count)],
    )
    below = shifted_2(pixels[:RAD], "strip", -1)
    keep_mask = (lax.axis_index("sec") < sec_count - 1).astype(jnp.float32)
    match_weight = validity[0].astype(jnp.float32) * keep_mask
    node_rows, node_cols = (springs.shape[2], springs.shape[3])
    global_rows = lax.axis_index("strip") * node_rows + jnp.arange(node_rows, dtype=jnp.int32)
    row_keep = (global_rows < node_rows * lax.axis_size("strip") - 1).astype(jnp.float32)
    col_keep = (jnp.arange(node_cols) < node_cols - 1).astype(jnp.float32)
    row_weight = 0.25 * springs[0, 0].astype(jnp.float32) * row_keep[:, None]
    col_weight = 0.25 * springs[1, 0].astype(jnp.float32) * col_keep[None, :]
    halo = ITERS
    weights = jnp.stack([row_weight, col_weight, match_weight]).astype(jnp.bfloat16)
    weights = lax.all_to_all(jnp.transpose(weights, (0, 2, 1))[:, None], "sec", split_axis=2, concat_axis=1, tiled=True)
    weights = extended(weights, (("sec", 2), ("strip", 3)), halo).astype(jnp.float32)
    weights, successor_top, prior_bottom = lax.optimization_barrier((weights, successor_top, prior_bottom))
    flow_top = section_flow(pixels[:half], jnp.concatenate([corner, successor_top]), offsets) * keep_mask
    flow_bottom = section_flow(prior_bottom, jnp.concatenate([pixels[half - RAD :], below]), offsets)
    flow_field = jnp.concatenate([flow_top, flow_bottom], axis=1)
    flows = jnp.transpose(flow_field, (0, 2, 1))[:, None]
    tiled = lax.all_to_all(flows, "sec", split_axis=2, concat_axis=1, tiled=True)
    node_half = tiled.shape[3] // 2
    bottoms = tiled[:, 1:, :, node_half:]
    bottoms = jnp.concatenate([bottoms, jnp.zeros_like(bottoms[:, :1])], axis=1)
    tiled = jnp.concatenate([tiled[:, :, :, :node_half], bottoms], axis=3)
    flow_tiles = extended(tiled, (("sec", 2), ("strip", 3)), halo)
    tile_row = weights[0]
    tile_col = weights[1]
    tile_match = weights[2]
    weight_up = jnp.pad(tile_row, ((0, 0), (0, 0), (1, 0)))[:, :, :-1]
    weight_left = jnp.pad(tile_col, ((0, 0), (1, 0), (0, 0)))[:, :-1, :]
    match_prior = jnp.pad(tile_match, ((1, 0), (0, 0), (0, 0)))[:-1]
    diagonal = tile_row + weight_up + tile_col + weight_left + tile_match + match_prior
    positions = jnp.zeros_like(flow_tiles)
    for iteration in range(ITERS):
        padded = jnp.pad(positions, ((0, 0), (0, 0), (1, 1), (1, 1)))
        following = jnp.pad(positions, ((0, 0), (0, 1), (0, 0), (0, 0)))[:, 1:]
        pull_term = tile_match * (following - positions - flow_tiles)
        pull_prior = jnp.pad(pull_term, ((0, 0), (1, 0), (0, 0), (0, 0)))[:, :-1]
        positions = advance(
            positions,
            padded[:, :, 1:-1, 2:],
            padded[:, :, 1:-1, :-2],
            padded[:, :, 2:, 1:-1],
            padded[:, :, :-2, 1:-1],
            tile_row,
            weight_up,
            tile_col,
            weight_left,
            pull_term,
            pull_prior,
            diagonal,
        )
    core = positions[:, :, halo:-halo, halo:-halo]
    returned = lax.all_to_all(core, "sec", split_axis=1, concat_axis=2, tiled=True)
    return jnp.transpose(returned, (0, 1, 3, 2))


def solution(mesh):
    in_specs = (
        P("sec", "strip", None),
        P(),
        P(None, "sec", "strip", None),
        P("sec", "strip", None),
    )
    out_specs = P(None, "sec", "strip", None)
    return jax.shard_map(shards, mesh=mesh, in_specs=in_specs, out_specs=out_specs, check_vma=False)
```

```python
import jax
import jax.numpy as jnp
from jax import lax
from jax.experimental import pallas as pl
from jax.experimental.pallas import tpu as pltpu
from jax.sharding import PartitionSpec as P

RAD = 3
ITERS = 8


sharpness = 0.5
relax_rate = 0.8


def shifted_2(shard, axis, by):
    size = lax.axis_size(axis)
    pairs = [(i, i + by) for i in range(size) if 0 <= i + by < size]
    return lax.ppermute(shard, axis, pairs)


def extended(cells, sides, width):
    for axis, dim in sides:
        count = lax.axis_size(axis)
        ends = count - 1
        head = lax.slice_in_dim(cells, 0, width, axis=dim)
        tail = lax.slice_in_dim(cells, cells.shape[dim] - width, cells.shape[dim], axis=dim)
        cells = jnp.concatenate(
            [
                lax.ppermute(tail, axis, [(i, (i + 1) % count) for i in range(ends)]),
                cells,
                lax.ppermute(head, axis, [((i + 1) % count, i) for i in range(ends)]),
            ],
            axis=dim,
        )
    return cells


def lane_permutation():
    source = jnp.arange(512, dtype=jnp.int32)[:, None]
    target = jnp.arange(512, dtype=jnp.int32)[None, :]
    return ((source % 4) * 128 + source // 4 == target).astype(jnp.bfloat16)


def split_phases(pixels, permute, lanes_ref, phase_ref, node_rows):
    chunks = pixels.shape[1] // 512
    for c in range(chunks):
        permuted = jnp.dot(pixels[:, c * 512 : (c + 1) * 512], permute, preferred_element_type=jnp.float32)
        for t in range(4):
            lanes_ref[c * 4 + t, 0 : pixels.shape[0], :] = permuted[:, t * 128 : (t + 1) * 128]
    for q in range(4):
        for t in range(4):
            parts = [lanes_ref[pl.ds(c * 4 + t, 1), pl.ds(q, node_rows, stride=4), :][0] for c in range(chunks)]
            phase_ref[q * 4 + t] = jnp.concatenate(parts, axis=1)


def flow_kernel(
    offsets_ref, current_ref, following_ref, permute_ref, flow_ref, current_ph, following_ph, lanes_ref, shifted_ref, scores_ref
):
    tile_rows = current_ph.shape[1]
    node_cols = current_ph.shape[2]
    window = following_ph.shape[1]
    base = pl.multiple_of(pl.program_id(0) * tile_rows * 4, 32)
    permute = permute_ref[...]
    split_phases(current_ref[...], permute, lanes_ref, current_ph, tile_rows)
    split_phases(following_ref[pl.ds(base, window * 4), :], permute, lanes_ref, following_ph, window)
    column = lax.broadcasted_iota(jnp.int32, (window, node_cols), 1)

    def build(phase, carry):
        block = following_ph[phase]
        for col_shift in range(3):
            if col_shift == 1:
                moved = block
            else:
                moved = pltpu.roll(block, (1 - col_shift) % node_cols, 1)
                inside = (column + col_shift - 1 >= 0) & (column + col_shift - 1 < node_cols)
                moved = jnp.where(inside, moved, 0.0)
            for row_shift in range(3):
                rows = moved if row_shift == 0 else pltpu.roll(moved, window - row_shift, 0)
                shifted_ref[(row_shift * 3 + col_shift) * 16 + phase] = rows[:tile_rows]
        return carry

    lax.fori_loop(0, 16, build, 0)
    chunks = tile_rows // 8
    offset_count = scores_ref.shape[0]

    def score(k, carry):
        row_off = offsets_ref[k, 0]
        col_off = offsets_ref[k, 1]
        sources = []
        for q in range(4):
            u = q + row_off + 4
            u_node, u_phase = lax.shift_right_logical(u, 2), u & 3
            for t in range(4):
                v = t + col_off + 4
                v_node, v_phase = lax.shift_right_logical(v, 2), v & 3
                sources.append((u_node * 3 + v_node) * 16 + u_phase * 4 + v_phase)
        for c in range(chunks):
            rows = pl.ds(c * 8, 8)
            acc = current_ph[0, rows, :] * shifted_ref[sources[0], rows, :]
            for p in range(1, 16):
                acc = acc + current_ph[p, rows, :] * shifted_ref[sources[p], rows, :]
            scores_ref[k, rows, :] = sharpness * acc
        return carry

    lax.fori_loop(0, offset_count, score, 0)
    for c in range(chunks):
        rows = pl.ds(c * 8, 8)
        highest = scores_ref[0, rows, :]
        for k in range(1, offset_count):
            highest = jnp.maximum(highest, scores_ref[k, rows, :])
        weight_sum = jnp.zeros_like(highest)
        row_sum = jnp.zeros_like(highest)
        col_sum = jnp.zeros_like(highest)
        for k in range(offset_count):
            weight = jnp.exp(scores_ref[k, rows, :] - highest)
            weight_sum = weight_sum + weight
            row_sum = row_sum + weight * offsets_ref[k, 0].astype(jnp.float32)
            col_sum = col_sum + weight * offsets_ref[k, 1].astype(jnp.float32)
        flow_ref[0, rows, :] = row_sum / weight_sum
        flow_ref[1, rows, :] = col_sum / weight_sum


def section_flow(current, following, offsets, tile_rows=32):
    row_count, col_count = current.shape
    node_rows, node_cols = row_count // 4, col_count // 4
    window = tile_rows + 8
    padded = jnp.pad(following, ((4 - RAD, (node_rows + 8) * 4 - following.shape[0] - (4 - RAD)), (0, 0)))
    offset_count = offsets.shape[0]
    grid_spec = pltpu.PrefetchScalarGridSpec(
        num_scalar_prefetch=1,
        grid=(node_rows // tile_rows,),
        in_specs=[
            pl.BlockSpec((tile_rows * 4, col_count), lambda g, off: (g, 0)),
            pl.BlockSpec(padded.shape, lambda g, off: (0, 0)),
            pl.BlockSpec((512, 512), lambda g, off: (0, 0)),
        ],
        out_specs=pl.BlockSpec((2, tile_rows, node_cols), lambda g, off: (0, g, 0)),
        scratch_shapes=[
            pltpu.VMEM((16, tile_rows, node_cols), jnp.float32),
            pltpu.VMEM((16, window, node_cols), jnp.float32),
            pltpu.VMEM((col_count // 128, window * 4, 128), jnp.float32),
            pltpu.VMEM((144, tile_rows, node_cols), jnp.float32),
            pltpu.VMEM((offset_count, tile_rows, node_cols), jnp.float32),
        ],
    )
    return pl.pallas_call(
        flow_kernel,
        grid_spec=grid_spec,
        out_shape=jax.ShapeDtypeStruct((2, node_rows, node_cols), jnp.float32),
        compiler_params=pltpu.CompilerParams(
            dimension_semantics=("arbitrary",), vmem_limit_bytes=48 * 1024 * 1024
        ),
    )(offsets, current, padded, lane_permutation())


def advance(
    positions,
    from_below,
    from_above,
    from_right,
    from_left,
    row_weight,
    weight_up,
    col_weight,
    weight_left,
    pull_term,
    pull_prior,
    diagonal,
):
    force = row_weight * (from_below - positions) + weight_up * (from_above - positions)
    force = force + col_weight * (from_right - positions) + weight_left * (from_left - positions)
    force = force + pull_term - pull_prior
    return positions + relax_rate * force / (1.0 + diagonal)


def shards(images, offsets, springs, validity):
    pixels = images[0]
    half = pixels.shape[0] // 2
    sec_count = lax.axis_size("sec")
    strip_count = lax.axis_size("strip")
    successor_top = shifted_2(pixels[: half + RAD], "sec", -1)
    prior_bottom = shifted_2(pixels[half:], "sec", 1)
    corner = lax.ppermute(
        pixels[-RAD:],
        ("sec", "strip"),
        [((s + 1) * strip_count + p - 1, s * strip_count + p) for s in range(sec_count - 1) for p in range(1, strip_count)],
    )
    below = shifted_2(pixels[:RAD], "strip", -1)
    keep_mask = (lax.axis_index("sec") < sec_count - 1).astype(jnp.float32)
    springs, validity, prior_bottom = lax.optimization_barrier((springs, validity, prior_bottom))
    match_weight = validity[0].astype(jnp.float32) * keep_mask
    node_rows, node_cols = (springs.shape[2], springs.shape[3])
    global_rows = lax.axis_index("strip") * node_rows + jnp.arange(node_rows, dtype=jnp.int32)
    row_keep = (global_rows < node_rows * lax.axis_size("strip") - 1).astype(jnp.float32)
    col_keep = (jnp.arange(node_cols) < node_cols - 1).astype(jnp.float32)
    row_weight = 0.25 * springs[0, 0].astype(jnp.float32) * row_keep[:, None]
    col_weight = 0.25 * springs[1, 0].astype(jnp.float32) * col_keep[None, :]
    halo = ITERS
    weights = jnp.stack([row_weight, col_weight, match_weight]).astype(jnp.bfloat16)
    weights = lax.all_to_all(jnp.transpose(weights, (0, 2, 1))[:, None], "sec", split_axis=2, concat_axis=1, tiled=True)
    weights = extended(weights, (("sec", 2), ("strip", 3)), halo).astype(jnp.float32)
    flow_top = section_flow(pixels[:half], jnp.concatenate([corner, successor_top]), offsets) * keep_mask
    flow_bottom = section_flow(prior_bottom, jnp.concatenate([pixels[half - RAD :], below]), offsets)
    flow_field = jnp.concatenate([flow_top, flow_bottom], axis=1)
    flows = jnp.transpose(flow_field, (0, 2, 1))[:, None]
    tiled = lax.all_to_all(flows, "sec", split_axis=2, concat_axis=1, tiled=True)
    node_half = tiled.shape[3] // 2
    bottoms = tiled[:, 1:, :, node_half:]
    bottoms = jnp.concatenate([bottoms, jnp.zeros_like(bottoms[:, :1])], axis=1)
    tiled = jnp.concatenate([tiled[:, :, :, :node_half], bottoms], axis=3)
    flow_tiles = extended(tiled, (("sec", 2), ("strip", 3)), halo)
    tile_row = weights[0]
    tile_col = weights[1]
    tile_match = weights[2]
    weight_up = jnp.pad(tile_row, ((0, 0), (0, 0), (1, 0)))[:, :, :-1]
    weight_left = jnp.pad(tile_col, ((0, 0), (1, 0), (0, 0)))[:, :-1, :]
    match_prior = jnp.pad(tile_match, ((1, 0), (0, 0), (0, 0)))[:-1]
    diagonal = tile_row + weight_up + tile_col + weight_left + tile_match + match_prior
    positions = jnp.zeros_like(flow_tiles)
    for iteration in range(ITERS):
        padded = jnp.pad(positions, ((0, 0), (0, 0), (1, 1), (1, 1)))
        following = jnp.pad(positions, ((0, 0), (0, 1), (0, 0), (0, 0)))[:, 1:]
        pull_term = tile_match * (following - positions - flow_tiles)
        pull_prior = jnp.pad(pull_term, ((0, 0), (1, 0), (0, 0), (0, 0)))[:, :-1]
        positions = advance(
            positions,
            padded[:, :, 1:-1, 2:],
            padded[:, :, 1:-1, :-2],
            padded[:, :, 2:, 1:-1],
            padded[:, :, :-2, 1:-1],
            tile_row,
            weight_up,
            tile_col,
            weight_left,
            pull_term,
            pull_prior,
            diagonal,
        )
    core = positions[:, :, halo:-halo, halo:-halo]
    returned = lax.all_to_all(core, "sec", split_axis=1, concat_axis=2, tiled=True)
    return jnp.transpose(returned, (0, 1, 3, 2))


def solution(mesh):
    in_specs = (
        P("sec", "strip", None),
        P(),
        P(None, "sec", "strip", None),
        P("sec", "strip", None),
    )
    out_specs = P(None, "sec", "strip", None)
    return jax.shard_map(shards, mesh=mesh, in_specs=in_specs, out_specs=out_specs, check_vma=False)
```

```python
import jax
import jax.numpy as jnp
from jax import lax
from jax.experimental import pallas as pl
from jax.experimental.pallas import tpu as pltpu
from jax.sharding import PartitionSpec as P

RAD = 3
ITERS = 8


sharpness = 0.5
relax_rate = 0.8


def shifted_2(shard, axis, by):
    size = lax.axis_size(axis)
    pairs = [(i, i + by) for i in range(size) if 0 <= i + by < size]
    return lax.ppermute(shard, axis, pairs)


def extended(cells, sides, width):
    for axis, dim in sides:
        count = lax.axis_size(axis)
        ends = count - 1
        head = lax.slice_in_dim(cells, 0, width, axis=dim)
        tail = lax.slice_in_dim(cells, cells.shape[dim] - width, cells.shape[dim], axis=dim)
        cells = jnp.concatenate(
            [
                lax.ppermute(tail, axis, [(i, (i + 1) % count) for i in range(ends)]),
                cells,
                lax.ppermute(head, axis, [((i + 1) % count, i) for i in range(ends)]),
            ],
            axis=dim,
        )
    return cells


def lane_permutation():
    source = jnp.arange(512, dtype=jnp.int32)[:, None]
    target = jnp.arange(512, dtype=jnp.int32)[None, :]
    return ((source % 4) * 128 + source // 4 == target).astype(jnp.bfloat16)


def split_phases(pixels, permute, lanes_ref, phase_ref, node_rows):
    chunks = pixels.shape[1] // 512
    for c in range(chunks):
        permuted = jnp.dot(pixels[:, c * 512 : (c + 1) * 512], permute, preferred_element_type=jnp.float32)
        for t in range(4):
            lanes_ref[c * 4 + t, 0 : pixels.shape[0], :] = permuted[:, t * 128 : (t + 1) * 128]
    for q in range(4):
        for t in range(4):
            parts = [lanes_ref[pl.ds(c * 4 + t, 1), pl.ds(q, node_rows, stride=4), :][0] for c in range(chunks)]
            phase_ref[q * 4 + t] = jnp.concatenate(parts, axis=1)


def flow_kernel(
    offsets_ref, current_ref, following_ref, permute_ref, flow_ref, current_ph, following_ph, lanes_ref, shifted_ref, scores_ref
):
    tile_rows = current_ph.shape[1]
    node_cols = current_ph.shape[2]
    window = following_ph.shape[1]
    base = pl.multiple_of(pl.program_id(0) * tile_rows * 4, 32)
    permute = permute_ref[...]
    split_phases(current_ref[...], permute, lanes_ref, current_ph, tile_rows)
    split_phases(following_ref[pl.ds(base, window * 4), :], permute, lanes_ref, following_ph, window)
    column = lax.broadcasted_iota(jnp.int32, (window, node_cols), 1)

    def build(phase, carry):
        block = following_ph[phase]
        for col_shift in range(3):
            if col_shift == 1:
                moved = block
            else:
                moved = pltpu.roll(block, (1 - col_shift) % node_cols, 1)
                inside = (column + col_shift - 1 >= 0) & (column + col_shift - 1 < node_cols)
                moved = jnp.where(inside, moved, 0.0)
            for row_shift in range(3):
                rows = moved if row_shift == 0 else pltpu.roll(moved, window - row_shift, 0)
                shifted_ref[(row_shift * 3 + col_shift) * 16 + phase] = rows[:tile_rows]
        return carry

    lax.fori_loop(0, 16, build, 0)
    chunks = tile_rows // 8
    offset_count = scores_ref.shape[0]

    def score(k, carry):
        row_off = offsets_ref[k, 0]
        col_off = offsets_ref[k, 1]
        sources = []
        for q in range(4):
            u = q + row_off + 4
            u_node, u_phase = lax.shift_right_logical(u, 2), u & 3
            for t in range(4):
                v = t + col_off + 4
                v_node, v_phase = lax.shift_right_logical(v, 2), v & 3
                sources.append((u_node * 3 + v_node) * 16 + u_phase * 4 + v_phase)
        for c in range(chunks):
            rows = pl.ds(c * 8, 8)
            acc = current_ph[0, rows, :] * shifted_ref[sources[0], rows, :]
            for p in range(1, 16):
                acc = acc + current_ph[p, rows, :] * shifted_ref[sources[p], rows, :]
            scores_ref[k, rows, :] = sharpness * acc
        return carry

    lax.fori_loop(0, offset_count, score, 0)
    for c in range(chunks):
        rows = pl.ds(c * 8, 8)
        highest = scores_ref[0, rows, :]
        for k in range(1, offset_count):
            highest = jnp.maximum(highest, scores_ref[k, rows, :])
        weight_sum = jnp.zeros_like(highest)
        row_sum = jnp.zeros_like(highest)
        col_sum = jnp.zeros_like(highest)
        for k in range(offset_count):
            weight = jnp.exp(scores_ref[k, rows, :] - highest)
            weight_sum = weight_sum + weight
            row_sum = row_sum + weight * offsets_ref[k, 0].astype(jnp.float32)
            col_sum = col_sum + weight * offsets_ref[k, 1].astype(jnp.float32)
        flow_ref[0, rows, :] = row_sum / weight_sum
        flow_ref[1, rows, :] = col_sum / weight_sum


def section_flow(current, following, offsets, tile_rows=32):
    row_count, col_count = current.shape
    node_rows, node_cols = row_count // 4, col_count // 4
    window = tile_rows + 8
    padded = jnp.pad(following, ((4 - RAD, (node_rows + 8) * 4 - following.shape[0] - (4 - RAD)), (0, 0)))
    offset_count = offsets.shape[0]
    grid_spec = pltpu.PrefetchScalarGridSpec(
        num_scalar_prefetch=1,
        grid=(node_rows // tile_rows,),
        in_specs=[
            pl.BlockSpec((tile_rows * 4, col_count), lambda g, off: (g, 0)),
            pl.BlockSpec(padded.shape, lambda g, off: (0, 0)),
            pl.BlockSpec((512, 512), lambda g, off: (0, 0)),
        ],
        out_specs=pl.BlockSpec((2, tile_rows, node_cols), lambda g, off: (0, g, 0)),
        scratch_shapes=[
            pltpu.VMEM((16, tile_rows, node_cols), jnp.float32),
            pltpu.VMEM((16, window, node_cols), jnp.float32),
            pltpu.VMEM((col_count // 128, window * 4, 128), jnp.float32),
            pltpu.VMEM((144, tile_rows, node_cols), jnp.float32),
            pltpu.VMEM((offset_count, tile_rows, node_cols), jnp.float32),
        ],
    )
    return pl.pallas_call(
        flow_kernel,
        grid_spec=grid_spec,
        out_shape=jax.ShapeDtypeStruct((2, node_rows, node_cols), jnp.float32),
        compiler_params=pltpu.CompilerParams(
            dimension_semantics=("arbitrary",), vmem_limit_bytes=48 * 1024 * 1024
        ),
    )(offsets, current, padded, lane_permutation())


def advance(
    positions,
    from_below,
    from_above,
    from_right,
    from_left,
    row_weight,
    weight_up,
    col_weight,
    weight_left,
    pull_term,
    pull_prior,
    diagonal,
):
    force = row_weight * (from_below - positions) + weight_up * (from_above - positions)
    force = force + col_weight * (from_right - positions) + weight_left * (from_left - positions)
    force = force + pull_term - pull_prior
    return positions + relax_rate * force / (1.0 + diagonal)


def tiles_with_halo(fields, halo):
    count = lax.axis_size("sec")
    columns = jnp.transpose(fields, (0, 2, 1))
    width = columns.shape[1] // count
    columns = jnp.pad(columns, ((0, 0), (halo, halo), (0, 0)))
    windows = jnp.stack([columns[:, j * width : (j + 1) * width + 2 * halo] for j in range(count)], axis=1)
    return lax.all_to_all(windows, "sec", split_axis=1, concat_axis=1, tiled=True)


def shards(images, offsets, springs, validity):
    pixels = images[0]
    half = pixels.shape[0] // 2
    sec_count = lax.axis_size("sec")
    strip_count = lax.axis_size("strip")
    successor_top = shifted_2(pixels[: half + RAD], "sec", -1)
    prior_bottom = shifted_2(pixels[half:], "sec", 1)
    corner = lax.ppermute(
        pixels[-RAD:],
        ("sec", "strip"),
        [((s + 1) * strip_count + p - 1, s * strip_count + p) for s in range(sec_count - 1) for p in range(1, strip_count)],
    )
    below = shifted_2(pixels[:RAD], "strip", -1)
    keep_mask = (lax.axis_index("sec") < sec_count - 1).astype(jnp.float32)
    springs, validity, prior_bottom = lax.optimization_barrier((springs, validity, prior_bottom))
    match_weight = validity[0].astype(jnp.float32) * keep_mask
    node_rows, node_cols = (springs.shape[2], springs.shape[3])
    global_rows = lax.axis_index("strip") * node_rows + jnp.arange(node_rows, dtype=jnp.int32)
    row_keep = (global_rows < node_rows * lax.axis_size("strip") - 1).astype(jnp.float32)
    col_keep = (jnp.arange(node_cols) < node_cols - 1).astype(jnp.float32)
    row_weight = 0.25 * springs[0, 0].astype(jnp.float32) * row_keep[:, None]
    col_weight = 0.25 * springs[1, 0].astype(jnp.float32) * col_keep[None, :]
    halo = ITERS
    weights = jnp.stack([row_weight, col_weight, match_weight]).astype(jnp.bfloat16)
    weights = extended(tiles_with_halo(weights, halo), (("strip", 3),), halo).astype(jnp.float32)
    flow_top = section_flow(pixels[:half], jnp.concatenate([corner, successor_top]), offsets) * keep_mask
    flow_bottom = section_flow(prior_bottom, jnp.concatenate([pixels[half - RAD :], below]), offsets)
    flow_field = jnp.concatenate([flow_top, flow_bottom], axis=1)
    tiled = tiles_with_halo(flow_field, halo)
    node_half = tiled.shape[3] // 2
    bottoms = tiled[:, 1:, :, node_half:]
    bottoms = jnp.concatenate([bottoms, jnp.zeros_like(bottoms[:, :1])], axis=1)
    tiled = jnp.concatenate([tiled[:, :, :, :node_half], bottoms], axis=3)
    flow_tiles = extended(tiled, (("strip", 3),), halo)
    tile_row = weights[0]
    tile_col = weights[1]
    tile_match = weights[2]
    weight_up = jnp.pad(tile_row, ((0, 0), (0, 0), (1, 0)))[:, :, :-1]
    weight_left = jnp.pad(tile_col, ((0, 0), (1, 0), (0, 0)))[:, :-1, :]
    match_prior = jnp.pad(tile_match, ((1, 0), (0, 0), (0, 0)))[:-1]
    diagonal = tile_row + weight_up + tile_col + weight_left + tile_match + match_prior
    positions = jnp.zeros_like(flow_tiles)
    for iteration in range(ITERS):
        padded = jnp.pad(positions, ((0, 0), (0, 0), (1, 1), (1, 1)))
        following = jnp.pad(positions, ((0, 0), (0, 1), (0, 0), (0, 0)))[:, 1:]
        pull_term = tile_match * (following - positions - flow_tiles)
        pull_prior = jnp.pad(pull_term, ((0, 0), (1, 0), (0, 0), (0, 0)))[:, :-1]
        positions = advance(
            positions,
            padded[:, :, 1:-1, 2:],
            padded[:, :, 1:-1, :-2],
            padded[:, :, 2:, 1:-1],
            padded[:, :, :-2, 1:-1],
            tile_row,
            weight_up,
            tile_col,
            weight_left,
            pull_term,
            pull_prior,
            diagonal,
        )
    core = positions[:, :, halo:-halo, halo:-halo]
    returned = lax.all_to_all(core, "sec", split_axis=1, concat_axis=2, tiled=True)
    return jnp.transpose(returned, (0, 1, 3, 2))


def solution(mesh):
    in_specs = (
        P("sec", "strip", None),
        P(),
        P(None, "sec", "strip", None),
        P("sec", "strip", None),
    )
    out_specs = P(None, "sec", "strip", None)
    return jax.shard_map(shards, mesh=mesh, in_specs=in_specs, out_specs=out_specs, check_vma=False)
```

```python
import jax
import jax.numpy as jnp
from jax import lax
from jax.experimental import pallas as pl
from jax.experimental.pallas import tpu as pltpu
from jax.sharding import PartitionSpec as P

RAD = 3
ITERS = 8


sharpness = 0.5
relax_rate = 0.8


def shifted_2(shard, axis, by):
    size = lax.axis_size(axis)
    pairs = [(i, i + by) for i in range(size) if 0 <= i + by < size]
    return lax.ppermute(shard, axis, pairs)


def extended(cells, sides, width):
    for axis, dim in sides:
        count = lax.axis_size(axis)
        ends = count - 1
        head = lax.slice_in_dim(cells, 0, width, axis=dim)
        tail = lax.slice_in_dim(cells, cells.shape[dim] - width, cells.shape[dim], axis=dim)
        cells = jnp.concatenate(
            [
                lax.ppermute(tail, axis, [(i, (i + 1) % count) for i in range(ends)]),
                cells,
                lax.ppermute(head, axis, [((i + 1) % count, i) for i in range(ends)]),
            ],
            axis=dim,
        )
    return cells


def lane_permutation():
    source = jnp.arange(512, dtype=jnp.int32)[:, None]
    target = jnp.arange(512, dtype=jnp.int32)[None, :]
    return ((source % 4) * 128 + source // 4 == target).astype(jnp.bfloat16)


def split_phases(pixels, permute, lanes_ref, phase_ref, node_rows):
    chunks = pixels.shape[1] // 512
    for c in range(chunks):
        permuted = jnp.dot(pixels[:, c * 512 : (c + 1) * 512], permute, preferred_element_type=jnp.float32)
        for t in range(4):
            lanes_ref[c * 4 + t, 0 : pixels.shape[0], :] = permuted[:, t * 128 : (t + 1) * 128]
    for q in range(4):
        for t in range(4):
            parts = [lanes_ref[pl.ds(c * 4 + t, 1), pl.ds(q, node_rows, stride=4), :][0] for c in range(chunks)]
            phase_ref[q * 4 + t] = jnp.concatenate(parts, axis=1)


def flow_kernel(
    offsets_ref, current_ref, following_ref, permute_ref, flow_ref, current_ph, following_ph, lanes_ref, shifted_ref, scores_ref
):
    tile_rows = current_ph.shape[1]
    node_cols = current_ph.shape[2]
    window = following_ph.shape[1]
    base = pl.multiple_of(pl.program_id(0) * tile_rows * 4, 32)
    permute = permute_ref[...]
    split_phases(current_ref[...], permute, lanes_ref, current_ph, tile_rows)
    split_phases(following_ref[pl.ds(base, window * 4), :], permute, lanes_ref, following_ph, window)
    column = lax.broadcasted_iota(jnp.int32, (window, node_cols), 1)

    def build(phase, carry):
        block = following_ph[phase]
        for col_shift in range(3):
            if col_shift == 1:
                moved = block
            else:
                moved = pltpu.roll(block, (1 - col_shift) % node_cols, 1)
                inside = (column + col_shift - 1 >= 0) & (column + col_shift - 1 < node_cols)
                moved = jnp.where(inside, moved, 0.0)
            for row_shift in range(3):
                rows = moved if row_shift == 0 else pltpu.roll(moved, window - row_shift, 0)
                shifted_ref[(row_shift * 3 + col_shift) * 16 + phase] = rows[:tile_rows]
        return carry

    lax.fori_loop(0, 16, build, 0)
    chunks = tile_rows // 8
    offset_count = scores_ref.shape[0]

    def score(k, carry):
        row_off = offsets_ref[k, 0]
        col_off = offsets_ref[k, 1]
        sources = []
        for q in range(4):
            u = q + row_off + 4
            u_node, u_phase = lax.shift_right_logical(u, 2), u & 3
            for t in range(4):
                v = t + col_off + 4
                v_node, v_phase = lax.shift_right_logical(v, 2), v & 3
                sources.append((u_node * 3 + v_node) * 16 + u_phase * 4 + v_phase)
        for c in range(chunks):
            rows = pl.ds(c * 8, 8)
            acc = current_ph[0, rows, :] * shifted_ref[sources[0], rows, :]
            for p in range(1, 16):
                acc = acc + current_ph[p, rows, :] * shifted_ref[sources[p], rows, :]
            scores_ref[k, rows, :] = sharpness * acc
        return carry

    lax.fori_loop(0, offset_count, score, 0)
    for c in range(chunks):
        rows = pl.ds(c * 8, 8)
        highest = scores_ref[0, rows, :]
        for k in range(1, offset_count):
            highest = jnp.maximum(highest, scores_ref[k, rows, :])
        weight_sum = jnp.zeros_like(highest)
        row_sum = jnp.zeros_like(highest)
        col_sum = jnp.zeros_like(highest)
        for k in range(offset_count):
            weight = jnp.exp(scores_ref[k, rows, :] - highest)
            weight_sum = weight_sum + weight
            row_sum = row_sum + weight * offsets_ref[k, 0].astype(jnp.float32)
            col_sum = col_sum + weight * offsets_ref[k, 1].astype(jnp.float32)
        flow_ref[0, rows, :] = row_sum / weight_sum
        flow_ref[1, rows, :] = col_sum / weight_sum


def section_flow(current, following, offsets, tile_rows=32):
    row_count, col_count = current.shape
    node_rows, node_cols = row_count // 4, col_count // 4
    window = tile_rows + 8
    padded = jnp.pad(following, ((4 - RAD, (node_rows + 8) * 4 - following.shape[0] - (4 - RAD)), (0, 0)))
    offset_count = offsets.shape[0]
    grid_spec = pltpu.PrefetchScalarGridSpec(
        num_scalar_prefetch=1,
        grid=(node_rows // tile_rows,),
        in_specs=[
            pl.BlockSpec((tile_rows * 4, col_count), lambda g, off: (g, 0)),
            pl.BlockSpec(padded.shape, lambda g, off: (0, 0)),
            pl.BlockSpec((512, 512), lambda g, off: (0, 0)),
        ],
        out_specs=pl.BlockSpec((2, tile_rows, node_cols), lambda g, off: (0, g, 0)),
        scratch_shapes=[
            pltpu.VMEM((16, tile_rows, node_cols), jnp.float32),
            pltpu.VMEM((16, window, node_cols), jnp.float32),
            pltpu.VMEM((col_count // 128, window * 4, 128), jnp.float32),
            pltpu.VMEM((144, tile_rows, node_cols), jnp.float32),
            pltpu.VMEM((offset_count, tile_rows, node_cols), jnp.float32),
        ],
    )
    return pl.pallas_call(
        flow_kernel,
        grid_spec=grid_spec,
        out_shape=jax.ShapeDtypeStruct((2, node_rows, node_cols), jnp.float32),
        compiler_params=pltpu.CompilerParams(
            dimension_semantics=("arbitrary",), vmem_limit_bytes=48 * 1024 * 1024
        ),
    )(offsets, current, padded, lane_permutation())


def advance(
    positions,
    from_below,
    from_above,
    from_right,
    from_left,
    row_weight,
    weight_up,
    col_weight,
    weight_left,
    pull_term,
    pull_prior,
    diagonal,
):
    force = row_weight * (from_below - positions) + weight_up * (from_above - positions)
    force = force + col_weight * (from_right - positions) + weight_left * (from_left - positions)
    force = force + pull_term - pull_prior
    return positions + relax_rate * force / (1.0 + diagonal)


def tiles_with_halo(fields, halo):
    count = lax.axis_size("sec")
    columns = jnp.transpose(fields, (0, 2, 1))
    width = columns.shape[1] // count
    columns = jnp.pad(columns, ((0, 0), (halo, halo), (0, 0)))
    windows = jnp.stack([columns[:, j * width : (j + 1) * width + 2 * halo] for j in range(count)], axis=1)
    return lax.all_to_all(windows, "sec", split_axis=1, concat_axis=1, tiled=True)


def shards(images, offsets, springs, validity):
    pixels = images[0]
    half = pixels.shape[0] // 2
    sec_count = lax.axis_size("sec")
    strip_count = lax.axis_size("strip")
    quarter = half // 2
    successor_first = shifted_2(pixels[: quarter + RAD], "sec", -1)
    successor_second = shifted_2(pixels[quarter + RAD : half + RAD], "sec", -1)
    prior_first = shifted_2(pixels[half : half + quarter], "sec", 1)
    prior_second = shifted_2(pixels[half + quarter :], "sec", 1)
    corner = lax.ppermute(
        pixels[-RAD:],
        ("sec", "strip"),
        [((s + 1) * strip_count + p - 1, s * strip_count + p) for s in range(sec_count - 1) for p in range(1, strip_count)],
    )
    below = shifted_2(pixels[:RAD], "strip", -1)
    keep_mask = (lax.axis_index("sec") < sec_count - 1).astype(jnp.float32)
    springs, validity, prior_first = lax.optimization_barrier((springs, validity, prior_first))
    match_weight = validity[0].astype(jnp.float32) * keep_mask
    node_rows, node_cols = (springs.shape[2], springs.shape[3])
    global_rows = lax.axis_index("strip") * node_rows + jnp.arange(node_rows, dtype=jnp.int32)
    row_keep = (global_rows < node_rows * lax.axis_size("strip") - 1).astype(jnp.float32)
    col_keep = (jnp.arange(node_cols) < node_cols - 1).astype(jnp.float32)
    row_weight = 0.25 * springs[0, 0].astype(jnp.float32) * row_keep[:, None]
    col_weight = 0.25 * springs[1, 0].astype(jnp.float32) * col_keep[None, :]
    halo = ITERS
    weights = jnp.stack([row_weight, col_weight, match_weight]).astype(jnp.bfloat16)
    weights = extended(tiles_with_halo(weights, halo), (("strip", 3),), halo).astype(jnp.float32)
    first_top = section_flow(pixels[:quarter], jnp.concatenate([corner, successor_first]), offsets)
    first_bottom = section_flow(prior_first, pixels[half - RAD : half + quarter + RAD], offsets)
    second_top = section_flow(
        pixels[quarter:half], jnp.concatenate([successor_first[quarter - RAD :], successor_second]), offsets
    )
    second_bottom = section_flow(prior_second, jnp.concatenate([pixels[half + quarter - RAD :], below]), offsets)
    flow_field = jnp.concatenate(
        [first_top * keep_mask, second_top * keep_mask, first_bottom, second_bottom], axis=1
    )
    tiled = tiles_with_halo(flow_field, halo)
    node_half = tiled.shape[3] // 2
    bottoms = tiled[:, 1:, :, node_half:]
    bottoms = jnp.concatenate([bottoms, jnp.zeros_like(bottoms[:, :1])], axis=1)
    tiled = jnp.concatenate([tiled[:, :, :, :node_half], bottoms], axis=3)
    flow_tiles = extended(tiled, (("strip", 3),), halo)
    tile_row = weights[0]
    tile_col = weights[1]
    tile_match = weights[2]
    weight_up = jnp.pad(tile_row, ((0, 0), (0, 0), (1, 0)))[:, :, :-1]
    weight_left = jnp.pad(tile_col, ((0, 0), (1, 0), (0, 0)))[:, :-1, :]
    match_prior = jnp.pad(tile_match, ((1, 0), (0, 0), (0, 0)))[:-1]
    diagonal = tile_row + weight_up + tile_col + weight_left + tile_match + match_prior
    positions = jnp.zeros_like(flow_tiles)
    for iteration in range(ITERS):
        padded = jnp.pad(positions, ((0, 0), (0, 0), (1, 1), (1, 1)))
        following = jnp.pad(positions, ((0, 0), (0, 1), (0, 0), (0, 0)))[:, 1:]
        pull_term = tile_match * (following - positions - flow_tiles)
        pull_prior = jnp.pad(pull_term, ((0, 0), (1, 0), (0, 0), (0, 0)))[:, :-1]
        positions = advance(
            positions,
            padded[:, :, 1:-1, 2:],
            padded[:, :, 1:-1, :-2],
            padded[:, :, 2:, 1:-1],
            padded[:, :, :-2, 1:-1],
            tile_row,
            weight_up,
            tile_col,
            weight_left,
            pull_term,
            pull_prior,
            diagonal,
        )
    core = positions[:, :, halo:-halo, halo:-halo]
    returned = lax.all_to_all(core, "sec", split_axis=1, concat_axis=2, tiled=True)
    return jnp.transpose(returned, (0, 1, 3, 2))


def solution(mesh):
    in_specs = (
        P("sec", "strip", None),
        P(),
        P(None, "sec", "strip", None),
        P("sec", "strip", None),
    )
    out_specs = P(None, "sec", "strip", None)
    return jax.shard_map(shards, mesh=mesh, in_specs=in_specs, out_specs=out_specs, check_vma=False)
```

```python
import jax
import jax.numpy as jnp
from jax import lax
from jax.experimental import pallas as pl
from jax.experimental.pallas import tpu as pltpu
from jax.sharding import PartitionSpec as P

RAD = 3
ITERS = 8


sharpness = 0.5
relax_rate = 0.8


def shifted_2(shard, axis, by):
    size = lax.axis_size(axis)
    pairs = [(i, i + by) for i in range(size) if 0 <= i + by < size]
    return lax.ppermute(shard, axis, pairs)


def extended(cells, sides, width):
    for axis, dim in sides:
        count = lax.axis_size(axis)
        ends = count - 1
        head = lax.slice_in_dim(cells, 0, width, axis=dim)
        tail = lax.slice_in_dim(cells, cells.shape[dim] - width, cells.shape[dim], axis=dim)
        cells = jnp.concatenate(
            [
                lax.ppermute(tail, axis, [(i, (i + 1) % count) for i in range(ends)]),
                cells,
                lax.ppermute(head, axis, [((i + 1) % count, i) for i in range(ends)]),
            ],
            axis=dim,
        )
    return cells


def lane_permutation():
    source = jnp.arange(512, dtype=jnp.int32)[:, None]
    target = jnp.arange(512, dtype=jnp.int32)[None, :]
    return ((source % 4) * 128 + source // 4 == target).astype(jnp.bfloat16)


def split_phases(pixels, permute, lanes_ref, phase_ref, node_rows):
    chunks = pixels.shape[1] // 512
    for c in range(chunks):
        permuted = jnp.dot(pixels[:, c * 512 : (c + 1) * 512], permute, preferred_element_type=jnp.float32)
        for t in range(4):
            lanes_ref[c * 4 + t, 0 : pixels.shape[0], :] = permuted[:, t * 128 : (t + 1) * 128]
    for q in range(4):
        for t in range(4):
            parts = [lanes_ref[pl.ds(c * 4 + t, 1), pl.ds(q, node_rows, stride=4), :][0] for c in range(chunks)]
            phase_ref[q * 4 + t] = jnp.concatenate(parts, axis=1)


def flow_kernel(
    offsets_ref, current_ref, following_ref, permute_ref, flow_ref, current_ph, following_ph, lanes_ref, shifted_ref, scores_ref
):
    tile_rows = current_ph.shape[1]
    node_cols = current_ph.shape[2]
    window = following_ph.shape[1]
    base = pl.multiple_of(pl.program_id(0) * tile_rows * 4, 32)
    permute = permute_ref[...]
    split_phases(current_ref[...], permute, lanes_ref, current_ph, tile_rows)
    split_phases(following_ref[pl.ds(base, window * 4), :], permute, lanes_ref, following_ph, window)
    column = lax.broadcasted_iota(jnp.int32, (window, node_cols), 1)

    def build(phase, carry):
        block = following_ph[phase]
        for col_shift in range(3):
            if col_shift == 1:
                moved = block
            else:
                moved = pltpu.roll(block, (1 - col_shift) % node_cols, 1)
                inside = (column + col_shift - 1 >= 0) & (column + col_shift - 1 < node_cols)
                moved = jnp.where(inside, moved, 0.0)
            for row_shift in range(3):
                rows = moved if row_shift == 0 else pltpu.roll(moved, window - row_shift, 0)
                shifted_ref[(row_shift * 3 + col_shift) * 16 + phase] = rows[:tile_rows]
        return carry

    lax.fori_loop(0, 16, build, 0)
    chunks = tile_rows // 8
    offset_count = scores_ref.shape[0]

    def score(k, carry):
        row_off = offsets_ref[k, 0]
        col_off = offsets_ref[k, 1]
        sources = []
        for q in range(4):
            u = q + row_off + 4
            u_node, u_phase = lax.shift_right_logical(u, 2), u & 3
            for t in range(4):
                v = t + col_off + 4
                v_node, v_phase = lax.shift_right_logical(v, 2), v & 3
                sources.append((u_node * 3 + v_node) * 16 + u_phase * 4 + v_phase)
        for c in range(chunks):
            rows = pl.ds(c * 8, 8)
            acc = current_ph[0, rows, :] * shifted_ref[sources[0], rows, :]
            for p in range(1, 16):
                acc = acc + current_ph[p, rows, :] * shifted_ref[sources[p], rows, :]
            scores_ref[k, rows, :] = sharpness * acc
        return carry

    lax.fori_loop(0, offset_count, score, 0)
    for c in range(chunks):
        rows = pl.ds(c * 8, 8)
        highest = scores_ref[0, rows, :]
        for k in range(1, offset_count):
            highest = jnp.maximum(highest, scores_ref[k, rows, :])
        weight_sum = jnp.zeros_like(highest)
        row_sum = jnp.zeros_like(highest)
        col_sum = jnp.zeros_like(highest)
        for k in range(offset_count):
            weight = jnp.exp(scores_ref[k, rows, :] - highest)
            weight_sum = weight_sum + weight
            row_sum = row_sum + weight * offsets_ref[k, 0].astype(jnp.float32)
            col_sum = col_sum + weight * offsets_ref[k, 1].astype(jnp.float32)
        flow_ref[0, rows, :] = row_sum / weight_sum
        flow_ref[1, rows, :] = col_sum / weight_sum


def section_flow(current, following, offsets, tile_rows=32):
    row_count, col_count = current.shape
    node_rows, node_cols = row_count // 4, col_count // 4
    window = tile_rows + 8
    padded = jnp.pad(following, ((4 - RAD, (node_rows + 8) * 4 - following.shape[0] - (4 - RAD)), (0, 0)))
    offset_count = offsets.shape[0]
    grid_spec = pltpu.PrefetchScalarGridSpec(
        num_scalar_prefetch=1,
        grid=(node_rows // tile_rows,),
        in_specs=[
            pl.BlockSpec((tile_rows * 4, col_count), lambda g, off: (g, 0)),
            pl.BlockSpec(padded.shape, lambda g, off: (0, 0)),
            pl.BlockSpec((512, 512), lambda g, off: (0, 0)),
        ],
        out_specs=pl.BlockSpec((2, tile_rows, node_cols), lambda g, off: (0, g, 0)),
        scratch_shapes=[
            pltpu.VMEM((16, tile_rows, node_cols), jnp.float32),
            pltpu.VMEM((16, window, node_cols), jnp.float32),
            pltpu.VMEM((col_count // 128, window * 4, 128), jnp.float32),
            pltpu.VMEM((144, tile_rows, node_cols), jnp.float32),
            pltpu.VMEM((offset_count, tile_rows, node_cols), jnp.float32),
        ],
    )
    return pl.pallas_call(
        flow_kernel,
        grid_spec=grid_spec,
        out_shape=jax.ShapeDtypeStruct((2, node_rows, node_cols), jnp.float32),
        compiler_params=pltpu.CompilerParams(
            dimension_semantics=("arbitrary",), vmem_limit_bytes=48 * 1024 * 1024
        ),
    )(offsets, current, padded, lane_permutation())


def advance(
    positions,
    from_below,
    from_above,
    from_right,
    from_left,
    row_weight,
    weight_up,
    col_weight,
    weight_left,
    pull_term,
    pull_prior,
    diagonal,
):
    force = row_weight * (from_below - positions) + weight_up * (from_above - positions)
    force = force + col_weight * (from_right - positions) + weight_left * (from_left - positions)
    force = force + pull_term - pull_prior
    return positions + relax_rate * force / (1.0 + diagonal)


def tiles_with_halo(fields, halo):
    count = lax.axis_size("sec")
    fields = extended(fields, (("strip", 1),), halo)
    width = fields.shape[2] // count
    columns = jnp.pad(fields, ((0, 0), (0, 0), (halo, halo)))
    windows = jnp.stack([columns[:, :, j * width : (j + 1) * width + 2 * halo] for j in range(count)], axis=1)
    return lax.all_to_all(windows, "sec", split_axis=1, concat_axis=1, tiled=True)


def shards(images, offsets, springs, validity):
    pixels = images[0]
    half = pixels.shape[0] // 2
    sec_count = lax.axis_size("sec")
    strip_count = lax.axis_size("strip")
    successor_top = shifted_2(pixels[: half + RAD], "sec", -1)
    prior_bottom = shifted_2(pixels[half:], "sec", 1)
    corner = lax.ppermute(
        pixels[-RAD:],
        ("sec", "strip"),
        [((s + 1) * strip_count + p - 1, s * strip_count + p) for s in range(sec_count - 1) for p in range(1, strip_count)],
    )
    below = shifted_2(pixels[:RAD], "strip", -1)
    keep_mask = (lax.axis_index("sec") < sec_count - 1).astype(jnp.float32)
    springs, validity, prior_bottom = lax.optimization_barrier((springs, validity, prior_bottom))
    match_weight = validity[0].astype(jnp.float32) * keep_mask
    node_rows, node_cols = (springs.shape[2], springs.shape[3])
    global_rows = lax.axis_index("strip") * node_rows + jnp.arange(node_rows, dtype=jnp.int32)
    row_keep = (global_rows < node_rows * lax.axis_size("strip") - 1).astype(jnp.float32)
    col_keep = (jnp.arange(node_cols) < node_cols - 1).astype(jnp.float32)
    row_weight = 0.25 * springs[0, 0].astype(jnp.float32) * row_keep[:, None]
    col_weight = 0.25 * springs[1, 0].astype(jnp.float32) * col_keep[None, :]
    halo = ITERS
    weights = jnp.stack([row_weight, col_weight, match_weight]).astype(jnp.bfloat16)
    weights = tiles_with_halo(weights, halo).astype(jnp.float32)
    flow_top = section_flow(pixels[:half], jnp.concatenate([corner, successor_top]), offsets) * keep_mask
    flow_bottom = section_flow(prior_bottom, jnp.concatenate([pixels[half - RAD :], below]), offsets)
    flow_field = jnp.concatenate([flow_top, flow_bottom], axis=1)
    tiled = tiles_with_halo(flow_field, halo)
    node_half = flow_field.shape[1] // 2
    following = jnp.concatenate([tiled[:, 1:], jnp.zeros_like(tiled[:, :1])], axis=1)
    row_ids = jnp.arange(tiled.shape[2], dtype=jnp.int32)[:, None]
    from_prior = (row_ids < halo) | ((row_ids >= halo + node_half) & (row_ids < halo + 2 * node_half))
    flow_tiles = jnp.where(from_prior, following, tiled)
    tile_row = weights[0]
    tile_col = weights[1]
    tile_match = weights[2]
    weight_up = jnp.pad(tile_row, ((0, 0), (1, 0), (0, 0)))[:, :-1, :]
    weight_left = jnp.pad(tile_col, ((0, 0), (0, 0), (1, 0)))[:, :, :-1]
    match_prior = jnp.pad(tile_match, ((1, 0), (0, 0), (0, 0)))[:-1]
    diagonal = tile_row + weight_up + tile_col + weight_left + tile_match + match_prior
    positions = jnp.zeros_like(flow_tiles)
    for iteration in range(ITERS):
        padded = jnp.pad(positions, ((0, 0), (0, 0), (1, 1), (1, 1)))
        following = jnp.pad(positions, ((0, 0), (0, 1), (0, 0), (0, 0)))[:, 1:]
        pull_term = tile_match * (following - positions - flow_tiles)
        pull_prior = jnp.pad(pull_term, ((0, 0), (1, 0), (0, 0), (0, 0)))[:, :-1]
        positions = advance(
            positions,
            padded[:, :, 2:, 1:-1],
            padded[:, :, :-2, 1:-1],
            padded[:, :, 1:-1, 2:],
            padded[:, :, 1:-1, :-2],
            tile_row,
            weight_up,
            tile_col,
            weight_left,
            pull_term,
            pull_prior,
            diagonal,
        )
    core = positions[:, :, halo:-halo, halo:-halo]
    return lax.all_to_all(core, "sec", split_axis=1, concat_axis=3, tiled=True)


def solution(mesh):
    in_specs = (
        P("sec", "strip", None),
        P(),
        P(None, "sec", "strip", None),
        P("sec", "strip", None),
    )
    out_specs = P(None, "sec", "strip", None)
    return jax.shard_map(shards, mesh=mesh, in_specs=in_specs, out_specs=out_specs, check_vma=False)
```

```python
import jax
import jax.numpy as jnp
from jax import lax
from jax.experimental import pallas as pl
from jax.experimental.pallas import tpu as pltpu
from jax.sharding import PartitionSpec as P

RAD = 3
ITERS = 8


sharpness = 0.5
relax_rate = 0.8


def shifted_2(shard, axis, by):
    size = lax.axis_size(axis)
    pairs = [(i, i + by) for i in range(size) if 0 <= i + by < size]
    return lax.ppermute(shard, axis, pairs)


def extended(cells, sides, width):
    for axis, dim in sides:
        count = lax.axis_size(axis)
        ends = count - 1
        head = lax.slice_in_dim(cells, 0, width, axis=dim)
        tail = lax.slice_in_dim(cells, cells.shape[dim] - width, cells.shape[dim], axis=dim)
        cells = jnp.concatenate(
            [
                lax.ppermute(tail, axis, [(i, (i + 1) % count) for i in range(ends)]),
                cells,
                lax.ppermute(head, axis, [((i + 1) % count, i) for i in range(ends)]),
            ],
            axis=dim,
        )
    return cells


def lane_permutation():
    source = jnp.arange(512, dtype=jnp.int32)[:, None]
    target = jnp.arange(512, dtype=jnp.int32)[None, :]
    return ((source % 4) * 128 + source // 4 == target).astype(jnp.bfloat16)


def split_phases(pixels, permute, lanes_ref, phase_ref, node_rows):
    chunks = pixels.shape[1] // 512
    for c in range(chunks):
        permuted = jnp.dot(pixels[:, c * 512 : (c + 1) * 512], permute, preferred_element_type=jnp.float32)
        for t in range(4):
            lanes_ref[c * 4 + t, 0 : pixels.shape[0], :] = permuted[:, t * 128 : (t + 1) * 128]
    for q in range(4):
        for t in range(4):
            parts = [lanes_ref[pl.ds(c * 4 + t, 1), pl.ds(q, node_rows, stride=4), :][0] for c in range(chunks)]
            phase_ref[q * 4 + t] = jnp.concatenate(parts, axis=1)


def flow_kernel(
    offsets_ref, current_ref, following_ref, permute_ref, flow_ref, current_ph, following_ph, lanes_ref, shifted_ref, scores_ref
):
    tile_rows = current_ph.shape[1]
    node_cols = current_ph.shape[2]
    window = following_ph.shape[1]
    base = pl.multiple_of(pl.program_id(0) * tile_rows * 4, 32)
    permute = permute_ref[...]
    split_phases(current_ref[...], permute, lanes_ref, current_ph, tile_rows)
    split_phases(following_ref[pl.ds(base, window * 4), :], permute, lanes_ref, following_ph, window)
    column = lax.broadcasted_iota(jnp.int32, (window, node_cols), 1)

    def build(phase, carry):
        block = following_ph[phase]
        for col_shift in range(3):
            if col_shift == 1:
                moved = block
            else:
                moved = pltpu.roll(block, (1 - col_shift) % node_cols, 1)
                inside = (column + col_shift - 1 >= 0) & (column + col_shift - 1 < node_cols)
                moved = jnp.where(inside, moved, 0.0)
            for row_shift in range(3):
                rows = moved if row_shift == 0 else pltpu.roll(moved, window - row_shift, 0)
                shifted_ref[(row_shift * 3 + col_shift) * 16 + phase] = rows[:tile_rows]
        return carry

    lax.fori_loop(0, 16, build, 0)
    chunks = tile_rows // 8
    offset_count = scores_ref.shape[0]

    def score(k, carry):
        row_off = offsets_ref[k, 0]
        col_off = offsets_ref[k, 1]
        sources = []
        for q in range(4):
            u = q + row_off + 4
            u_node, u_phase = lax.shift_right_logical(u, 2), u & 3
            for t in range(4):
                v = t + col_off + 4
                v_node, v_phase = lax.shift_right_logical(v, 2), v & 3
                sources.append((u_node * 3 + v_node) * 16 + u_phase * 4 + v_phase)
        for c in range(chunks):
            rows = pl.ds(c * 8, 8)
            acc = current_ph[0, rows, :] * shifted_ref[sources[0], rows, :]
            for p in range(1, 16):
                acc = acc + current_ph[p, rows, :] * shifted_ref[sources[p], rows, :]
            scores_ref[k, rows, :] = sharpness * acc
        return carry

    lax.fori_loop(0, offset_count, score, 0)
    for c in range(chunks):
        rows = pl.ds(c * 8, 8)
        highest = scores_ref[0, rows, :]
        for k in range(1, offset_count):
            highest = jnp.maximum(highest, scores_ref[k, rows, :])
        weight_sum = jnp.zeros_like(highest)
        row_sum = jnp.zeros_like(highest)
        col_sum = jnp.zeros_like(highest)
        for k in range(offset_count):
            weight = jnp.exp(scores_ref[k, rows, :] - highest)
            weight_sum = weight_sum + weight
            row_sum = row_sum + weight * offsets_ref[k, 0].astype(jnp.float32)
            col_sum = col_sum + weight * offsets_ref[k, 1].astype(jnp.float32)
        flow_ref[0, rows, :] = row_sum / weight_sum
        flow_ref[1, rows, :] = col_sum / weight_sum


def section_flow(current, following, offsets, tile_rows=32):
    row_count, col_count = current.shape
    node_rows, node_cols = row_count // 4, col_count // 4
    window = tile_rows + 8
    padded = jnp.pad(following, ((4 - RAD, (node_rows + 8) * 4 - following.shape[0] - (4 - RAD)), (0, 0)))
    offset_count = offsets.shape[0]
    grid_spec = pltpu.PrefetchScalarGridSpec(
        num_scalar_prefetch=1,
        grid=(node_rows // tile_rows,),
        in_specs=[
            pl.BlockSpec((tile_rows * 4, col_count), lambda g, off: (g, 0)),
            pl.BlockSpec(padded.shape, lambda g, off: (0, 0)),
            pl.BlockSpec((512, 512), lambda g, off: (0, 0)),
        ],
        out_specs=pl.BlockSpec((2, tile_rows, node_cols), lambda g, off: (0, g, 0)),
        scratch_shapes=[
            pltpu.VMEM((16, tile_rows, node_cols), jnp.float32),
            pltpu.VMEM((16, window, node_cols), jnp.float32),
            pltpu.VMEM((col_count // 128, window * 4, 128), jnp.float32),
            pltpu.VMEM((144, tile_rows, node_cols), jnp.float32),
            pltpu.VMEM((offset_count, tile_rows, node_cols), jnp.float32),
        ],
    )
    return pl.pallas_call(
        flow_kernel,
        grid_spec=grid_spec,
        out_shape=jax.ShapeDtypeStruct((2, node_rows, node_cols), jnp.float32),
        compiler_params=pltpu.CompilerParams(
            dimension_semantics=("arbitrary",), vmem_limit_bytes=48 * 1024 * 1024
        ),
    )(offsets, current, padded, lane_permutation())


def advance(
    positions,
    from_below,
    from_above,
    from_right,
    from_left,
    row_weight,
    weight_up,
    col_weight,
    weight_left,
    pull_term,
    pull_prior,
    diagonal,
):
    force = row_weight * (from_below - positions) + weight_up * (from_above - positions)
    force = force + col_weight * (from_right - positions) + weight_left * (from_left - positions)
    force = force + pull_term - pull_prior
    return positions + relax_rate * force / (1.0 + diagonal)


def tiles_with_halo(fields, halo):
    count = lax.axis_size("sec")
    fields = extended(fields, (("strip", 1),), halo)
    width = fields.shape[2] // count
    columns = jnp.pad(fields, ((0, 0), (0, 0), (halo, halo)))
    windows = jnp.stack([columns[:, :, j * width : (j + 1) * width + 2 * halo] for j in range(count)], axis=1)
    shape = windows.shape
    flat = windows.reshape(shape[0], shape[1], shape[2] * shape[3])
    return lax.all_to_all(flat, "sec", split_axis=1, concat_axis=1, tiled=True).reshape(shape)


def shards(images, offsets, springs, validity):
    pixels = images[0]
    half = pixels.shape[0] // 2
    sec_count = lax.axis_size("sec")
    strip_count = lax.axis_size("strip")
    successor_top = shifted_2(pixels[: half + RAD], "sec", -1)
    prior_bottom = shifted_2(pixels[half:], "sec", 1)
    corner = lax.ppermute(
        pixels[-RAD:],
        ("sec", "strip"),
        [((s + 1) * strip_count + p - 1, s * strip_count + p) for s in range(sec_count - 1) for p in range(1, strip_count)],
    )
    below = shifted_2(pixels[:RAD], "strip", -1)
    keep_mask = (lax.axis_index("sec") < sec_count - 1).astype(jnp.float32)
    springs, validity, prior_bottom = lax.optimization_barrier((springs, validity, prior_bottom))
    match_weight = validity[0].astype(jnp.float32) * keep_mask
    node_rows, node_cols = (springs.shape[2], springs.shape[3])
    global_rows = lax.axis_index("strip") * node_rows + jnp.arange(node_rows, dtype=jnp.int32)
    row_keep = (global_rows < node_rows * lax.axis_size("strip") - 1).astype(jnp.float32)
    col_keep = (jnp.arange(node_cols) < node_cols - 1).astype(jnp.float32)
    row_weight = 0.25 * springs[0, 0].astype(jnp.float32) * row_keep[:, None]
    col_weight = 0.25 * springs[1, 0].astype(jnp.float32) * col_keep[None, :]
    halo = ITERS
    weights = jnp.stack([row_weight, col_weight, match_weight]).astype(jnp.bfloat16)
    weights = tiles_with_halo(weights, halo).astype(jnp.float32)
    flow_top = section_flow(pixels[:half], jnp.concatenate([corner, successor_top]), offsets) * keep_mask
    flow_bottom = section_flow(prior_bottom, jnp.concatenate([pixels[half - RAD :], below]), offsets)
    flow_field = jnp.concatenate([flow_top, flow_bottom], axis=1)
    tiled = tiles_with_halo(flow_field, halo)
    node_half = flow_field.shape[1] // 2
    following = jnp.concatenate([tiled[:, 1:], jnp.zeros_like(tiled[:, :1])], axis=1)
    row_ids = jnp.arange(tiled.shape[2], dtype=jnp.int32)[:, None]
    from_prior = (row_ids < halo) | ((row_ids >= halo + node_half) & (row_ids < halo + 2 * node_half))
    flow_tiles = jnp.where(from_prior, following, tiled)
    tile_row = weights[0]
    tile_col = weights[1]
    tile_match = weights[2]
    weight_up = jnp.pad(tile_row, ((0, 0), (1, 0), (0, 0)))[:, :-1, :]
    weight_left = jnp.pad(tile_col, ((0, 0), (0, 0), (1, 0)))[:, :, :-1]
    match_prior = jnp.pad(tile_match, ((1, 0), (0, 0), (0, 0)))[:-1]
    diagonal = tile_row + weight_up + tile_col + weight_left + tile_match + match_prior
    positions = jnp.zeros_like(flow_tiles)
    for iteration in range(ITERS):
        padded = jnp.pad(positions, ((0, 0), (0, 0), (1, 1), (1, 1)))
        following = jnp.pad(positions, ((0, 0), (0, 1), (0, 0), (0, 0)))[:, 1:]
        pull_term = tile_match * (following - positions - flow_tiles)
        pull_prior = jnp.pad(pull_term, ((0, 0), (1, 0), (0, 0), (0, 0)))[:, :-1]
        positions = advance(
            positions,
            padded[:, :, 2:, 1:-1],
            padded[:, :, :-2, 1:-1],
            padded[:, :, 1:-1, 2:],
            padded[:, :, 1:-1, :-2],
            tile_row,
            weight_up,
            tile_col,
            weight_left,
            pull_term,
            pull_prior,
            diagonal,
        )
    core = positions[:, :, halo:-halo, halo:-halo]
    shape = core.shape
    flat = core.reshape(shape[0], shape[1], shape[2] * shape[3])
    returned = lax.all_to_all(flat, "sec", split_axis=1, concat_axis=1, tiled=True).reshape(shape)
    return jnp.transpose(returned, (0, 2, 1, 3)).reshape(shape[0], 1, shape[2], shape[1] * shape[3])


def solution(mesh):
    in_specs = (
        P("sec", "strip", None),
        P(),
        P(None, "sec", "strip", None),
        P("sec", "strip", None),
    )
    out_specs = P(None, "sec", "strip", None)
    return jax.shard_map(shards, mesh=mesh, in_specs=in_specs, out_specs=out_specs, check_vma=False)
```

```python
import jax
import jax.numpy as jnp
from jax import lax
from jax.experimental import pallas as pl
from jax.experimental.pallas import tpu as pltpu
from jax.sharding import PartitionSpec as P

RAD = 3
ITERS = 8


sharpness = 0.5
relax_rate = 0.8


def shifted_2(shard, axis, by):
    size = lax.axis_size(axis)
    pairs = [(i, i + by) for i in range(size) if 0 <= i + by < size]
    return lax.ppermute(shard, axis, pairs)


def extended(cells, sides, width):
    for axis, dim in sides:
        count = lax.axis_size(axis)
        ends = count - 1
        head = lax.slice_in_dim(cells, 0, width, axis=dim)
        tail = lax.slice_in_dim(cells, cells.shape[dim] - width, cells.shape[dim], axis=dim)
        cells = jnp.concatenate(
            [
                lax.ppermute(tail, axis, [(i, (i + 1) % count) for i in range(ends)]),
                cells,
                lax.ppermute(head, axis, [((i + 1) % count, i) for i in range(ends)]),
            ],
            axis=dim,
        )
    return cells


def lane_permutation():
    source = jnp.arange(512, dtype=jnp.int32)[:, None]
    target = jnp.arange(512, dtype=jnp.int32)[None, :]
    return ((source % 4) * 128 + source // 4 == target).astype(jnp.bfloat16)


def split_phases(pixels, permute, lanes_ref, phase_ref, node_rows):
    chunks = pixels.shape[1] // 512
    for c in range(chunks):
        permuted = jnp.dot(pixels[:, c * 512 : (c + 1) * 512], permute, preferred_element_type=jnp.float32)
        for t in range(4):
            lanes_ref[c * 4 + t, 0 : pixels.shape[0], :] = permuted[:, t * 128 : (t + 1) * 128]
    for q in range(4):
        for t in range(4):
            parts = [lanes_ref[pl.ds(c * 4 + t, 1), pl.ds(q, node_rows, stride=4), :][0] for c in range(chunks)]
            phase_ref[q * 4 + t] = jnp.concatenate(parts, axis=1)


def flow_kernel(
    offsets_ref, current_ref, following_ref, permute_ref, flow_ref, current_ph, following_ph, lanes_ref, shifted_ref, scores_ref
):
    tile_rows = current_ph.shape[1]
    node_cols = current_ph.shape[2]
    window = following_ph.shape[1]
    base = pl.multiple_of(pl.program_id(0) * tile_rows * 4, 32)
    permute = permute_ref[...]
    split_phases(current_ref[...], permute, lanes_ref, current_ph, tile_rows)
    split_phases(following_ref[pl.ds(base, window * 4), :], permute, lanes_ref, following_ph, window)
    column = lax.broadcasted_iota(jnp.int32, (window, node_cols), 1)

    def build(phase, carry):
        block = following_ph[phase]
        for col_shift in range(3):
            if col_shift == 1:
                moved = block
            else:
                moved = pltpu.roll(block, (1 - col_shift) % node_cols, 1)
                inside = (column + col_shift - 1 >= 0) & (column + col_shift - 1 < node_cols)
                moved = jnp.where(inside, moved, 0.0)
            for row_shift in range(3):
                rows = moved if row_shift == 0 else pltpu.roll(moved, window - row_shift, 0)
                shifted_ref[(row_shift * 3 + col_shift) * 16 + phase] = rows[:tile_rows]
        return carry

    lax.fori_loop(0, 16, build, 0)
    chunks = tile_rows // 8
    offset_count = scores_ref.shape[0]

    def score(k, carry):
        row_off = offsets_ref[k, 0]
        col_off = offsets_ref[k, 1]
        sources = []
        for q in range(4):
            u = q + row_off + 4
            u_node, u_phase = lax.shift_right_logical(u, 2), u & 3
            for t in range(4):
                v = t + col_off + 4
                v_node, v_phase = lax.shift_right_logical(v, 2), v & 3
                sources.append((u_node * 3 + v_node) * 16 + u_phase * 4 + v_phase)
        for c in range(chunks):
            rows = pl.ds(c * 8, 8)
            acc = current_ph[0, rows, :] * shifted_ref[sources[0], rows, :]
            for p in range(1, 16):
                acc = acc + current_ph[p, rows, :] * shifted_ref[sources[p], rows, :]
            scores_ref[k, rows, :] = sharpness * acc
        return carry

    lax.fori_loop(0, offset_count, score, 0)
    for c in range(chunks):
        rows = pl.ds(c * 8, 8)
        highest = scores_ref[0, rows, :]
        for k in range(1, offset_count):
            highest = jnp.maximum(highest, scores_ref[k, rows, :])
        weight_sum = jnp.zeros_like(highest)
        row_sum = jnp.zeros_like(highest)
        col_sum = jnp.zeros_like(highest)
        for k in range(offset_count):
            weight = jnp.exp(scores_ref[k, rows, :] - highest)
            weight_sum = weight_sum + weight
            row_sum = row_sum + weight * offsets_ref[k, 0].astype(jnp.float32)
            col_sum = col_sum + weight * offsets_ref[k, 1].astype(jnp.float32)
        flow_ref[0, rows, :] = row_sum / weight_sum
        flow_ref[1, rows, :] = col_sum / weight_sum


def section_flow(current, following, offsets, tile_rows=32):
    row_count, col_count = current.shape
    node_rows, node_cols = row_count // 4, col_count // 4
    window = tile_rows + 8
    padded = jnp.pad(following, ((4 - RAD, (node_rows + 8) * 4 - following.shape[0] - (4 - RAD)), (0, 0)))
    offset_count = offsets.shape[0]
    grid_spec = pltpu.PrefetchScalarGridSpec(
        num_scalar_prefetch=1,
        grid=(node_rows // tile_rows,),
        in_specs=[
            pl.BlockSpec((tile_rows * 4, col_count), lambda g, off: (g, 0)),
            pl.BlockSpec(padded.shape, lambda g, off: (0, 0)),
            pl.BlockSpec((512, 512), lambda g, off: (0, 0)),
        ],
        out_specs=pl.BlockSpec((2, tile_rows, node_cols), lambda g, off: (0, g, 0)),
        scratch_shapes=[
            pltpu.VMEM((16, tile_rows, node_cols), jnp.float32),
            pltpu.VMEM((16, window, node_cols), jnp.float32),
            pltpu.VMEM((col_count // 128, window * 4, 128), jnp.float32),
            pltpu.VMEM((144, tile_rows, node_cols), jnp.float32),
            pltpu.VMEM((offset_count, tile_rows, node_cols), jnp.float32),
        ],
    )
    return pl.pallas_call(
        flow_kernel,
        grid_spec=grid_spec,
        out_shape=jax.ShapeDtypeStruct((2, node_rows, node_cols), jnp.float32),
        compiler_params=pltpu.CompilerParams(
            dimension_semantics=("arbitrary",), vmem_limit_bytes=48 * 1024 * 1024
        ),
    )(offsets, current, padded, lane_permutation())


def advance(
    positions,
    from_below,
    from_above,
    from_right,
    from_left,
    row_weight,
    weight_up,
    col_weight,
    weight_left,
    pull_term,
    pull_prior,
    diagonal,
):
    force = row_weight * (from_below - positions) + weight_up * (from_above - positions)
    force = force + col_weight * (from_right - positions) + weight_left * (from_left - positions)
    force = force + pull_term - pull_prior
    return positions + relax_rate * force / (1.0 + diagonal)


def tiles_with_halo(fields, halo):
    count = lax.axis_size("sec")
    fields = extended(fields, (("strip", 1),), halo)
    width = fields.shape[2] // count
    columns = jnp.pad(fields, ((0, 0), (0, 0), (halo, halo)))
    windows = jnp.stack([columns[:, :, j * width : (j + 1) * width + 2 * halo] for j in range(count)], axis=1)
    shape = windows.shape
    flat = windows.reshape(shape[0], shape[1], shape[2] * shape[3])
    return lax.all_to_all(flat, "sec", split_axis=1, concat_axis=1, tiled=True).reshape(shape)


def shards(images, offsets, springs, validity):
    pixels = images[0]
    half = pixels.shape[0] // 2
    sec_count = lax.axis_size("sec")
    strip_count = lax.axis_size("strip")
    successor_top = shifted_2(pixels[: half + RAD], "sec", -1)
    prior_bottom = shifted_2(pixels[half:], "sec", 1)
    corner = lax.ppermute(
        pixels[-RAD:],
        ("sec", "strip"),
        [((s + 1) * strip_count + p - 1, s * strip_count + p) for s in range(sec_count - 1) for p in range(1, strip_count)],
    )
    below = shifted_2(pixels[:RAD], "strip", -1)
    keep_mask = (lax.axis_index("sec") < sec_count - 1).astype(jnp.float32)
    springs, validity, prior_bottom = lax.optimization_barrier((springs, validity, prior_bottom))
    match_weight = validity[0].astype(jnp.float32) * keep_mask
    node_rows, node_cols = (springs.shape[2], springs.shape[3])
    global_rows = lax.axis_index("strip") * node_rows + jnp.arange(node_rows, dtype=jnp.int32)
    row_keep = (global_rows < node_rows * lax.axis_size("strip") - 1).astype(jnp.float32)
    col_keep = (jnp.arange(node_cols) < node_cols - 1).astype(jnp.float32)
    row_weight = 0.25 * springs[0, 0].astype(jnp.float32) * row_keep[:, None]
    col_weight = 0.25 * springs[1, 0].astype(jnp.float32) * col_keep[None, :]
    halo = ITERS
    flow_top = section_flow(pixels[:half], jnp.concatenate([corner, successor_top]), offsets) * keep_mask
    flow_bottom = section_flow(prior_bottom, jnp.concatenate([pixels[half - RAD :], below]), offsets)
    flow_field = jnp.concatenate([flow_top, flow_bottom], axis=1)
    tiled = tiles_with_halo(jnp.concatenate([flow_field, jnp.stack([row_weight, col_weight, match_weight])]), halo)
    weights = tiled[2:]
    tiled = tiled[:2]
    node_half = flow_field.shape[1] // 2
    following = jnp.concatenate([tiled[:, 1:], jnp.zeros_like(tiled[:, :1])], axis=1)
    row_ids = jnp.arange(tiled.shape[2], dtype=jnp.int32)[:, None]
    from_prior = (row_ids < halo) | ((row_ids >= halo + node_half) & (row_ids < halo + 2 * node_half))
    flow_tiles = jnp.where(from_prior, following, tiled)
    tile_row = weights[0]
    tile_col = weights[1]
    tile_match = weights[2]
    weight_up = jnp.pad(tile_row, ((0, 0), (1, 0), (0, 0)))[:, :-1, :]
    weight_left = jnp.pad(tile_col, ((0, 0), (0, 0), (1, 0)))[:, :, :-1]
    match_prior = jnp.pad(tile_match, ((1, 0), (0, 0), (0, 0)))[:-1]
    diagonal = tile_row + weight_up + tile_col + weight_left + tile_match + match_prior
    positions = jnp.zeros_like(flow_tiles)
    for iteration in range(ITERS):
        padded = jnp.pad(positions, ((0, 0), (0, 0), (1, 1), (1, 1)))
        following = jnp.pad(positions, ((0, 0), (0, 1), (0, 0), (0, 0)))[:, 1:]
        pull_term = tile_match * (following - positions - flow_tiles)
        pull_prior = jnp.pad(pull_term, ((0, 0), (1, 0), (0, 0), (0, 0)))[:, :-1]
        positions = advance(
            positions,
            padded[:, :, 2:, 1:-1],
            padded[:, :, :-2, 1:-1],
            padded[:, :, 1:-1, 2:],
            padded[:, :, 1:-1, :-2],
            tile_row,
            weight_up,
            tile_col,
            weight_left,
            pull_term,
            pull_prior,
            diagonal,
        )
    core = positions[:, :, halo:-halo, halo:-halo]
    shape = core.shape
    flat = core.reshape(shape[0], shape[1], shape[2] * shape[3])
    returned = lax.all_to_all(flat, "sec", split_axis=1, concat_axis=1, tiled=True).reshape(shape)
    return jnp.transpose(returned, (0, 2, 1, 3)).reshape(shape[0], 1, shape[2], shape[1] * shape[3])


def solution(mesh):
    in_specs = (
        P("sec", "strip", None),
        P(),
        P(None, "sec", "strip", None),
        P("sec", "strip", None),
    )
    out_specs = P(None, "sec", "strip", None)
    return jax.shard_map(shards, mesh=mesh, in_specs=in_specs, out_specs=out_specs, check_vma=False)
```

```python
import jax
import jax.numpy as jnp
from jax import lax
from jax.experimental import pallas as pl
from jax.experimental.pallas import tpu as pltpu
from jax.sharding import PartitionSpec as P

RAD = 3
ITERS = 8


sharpness = 0.5
relax_rate = 0.8


def shifted_2(shard, axis, by):
    size = lax.axis_size(axis)
    pairs = [(i, i + by) for i in range(size) if 0 <= i + by < size]
    return lax.ppermute(shard, axis, pairs)


def extended(cells, sides, width):
    for axis, dim in sides:
        count = lax.axis_size(axis)
        ends = count - 1
        head = lax.slice_in_dim(cells, 0, width, axis=dim)
        tail = lax.slice_in_dim(cells, cells.shape[dim] - width, cells.shape[dim], axis=dim)
        cells = jnp.concatenate(
            [
                lax.ppermute(tail, axis, [(i, (i + 1) % count) for i in range(ends)]),
                cells,
                lax.ppermute(head, axis, [((i + 1) % count, i) for i in range(ends)]),
            ],
            axis=dim,
        )
    return cells


def lane_permutation():
    source = jnp.arange(512, dtype=jnp.int32)[:, None]
    target = jnp.arange(512, dtype=jnp.int32)[None, :]
    return ((source % 4) * 128 + source // 4 == target).astype(jnp.bfloat16)


def split_phases(pixels, permute, lanes_ref, phase_ref, node_rows):
    chunks = pixels.shape[1] // 512
    for c in range(chunks):
        permuted = jnp.dot(pixels[:, c * 512 : (c + 1) * 512], permute, preferred_element_type=jnp.float32)
        for t in range(4):
            lanes_ref[c * 4 + t, 0 : pixels.shape[0], :] = permuted[:, t * 128 : (t + 1) * 128]
    for q in range(4):
        for t in range(4):
            parts = [lanes_ref[pl.ds(c * 4 + t, 1), pl.ds(q, node_rows, stride=4), :][0] for c in range(chunks)]
            phase_ref[q * 4 + t] = jnp.concatenate(parts, axis=1)


def flow_kernel(
    offsets_ref, current_ref, following_ref, permute_ref, flow_ref, current_ph, following_ph, lanes_ref, shifted_ref, scores_ref
):
    tile_rows = current_ph.shape[1]
    node_cols = current_ph.shape[2]
    window = following_ph.shape[1]
    base = pl.multiple_of(pl.program_id(0) * tile_rows * 4, 32)
    permute = permute_ref[...]
    split_phases(current_ref[...], permute, lanes_ref, current_ph, tile_rows)
    split_phases(following_ref[pl.ds(base, window * 4), :], permute, lanes_ref, following_ph, window)
    column = lax.broadcasted_iota(jnp.int32, (window, node_cols), 1)

    def build(phase, carry):
        block = following_ph[phase]
        for col_shift in range(3):
            if col_shift == 1:
                moved = block
            else:
                moved = pltpu.roll(block, (1 - col_shift) % node_cols, 1)
                inside = (column + col_shift - 1 >= 0) & (column + col_shift - 1 < node_cols)
                moved = jnp.where(inside, moved, 0.0)
            for row_shift in range(3):
                rows = moved if row_shift == 0 else pltpu.roll(moved, window - row_shift, 0)
                shifted_ref[(row_shift * 3 + col_shift) * 16 + phase] = rows[:tile_rows]
        return carry

    lax.fori_loop(0, 16, build, 0)
    chunks = tile_rows // 8
    offset_count = scores_ref.shape[0]

    def score(k, carry):
        row_off = offsets_ref[k, 0]
        col_off = offsets_ref[k, 1]
        sources = []
        for q in range(4):
            u = q + row_off + 4
            u_node, u_phase = lax.shift_right_logical(u, 2), u & 3
            for t in range(4):
                v = t + col_off + 4
                v_node, v_phase = lax.shift_right_logical(v, 2), v & 3
                sources.append((u_node * 3 + v_node) * 16 + u_phase * 4 + v_phase)
        for c in range(chunks):
            rows = pl.ds(c * 8, 8)
            acc = current_ph[0, rows, :] * shifted_ref[sources[0], rows, :]
            for p in range(1, 16):
                acc = acc + current_ph[p, rows, :] * shifted_ref[sources[p], rows, :]
            scores_ref[k, rows, :] = sharpness * acc
        return carry

    lax.fori_loop(0, offset_count, score, 0)
    for c in range(chunks):
        rows = pl.ds(c * 8, 8)
        highest = scores_ref[0, rows, :]
        for k in range(1, offset_count):
            highest = jnp.maximum(highest, scores_ref[k, rows, :])
        weight_sum = jnp.zeros_like(highest)
        row_sum = jnp.zeros_like(highest)
        col_sum = jnp.zeros_like(highest)
        for k in range(offset_count):
            weight = jnp.exp(scores_ref[k, rows, :] - highest)
            weight_sum = weight_sum + weight
            row_sum = row_sum + weight * offsets_ref[k, 0].astype(jnp.float32)
            col_sum = col_sum + weight * offsets_ref[k, 1].astype(jnp.float32)
        flow_ref[0, rows, :] = row_sum / weight_sum
        flow_ref[1, rows, :] = col_sum / weight_sum


def section_flow(current, following, offsets, tile_rows=32):
    row_count, col_count = current.shape
    node_rows, node_cols = row_count // 4, col_count // 4
    window = tile_rows + 8
    padded = jnp.pad(following, ((4 - RAD, (node_rows + 8) * 4 - following.shape[0] - (4 - RAD)), (0, 0)))
    offset_count = offsets.shape[0]
    grid_spec = pltpu.PrefetchScalarGridSpec(
        num_scalar_prefetch=1,
        grid=(node_rows // tile_rows,),
        in_specs=[
            pl.BlockSpec((tile_rows * 4, col_count), lambda g, off: (g, 0)),
            pl.BlockSpec(padded.shape, lambda g, off: (0, 0)),
            pl.BlockSpec((512, 512), lambda g, off: (0, 0)),
        ],
        out_specs=pl.BlockSpec((2, tile_rows, node_cols), lambda g, off: (0, g, 0)),
        scratch_shapes=[
            pltpu.VMEM((16, tile_rows, node_cols), jnp.float32),
            pltpu.VMEM((16, window, node_cols), jnp.float32),
            pltpu.VMEM((col_count // 128, window * 4, 128), jnp.float32),
            pltpu.VMEM((144, tile_rows, node_cols), jnp.float32),
            pltpu.VMEM((offset_count, tile_rows, node_cols), jnp.float32),
        ],
    )
    return pl.pallas_call(
        flow_kernel,
        grid_spec=grid_spec,
        out_shape=jax.ShapeDtypeStruct((2, node_rows, node_cols), jnp.float32),
        compiler_params=pltpu.CompilerParams(
            dimension_semantics=("arbitrary",), vmem_limit_bytes=48 * 1024 * 1024
        ),
    )(offsets, current, padded, lane_permutation())


def advance(
    positions,
    from_below,
    from_above,
    from_right,
    from_left,
    row_weight,
    weight_up,
    col_weight,
    weight_left,
    pull_term,
    pull_prior,
    diagonal,
):
    force = row_weight * (from_below - positions) + weight_up * (from_above - positions)
    force = force + col_weight * (from_right - positions) + weight_left * (from_left - positions)
    force = force + pull_term - pull_prior
    return positions + relax_rate * force / (1.0 + diagonal)


def tiles_with_halo(fields, halo):
    count = lax.axis_size("sec")
    fields = extended(fields, (("strip", 1),), halo)
    width = fields.shape[2] // count
    columns = jnp.pad(fields, ((0, 0), (0, 0), (halo, halo)))
    windows = jnp.stack([columns[:, :, j * width : (j + 1) * width + 2 * halo] for j in range(count)], axis=1)
    shape = windows.shape
    flat = windows.reshape(shape[0], shape[1], shape[2] * shape[3])
    return lax.all_to_all(flat, "sec", split_axis=1, concat_axis=1, tiled=True).reshape(shape)


def shards(images, offsets, springs, validity):
    pixels = images[0]
    half = pixels.shape[0] // 2
    sec_count = lax.axis_size("sec")
    strip_count = lax.axis_size("strip")
    successor_top = shifted_2(pixels[: half + RAD], "sec", -1)
    prior_bottom = shifted_2(pixels[half:], "sec", 1)
    corner = lax.ppermute(
        pixels[-RAD:],
        ("sec", "strip"),
        [((s + 1) * strip_count + p - 1, s * strip_count + p) for s in range(sec_count - 1) for p in range(1, strip_count)],
    )
    below = shifted_2(pixels[:RAD], "strip", -1)
    keep_mask = (lax.axis_index("sec") < sec_count - 1).astype(jnp.float32)
    springs, validity, below = lax.optimization_barrier((springs, validity, below))
    match_weight = validity[0].astype(jnp.float32) * keep_mask
    node_rows, node_cols = (springs.shape[2], springs.shape[3])
    global_rows = lax.axis_index("strip") * node_rows + jnp.arange(node_rows, dtype=jnp.int32)
    row_keep = (global_rows < node_rows * lax.axis_size("strip") - 1).astype(jnp.float32)
    col_keep = (jnp.arange(node_cols) < node_cols - 1).astype(jnp.float32)
    row_weight = 0.25 * springs[0, 0].astype(jnp.float32) * row_keep[:, None]
    col_weight = 0.25 * springs[1, 0].astype(jnp.float32) * col_keep[None, :]
    halo = ITERS
    weights = jnp.stack([row_weight, col_weight, match_weight]).astype(jnp.bfloat16)
    weights = tiles_with_halo(weights, halo)
    weights, successor_top, prior_bottom = lax.optimization_barrier((weights, successor_top, prior_bottom))
    weights = weights.astype(jnp.float32)
    flow_top = section_flow(pixels[:half], jnp.concatenate([corner, successor_top]), offsets) * keep_mask
    flow_bottom = section_flow(prior_bottom, jnp.concatenate([pixels[half - RAD :], below]), offsets)
    flow_field = jnp.concatenate([flow_top, flow_bottom], axis=1)
    tiled = tiles_with_halo(flow_field, halo)
    node_half = flow_field.shape[1] // 2
    following = jnp.concatenate([tiled[:, 1:], jnp.zeros_like(tiled[:, :1])], axis=1)
    row_ids = jnp.arange(tiled.shape[2], dtype=jnp.int32)[:, None]
    from_prior = (row_ids < halo) | ((row_ids >= halo + node_half) & (row_ids < halo + 2 * node_half))
    flow_tiles = jnp.where(from_prior, following, tiled)
    tile_row = weights[0]
    tile_col = weights[1]
    tile_match = weights[2]
    weight_up = jnp.pad(tile_row, ((0, 0), (1, 0), (0, 0)))[:, :-1, :]
    weight_left = jnp.pad(tile_col, ((0, 0), (0, 0), (1, 0)))[:, :, :-1]
    match_prior = jnp.pad(tile_match, ((1, 0), (0, 0), (0, 0)))[:-1]
    diagonal = tile_row + weight_up + tile_col + weight_left + tile_match + match_prior
    positions = jnp.zeros_like(flow_tiles)
    for iteration in range(ITERS):
        padded = jnp.pad(positions, ((0, 0), (0, 0), (1, 1), (1, 1)))
        following = jnp.pad(positions, ((0, 0), (0, 1), (0, 0), (0, 0)))[:, 1:]
        pull_term = tile_match * (following - positions - flow_tiles)
        pull_prior = jnp.pad(pull_term, ((0, 0), (1, 0), (0, 0), (0, 0)))[:, :-1]
        positions = advance(
            positions,
            padded[:, :, 2:, 1:-1],
            padded[:, :, :-2, 1:-1],
            padded[:, :, 1:-1, 2:],
            padded[:, :, 1:-1, :-2],
            tile_row,
            weight_up,
            tile_col,
            weight_left,
            pull_term,
            pull_prior,
            diagonal,
        )
    core = positions[:, :, halo:-halo, halo:-halo]
    shape = core.shape
    flat = core.reshape(shape[0], shape[1], shape[2] * shape[3])
    returned = lax.all_to_all(flat, "sec", split_axis=1, concat_axis=1, tiled=True).reshape(shape)
    return jnp.transpose(returned, (0, 2, 1, 3)).reshape(shape[0], 1, shape[2], shape[1] * shape[3])


def solution(mesh):
    in_specs = (
        P("sec", "strip", None),
        P(),
        P(None, "sec", "strip", None),
        P("sec", "strip", None),
    )
    out_specs = P(None, "sec", "strip", None)
    return jax.shard_map(shards, mesh=mesh, in_specs=in_specs, out_specs=out_specs, check_vma=False)
```

```python
import jax
import jax.numpy as jnp
from jax import lax
from jax.experimental import pallas as pl
from jax.experimental.pallas import tpu as pltpu
from jax.sharding import PartitionSpec as P

RAD = 3
ITERS = 8


sharpness = 0.5
relax_rate = 0.8


def shifted_2(shard, axis, by):
    size = lax.axis_size(axis)
    pairs = [(i, i + by) for i in range(size) if 0 <= i + by < size]
    return lax.ppermute(shard, axis, pairs)


def extended(cells, sides, width):
    for axis, dim in sides:
        count = lax.axis_size(axis)
        ends = count - 1
        head = lax.slice_in_dim(cells, 0, width, axis=dim)
        tail = lax.slice_in_dim(cells, cells.shape[dim] - width, cells.shape[dim], axis=dim)
        cells = jnp.concatenate(
            [
                lax.ppermute(tail, axis, [(i, (i + 1) % count) for i in range(ends)]),
                cells,
                lax.ppermute(head, axis, [((i + 1) % count, i) for i in range(ends)]),
            ],
            axis=dim,
        )
    return cells


def lane_permutation():
    source = jnp.arange(512, dtype=jnp.int32)[:, None]
    target = jnp.arange(512, dtype=jnp.int32)[None, :]
    return ((source % 4) * 128 + source // 4 == target).astype(jnp.bfloat16)


def split_phases(pixels, permute, lanes_ref, phase_ref, node_rows):
    chunks = pixels.shape[1] // 512
    for c in range(chunks):
        permuted = jnp.dot(pixels[:, c * 512 : (c + 1) * 512], permute, preferred_element_type=jnp.float32)
        for t in range(4):
            lanes_ref[c * 4 + t, 0 : pixels.shape[0], :] = permuted[:, t * 128 : (t + 1) * 128]
    for q in range(4):
        for t in range(4):
            parts = [lanes_ref[pl.ds(c * 4 + t, 1), pl.ds(q, node_rows, stride=4), :][0] for c in range(chunks)]
            phase_ref[q * 4 + t] = jnp.concatenate(parts, axis=1)


def flow_kernel(
    offsets_ref, current_ref, following_ref, permute_ref, flow_ref, current_ph, following_ph, lanes_ref, shifted_ref, scores_ref, sources_ref
):
    tile_rows = current_ph.shape[1]
    node_cols = current_ph.shape[2]
    window = following_ph.shape[1]
    base = pl.multiple_of(pl.program_id(0) * tile_rows * 4, 32)
    permute = permute_ref[...]
    split_phases(current_ref[...], permute, lanes_ref, current_ph, tile_rows)
    split_phases(following_ref[pl.ds(base, window * 4), :], permute, lanes_ref, following_ph, window)
    column = lax.broadcasted_iota(jnp.int32, (window, node_cols), 1)

    def build(phase, carry):
        block = following_ph[phase]
        for col_shift in range(3):
            if col_shift == 1:
                moved = block
            else:
                moved = pltpu.roll(block, (1 - col_shift) % node_cols, 1)
                inside = (column + col_shift - 1 >= 0) & (column + col_shift - 1 < node_cols)
                moved = jnp.where(inside, moved, 0.0)
            for row_shift in range(3):
                rows = moved if row_shift == 0 else pltpu.roll(moved, window - row_shift, 0)
                shifted_ref[(row_shift * 3 + col_shift) * 16 + phase] = rows[:tile_rows]
        return carry

    lax.fori_loop(0, 16, build, 0)
    chunks = tile_rows // 8
    offset_count = scores_ref.shape[0]

    def fill(k, carry):
        row_off = offsets_ref[k, 0]
        col_off = offsets_ref[k, 1]
        for q in range(4):
            u = q + row_off + 4
            u_node, u_phase = lax.shift_right_logical(u, 2), u & 3
            for t in range(4):
                v = t + col_off + 4
                v_node, v_phase = lax.shift_right_logical(v, 2), v & 3
                sources_ref[k * 16 + q * 4 + t] = (u_node * 3 + v_node) * 16 + u_phase * 4 + v_phase
        return carry

    lax.fori_loop(0, offset_count, fill, 0)
    for c in range(chunks):
        for h in range(node_cols // 256):
            rows = pl.ds(c * 8, 8)
            lanes = pl.ds(h * 256, 256)
            current = [current_ph[p, rows, lanes] for p in range(16)]

            def score(k, carry):
                acc = current[0] * shifted_ref[sources_ref[k * 16], rows, lanes]
                for p in range(1, 16):
                    acc = acc + current[p] * shifted_ref[sources_ref[k * 16 + p], rows, lanes]
                scores_ref[k, rows, lanes] = sharpness * acc
                return carry

            lax.fori_loop(0, offset_count, score, 0)
    for c in range(chunks):
        rows = pl.ds(c * 8, 8)
        highest = scores_ref[0, rows, :]
        for k in range(1, offset_count):
            highest = jnp.maximum(highest, scores_ref[k, rows, :])
        weight_sum = jnp.zeros_like(highest)
        row_sum = jnp.zeros_like(highest)
        col_sum = jnp.zeros_like(highest)
        for k in range(offset_count):
            weight = jnp.exp(scores_ref[k, rows, :] - highest)
            weight_sum = weight_sum + weight
            row_sum = row_sum + weight * offsets_ref[k, 0].astype(jnp.float32)
            col_sum = col_sum + weight * offsets_ref[k, 1].astype(jnp.float32)
        flow_ref[0, rows, :] = row_sum / weight_sum
        flow_ref[1, rows, :] = col_sum / weight_sum


def section_flow(current, following, offsets, tile_rows=32):
    row_count, col_count = current.shape
    node_rows, node_cols = row_count // 4, col_count // 4
    window = tile_rows + 8
    padded = jnp.pad(following, ((4 - RAD, (node_rows + 8) * 4 - following.shape[0] - (4 - RAD)), (0, 0)))
    offset_count = offsets.shape[0]
    grid_spec = pltpu.PrefetchScalarGridSpec(
        num_scalar_prefetch=1,
        grid=(node_rows // tile_rows,),
        in_specs=[
            pl.BlockSpec((tile_rows * 4, col_count), lambda g, off: (g, 0)),
            pl.BlockSpec(padded.shape, lambda g, off: (0, 0)),
            pl.BlockSpec((512, 512), lambda g, off: (0, 0)),
        ],
        out_specs=pl.BlockSpec((2, tile_rows, node_cols), lambda g, off: (0, g, 0)),
        scratch_shapes=[
            pltpu.VMEM((16, tile_rows, node_cols), jnp.float32),
            pltpu.VMEM((16, window, node_cols), jnp.float32),
            pltpu.VMEM((col_count // 128, window * 4, 128), jnp.float32),
            pltpu.VMEM((144, tile_rows, node_cols), jnp.float32),
            pltpu.VMEM((offset_count, tile_rows, node_cols), jnp.float32),
            pltpu.SMEM((offset_count * 16,), jnp.int32),
        ],
    )
    return pl.pallas_call(
        flow_kernel,
        grid_spec=grid_spec,
        out_shape=jax.ShapeDtypeStruct((2, node_rows, node_cols), jnp.float32),
        compiler_params=pltpu.CompilerParams(
            dimension_semantics=("arbitrary",), vmem_limit_bytes=48 * 1024 * 1024
        ),
    )(offsets, current, padded, lane_permutation())


def advance(
    positions,
    from_below,
    from_above,
    from_right,
    from_left,
    row_weight,
    weight_up,
    col_weight,
    weight_left,
    pull_term,
    pull_prior,
    diagonal,
):
    force = row_weight * (from_below - positions) + weight_up * (from_above - positions)
    force = force + col_weight * (from_right - positions) + weight_left * (from_left - positions)
    force = force + pull_term - pull_prior
    return positions + relax_rate * force / (1.0 + diagonal)


def tiles_with_halo(fields, halo):
    count = lax.axis_size("sec")
    fields = extended(fields, (("strip", 1),), halo)
    width = fields.shape[2] // count
    columns = jnp.pad(fields, ((0, 0), (0, 0), (halo, halo)))
    windows = jnp.stack([columns[:, :, j * width : (j + 1) * width + 2 * halo] for j in range(count)], axis=1)
    shape = windows.shape
    flat = windows.reshape(shape[0], shape[1], shape[2] * shape[3])
    return lax.all_to_all(flat, "sec", split_axis=1, concat_axis=1, tiled=True).reshape(shape)


def shards(images, offsets, springs, validity):
    pixels = images[0]
    half = pixels.shape[0] // 2
    sec_count = lax.axis_size("sec")
    strip_count = lax.axis_size("strip")
    successor_top = shifted_2(pixels[: half + RAD], "sec", -1)
    prior_bottom = shifted_2(pixels[half:], "sec", 1)
    corner = lax.ppermute(
        pixels[-RAD:],
        ("sec", "strip"),
        [((s + 1) * strip_count + p - 1, s * strip_count + p) for s in range(sec_count - 1) for p in range(1, strip_count)],
    )
    below = shifted_2(pixels[:RAD], "strip", -1)
    keep_mask = (lax.axis_index("sec") < sec_count - 1).astype(jnp.float32)
    springs, validity, below = lax.optimization_barrier((springs, validity, below))
    match_weight = validity[0].astype(jnp.float32) * keep_mask
    node_rows, node_cols = (springs.shape[2], springs.shape[3])
    global_rows = lax.axis_index("strip") * node_rows + jnp.arange(node_rows, dtype=jnp.int32)
    row_keep = (global_rows < node_rows * lax.axis_size("strip") - 1).astype(jnp.float32)
    col_keep = (jnp.arange(node_cols) < node_cols - 1).astype(jnp.float32)
    row_weight = 0.25 * springs[0, 0].astype(jnp.float32) * row_keep[:, None]
    col_weight = 0.25 * springs[1, 0].astype(jnp.float32) * col_keep[None, :]
    halo = ITERS
    weights = jnp.stack([row_weight, col_weight, match_weight]).astype(jnp.bfloat16)
    weights = tiles_with_halo(weights, halo)
    weights, successor_top, prior_bottom = lax.optimization_barrier((weights, successor_top, prior_bottom))
    weights = weights.astype(jnp.float32)
    flow_top = section_flow(pixels[:half], jnp.concatenate([corner, successor_top]), offsets) * keep_mask
    flow_bottom = section_flow(prior_bottom, jnp.concatenate([pixels[half - RAD :], below]), offsets)
    flow_field = jnp.concatenate([flow_top, flow_bottom], axis=1)
    tiled = tiles_with_halo(flow_field, halo)
    node_half = flow_field.shape[1] // 2
    following = jnp.concatenate([tiled[:, 1:], jnp.zeros_like(tiled[:, :1])], axis=1)
    row_ids = jnp.arange(tiled.shape[2], dtype=jnp.int32)[:, None]
    from_prior = (row_ids < halo) | ((row_ids >= halo + node_half) & (row_ids < halo + 2 * node_half))
    flow_tiles = jnp.where(from_prior, following, tiled)
    tile_row = weights[0]
    tile_col = weights[1]
    tile_match = weights[2]
    weight_up = jnp.pad(tile_row, ((0, 0), (1, 0), (0, 0)))[:, :-1, :]
    weight_left = jnp.pad(tile_col, ((0, 0), (0, 0), (1, 0)))[:, :, :-1]
    match_prior = jnp.pad(tile_match, ((1, 0), (0, 0), (0, 0)))[:-1]
    diagonal = tile_row + weight_up + tile_col + weight_left + tile_match + match_prior
    positions = jnp.zeros_like(flow_tiles)
    for iteration in range(ITERS):
        padded = jnp.pad(positions, ((0, 0), (0, 0), (1, 1), (1, 1)))
        following = jnp.pad(positions, ((0, 0), (0, 1), (0, 0), (0, 0)))[:, 1:]
        pull_term = tile_match * (following - positions - flow_tiles)
        pull_prior = jnp.pad(pull_term, ((0, 0), (1, 0), (0, 0), (0, 0)))[:, :-1]
        positions = advance(
            positions,
            padded[:, :, 2:, 1:-1],
            padded[:, :, :-2, 1:-1],
            padded[:, :, 1:-1, 2:],
            padded[:, :, 1:-1, :-2],
            tile_row,
            weight_up,
            tile_col,
            weight_left,
            pull_term,
            pull_prior,
            diagonal,
        )
    core = positions[:, :, halo:-halo, halo:-halo]
    shape = core.shape
    flat = core.reshape(shape[0], shape[1], shape[2] * shape[3])
    returned = lax.all_to_all(flat, "sec", split_axis=1, concat_axis=1, tiled=True).reshape(shape)
    return jnp.transpose(returned, (0, 2, 1, 3)).reshape(shape[0], 1, shape[2], shape[1] * shape[3])


def solution(mesh):
    in_specs = (
        P("sec", "strip", None),
        P(),
        P(None, "sec", "strip", None),
        P("sec", "strip", None),
    )
    out_specs = P(None, "sec", "strip", None)
    return jax.shard_map(shards, mesh=mesh, in_specs=in_specs, out_specs=out_specs, check_vma=False)
```

```python
import jax
import jax.numpy as jnp
from jax import lax
from jax.experimental import pallas as pl
from jax.experimental.pallas import tpu as pltpu
from jax.sharding import PartitionSpec as P

RAD = 3
ITERS = 8


sharpness = 0.5
relax_rate = 0.8


def shifted_2(shard, axis, by):
    size = lax.axis_size(axis)
    pairs = [(i, i + by) for i in range(size) if 0 <= i + by < size]
    return lax.ppermute(shard, axis, pairs)


def extended(cells, sides, width):
    for axis, dim in sides:
        count = lax.axis_size(axis)
        ends = count - 1
        head = lax.slice_in_dim(cells, 0, width, axis=dim)
        tail = lax.slice_in_dim(cells, cells.shape[dim] - width, cells.shape[dim], axis=dim)
        cells = jnp.concatenate(
            [
                lax.ppermute(tail, axis, [(i, (i + 1) % count) for i in range(ends)]),
                cells,
                lax.ppermute(head, axis, [((i + 1) % count, i) for i in range(ends)]),
            ],
            axis=dim,
        )
    return cells


def lane_permutation():
    source = jnp.arange(512, dtype=jnp.int32)[:, None]
    target = jnp.arange(512, dtype=jnp.int32)[None, :]
    return ((source % 4) * 128 + source // 4 == target).astype(jnp.bfloat16)


def split_phases(pixels, permute, lanes_ref, phase_ref, node_rows):
    chunks = pixels.shape[1] // 512
    for c in range(chunks):
        permuted = jnp.dot(pixels[:, c * 512 : (c + 1) * 512], permute, preferred_element_type=jnp.float32)
        for t in range(4):
            lanes_ref[c * 4 + t, 0 : pixels.shape[0], :] = permuted[:, t * 128 : (t + 1) * 128]
    for q in range(4):
        for t in range(4):
            parts = [lanes_ref[pl.ds(c * 4 + t, 1), pl.ds(q, node_rows, stride=4), :][0] for c in range(chunks)]
            phase_ref[q * 4 + t] = jnp.concatenate(parts, axis=1)


def flow_kernel(
    offsets_ref, current_ref, following_ref, permute_ref, flow_ref, current_ph, following_ph, lanes_ref, shifted_ref, scores_ref
):
    tile_rows = current_ph.shape[1]
    node_cols = current_ph.shape[2]
    window = following_ph.shape[1]
    base = pl.multiple_of(pl.program_id(0) * tile_rows * 4, 32)
    permute = permute_ref[...]
    split_phases(current_ref[...], permute, lanes_ref, current_ph, tile_rows)
    split_phases(following_ref[pl.ds(base, window * 4), :], permute, lanes_ref, following_ph, window)
    column = lax.broadcasted_iota(jnp.int32, (window, node_cols), 1)

    def build(phase, carry):
        block = following_ph[phase]
        for col_shift in range(3):
            if col_shift == 1:
                moved = block
            else:
                moved = pltpu.roll(block, (1 - col_shift) % node_cols, 1)
                inside = (column + col_shift - 1 >= 0) & (column + col_shift - 1 < node_cols)
                moved = jnp.where(inside, moved, 0.0)
            for row_shift in range(3):
                rows = moved if row_shift == 0 else pltpu.roll(moved, window - row_shift, 0)
                shifted_ref[(row_shift * 3 + col_shift) * 16 + phase] = rows[:tile_rows]
        return carry

    lax.fori_loop(0, 16, build, 0)
    chunks = tile_rows // 8
    offset_count = scores_ref.shape[0]

    def score(k, carry):
        row_off = offsets_ref[k, 0]
        col_off = offsets_ref[k, 1]
        sources = []
        for q in range(4):
            u = q + row_off + 4
            u_node, u_phase = lax.shift_right_logical(u, 2), u & 3
            for t in range(4):
                v = t + col_off + 4
                v_node, v_phase = lax.shift_right_logical(v, 2), v & 3
                sources.append((u_node * 3 + v_node) * 16 + u_phase * 4 + v_phase)
        for c in range(chunks):
            rows = pl.ds(c * 8, 8)
            acc = current_ph[0, rows, :] * shifted_ref[sources[0], rows, :]
            for p in range(1, 16):
                acc = acc + current_ph[p, rows, :] * shifted_ref[sources[p], rows, :]
            scores_ref[k, rows, :] = sharpness * acc
        return carry

    lax.fori_loop(0, offset_count, score, 0)
    for c in range(chunks):
        rows = pl.ds(c * 8, 8)
        highest = scores_ref[0, rows, :]
        for k in range(1, offset_count):
            highest = jnp.maximum(highest, scores_ref[k, rows, :])
        weight_sum = jnp.zeros_like(highest)
        row_sum = jnp.zeros_like(highest)
        col_sum = jnp.zeros_like(highest)
        for k in range(offset_count):
            weight = jnp.exp(scores_ref[k, rows, :] - highest)
            weight_sum = weight_sum + weight
            row_sum = row_sum + weight * offsets_ref[k, 0].astype(jnp.float32)
            col_sum = col_sum + weight * offsets_ref[k, 1].astype(jnp.float32)
        flow_ref[0, rows, :] = row_sum / weight_sum
        flow_ref[1, rows, :] = col_sum / weight_sum


def section_flow(current, following, offsets, tile_rows=32):
    row_count, col_count = current.shape
    node_rows, node_cols = row_count // 4, col_count // 4
    window = tile_rows + 8
    padded = jnp.pad(following, ((4 - RAD, (node_rows + 8) * 4 - following.shape[0] - (4 - RAD)), (0, 0)))
    offset_count = offsets.shape[0]
    grid_spec = pltpu.PrefetchScalarGridSpec(
        num_scalar_prefetch=1,
        grid=(node_rows // tile_rows,),
        in_specs=[
            pl.BlockSpec((tile_rows * 4, col_count), lambda g, off: (g, 0)),
            pl.BlockSpec(padded.shape, lambda g, off: (0, 0)),
            pl.BlockSpec((512, 512), lambda g, off: (0, 0)),
        ],
        out_specs=pl.BlockSpec((2, tile_rows, node_cols), lambda g, off: (0, g, 0)),
        scratch_shapes=[
            pltpu.VMEM((16, tile_rows, node_cols), jnp.float32),
            pltpu.VMEM((16, window, node_cols), jnp.float32),
            pltpu.VMEM((col_count // 128, window * 4, 128), jnp.float32),
            pltpu.VMEM((144, tile_rows, node_cols), jnp.float32),
            pltpu.VMEM((offset_count, tile_rows, node_cols), jnp.float32),
        ],
    )
    return pl.pallas_call(
        flow_kernel,
        grid_spec=grid_spec,
        out_shape=jax.ShapeDtypeStruct((2, node_rows, node_cols), jnp.float32),
        compiler_params=pltpu.CompilerParams(
            dimension_semantics=("arbitrary",), vmem_limit_bytes=48 * 1024 * 1024
        ),
    )(offsets, current, padded, lane_permutation())


def advance(
    positions,
    from_below,
    from_above,
    from_right,
    from_left,
    row_weight,
    weight_up,
    col_weight,
    weight_left,
    pull_term,
    pull_prior,
    diagonal,
):
    force = row_weight * (from_below - positions) + weight_up * (from_above - positions)
    force = force + col_weight * (from_right - positions) + weight_left * (from_left - positions)
    force = force + pull_term - pull_prior
    return positions + relax_rate * force / (1.0 + diagonal)


def tiles_with_halo(fields, halo):
    count = lax.axis_size("sec")
    fields = extended(fields, (("strip", 1),), halo)
    width = fields.shape[2] // count
    columns = jnp.pad(fields, ((0, 0), (0, 0), (halo, halo)))
    windows = jnp.stack([columns[:, :, j * width : (j + 1) * width + 2 * halo] for j in range(count)], axis=1)
    shape = windows.shape
    flat = windows.reshape(shape[0], shape[1], shape[2] * shape[3])
    return lax.all_to_all(flat, "sec", split_axis=1, concat_axis=1, tiled=True).reshape(shape)


def shards(images, offsets, springs, validity):
    pixels = images[0]
    half = pixels.shape[0] // 2
    sec_count = lax.axis_size("sec")
    strip_count = lax.axis_size("strip")
    aligned = -(-RAD // 16) * 16
    successor_top = shifted_2(pixels[: half + aligned], "sec", -1)[: half + RAD]
    prior_bottom = shifted_2(pixels[half:], "sec", 1)
    corner = lax.ppermute(
        pixels[-aligned:],
        ("sec", "strip"),
        [((s + 1) * strip_count + p - 1, s * strip_count + p) for s in range(sec_count - 1) for p in range(1, strip_count)],
    )[-RAD:]
    below = shifted_2(pixels[:aligned], "strip", -1)[:RAD]
    keep_mask = (lax.axis_index("sec") < sec_count - 1).astype(jnp.float32)
    springs, validity, below = lax.optimization_barrier((springs, validity, below))
    match_weight = validity[0].astype(jnp.float32) * keep_mask
    node_rows, node_cols = (springs.shape[2], springs.shape[3])
    global_rows = lax.axis_index("strip") * node_rows + jnp.arange(node_rows, dtype=jnp.int32)
    row_keep = (global_rows < node_rows * lax.axis_size("strip") - 1).astype(jnp.float32)
    col_keep = (jnp.arange(node_cols) < node_cols - 1).astype(jnp.float32)
    row_weight = 0.25 * springs[0, 0].astype(jnp.float32) * row_keep[:, None]
    col_weight = 0.25 * springs[1, 0].astype(jnp.float32) * col_keep[None, :]
    halo = ITERS
    weights = jnp.stack([row_weight, col_weight, match_weight]).astype(jnp.bfloat16)
    weights = tiles_with_halo(weights, halo)
    weights, successor_top, prior_bottom = lax.optimization_barrier((weights, successor_top, prior_bottom))
    weights = weights.astype(jnp.float32)
    flow_top = section_flow(pixels[:half], jnp.concatenate([corner, successor_top]), offsets) * keep_mask
    flow_bottom = section_flow(prior_bottom, jnp.concatenate([pixels[half - RAD :], below]), offsets)
    flow_field = jnp.concatenate([flow_top, flow_bottom], axis=1)
    tiled = tiles_with_halo(flow_field, halo)
    node_half = flow_field.shape[1] // 2
    following = jnp.concatenate([tiled[:, 1:], jnp.zeros_like(tiled[:, :1])], axis=1)
    row_ids = jnp.arange(tiled.shape[2], dtype=jnp.int32)[:, None]
    from_prior = (row_ids < halo) | ((row_ids >= halo + node_half) & (row_ids < halo + 2 * node_half))
    flow_tiles = jnp.where(from_prior, following, tiled)
    tile_row = weights[0]
    tile_col = weights[1]
    tile_match = weights[2]
    weight_up = jnp.pad(tile_row, ((0, 0), (1, 0), (0, 0)))[:, :-1, :]
    weight_left = jnp.pad(tile_col, ((0, 0), (0, 0), (1, 0)))[:, :, :-1]
    match_prior = jnp.pad(tile_match, ((1, 0), (0, 0), (0, 0)))[:-1]
    diagonal = tile_row + weight_up + tile_col + weight_left + tile_match + match_prior
    positions = jnp.zeros_like(flow_tiles)
    for iteration in range(ITERS):
        padded = jnp.pad(positions, ((0, 0), (0, 0), (1, 1), (1, 1)))
        following = jnp.pad(positions, ((0, 0), (0, 1), (0, 0), (0, 0)))[:, 1:]
        pull_term = tile_match * (following - positions - flow_tiles)
        pull_prior = jnp.pad(pull_term, ((0, 0), (1, 0), (0, 0), (0, 0)))[:, :-1]
        positions = advance(
            positions,
            padded[:, :, 2:, 1:-1],
            padded[:, :, :-2, 1:-1],
            padded[:, :, 1:-1, 2:],
            padded[:, :, 1:-1, :-2],
            tile_row,
            weight_up,
            tile_col,
            weight_left,
            pull_term,
            pull_prior,
            diagonal,
        )
    core = positions[:, :, halo:-halo, halo:-halo]
    shape = core.shape
    flat = core.reshape(shape[0], shape[1], shape[2] * shape[3])
    returned = lax.all_to_all(flat, "sec", split_axis=1, concat_axis=1, tiled=True).reshape(shape)
    return jnp.transpose(returned, (0, 2, 1, 3)).reshape(shape[0], 1, shape[2], shape[1] * shape[3])


def solution(mesh):
    in_specs = (
        P("sec", "strip", None),
        P(),
        P(None, "sec", "strip", None),
        P("sec", "strip", None),
    )
    out_specs = P(None, "sec", "strip", None)
    return jax.shard_map(shards, mesh=mesh, in_specs=in_specs, out_specs=out_specs, check_vma=False)
```

```python
import jax
import jax.numpy as jnp
from jax import lax
from jax.experimental import pallas as pl
from jax.experimental.pallas import tpu as pltpu
from jax.sharding import PartitionSpec as P

RAD = 3
ITERS = 8


sharpness = 0.5
relax_rate = 0.8


def shifted_2(shard, axis, by):
    size = lax.axis_size(axis)
    pairs = [(i, i + by) for i in range(size) if 0 <= i + by < size]
    return lax.ppermute(shard, axis, pairs)


def extended(cells, sides, width):
    for axis, dim in sides:
        count = lax.axis_size(axis)
        ends = count - 1
        head = lax.slice_in_dim(cells, 0, width, axis=dim)
        tail = lax.slice_in_dim(cells, cells.shape[dim] - width, cells.shape[dim], axis=dim)
        cells = jnp.concatenate(
            [
                lax.ppermute(tail, axis, [(i, (i + 1) % count) for i in range(ends)]),
                cells,
                lax.ppermute(head, axis, [((i + 1) % count, i) for i in range(ends)]),
            ],
            axis=dim,
        )
    return cells


def lane_permutation():
    source = jnp.arange(512, dtype=jnp.int32)[:, None]
    target = jnp.arange(512, dtype=jnp.int32)[None, :]
    return ((source % 4) * 128 + source // 4 == target).astype(jnp.bfloat16)


def split_phases(pixels, permute, lanes_ref, phase_ref, node_rows):
    chunks = pixels.shape[1] // 512
    for c in range(chunks):
        permuted = jnp.dot(pixels[:, c * 512 : (c + 1) * 512], permute, preferred_element_type=jnp.float32)
        for t in range(4):
            lanes_ref[c * 4 + t, 0 : pixels.shape[0], :] = permuted[:, t * 128 : (t + 1) * 128]
    for q in range(4):
        for t in range(4):
            parts = [lanes_ref[pl.ds(c * 4 + t, 1), pl.ds(q, node_rows, stride=4), :][0] for c in range(chunks)]
            phase_ref[q * 4 + t] = jnp.concatenate(parts, axis=1)


def flow_kernel(
    offsets_ref, current_ref, following_ref, permute_ref, flow_ref, current_ph, following_ph, lanes_ref, shifted_ref, scores_ref
):
    tile_rows = current_ph.shape[1]
    node_cols = current_ph.shape[2]
    window = following_ph.shape[1]
    base = pl.multiple_of(pl.program_id(0) * tile_rows * 4, 32)
    permute = permute_ref[...]
    split_phases(current_ref[...], permute, lanes_ref, current_ph, tile_rows)
    split_phases(following_ref[pl.ds(base, window * 4), :], permute, lanes_ref, following_ph, window)
    column = lax.broadcasted_iota(jnp.int32, (window, node_cols), 1)

    def build(phase, carry):
        block = following_ph[phase]
        for col_shift in range(3):
            if col_shift == 1:
                moved = block
            else:
                moved = pltpu.roll(block, (1 - col_shift) % node_cols, 1)
                inside = (column + col_shift - 1 >= 0) & (column + col_shift - 1 < node_cols)
                moved = jnp.where(inside, moved, 0.0)
            for row_shift in range(3):
                rows = moved if row_shift == 0 else pltpu.roll(moved, window - row_shift, 0)
                shifted_ref[(row_shift * 3 + col_shift) * 16 + phase] = rows[:tile_rows]
        return carry

    lax.fori_loop(0, 16, build, 0)
    chunks = tile_rows // 8
    offset_count = scores_ref.shape[0]

    def score(k, carry):
        row_off = offsets_ref[k, 0]
        col_off = offsets_ref[k, 1]
        sources = []
        for q in range(4):
            u = q + row_off + 4
            u_node, u_phase = lax.shift_right_logical(u, 2), u & 3
            for t in range(4):
                v = t + col_off + 4
                v_node, v_phase = lax.shift_right_logical(v, 2), v & 3
                sources.append((u_node * 3 + v_node) * 16 + u_phase * 4 + v_phase)
        for c in range(chunks):
            rows = pl.ds(c * 8, 8)
            acc = current_ph[0, rows, :] * shifted_ref[sources[0], rows, :]
            for p in range(1, 16):
                acc = acc + current_ph[p, rows, :] * shifted_ref[sources[p], rows, :]
            scores_ref[k, rows, :] = sharpness * acc
        return carry

    lax.fori_loop(0, offset_count, score, 0)
    for c in range(chunks):
        rows = pl.ds(c * 8, 8)
        highest = scores_ref[0, rows, :]
        for k in range(1, offset_count):
            highest = jnp.maximum(highest, scores_ref[k, rows, :])
        weight_sum = jnp.zeros_like(highest)
        row_sum = jnp.zeros_like(highest)
        col_sum = jnp.zeros_like(highest)
        for k in range(offset_count):
            weight = jnp.exp(scores_ref[k, rows, :] - highest)
            weight_sum = weight_sum + weight
            row_sum = row_sum + weight * offsets_ref[k, 0].astype(jnp.float32)
            col_sum = col_sum + weight * offsets_ref[k, 1].astype(jnp.float32)
        flow_ref[0, rows, :] = row_sum / weight_sum
        flow_ref[1, rows, :] = col_sum / weight_sum


def section_flow(current, following, offsets, tile_rows=64):
    row_count, col_count = current.shape
    node_rows, node_cols = row_count // 4, col_count // 4
    window = tile_rows + 8
    padded = jnp.pad(following, ((4 - RAD, (node_rows + 8) * 4 - following.shape[0] - (4 - RAD)), (0, 0)))
    offset_count = offsets.shape[0]
    grid_spec = pltpu.PrefetchScalarGridSpec(
        num_scalar_prefetch=1,
        grid=(node_rows // tile_rows,),
        in_specs=[
            pl.BlockSpec((tile_rows * 4, col_count), lambda g, off: (g, 0)),
            pl.BlockSpec(padded.shape, lambda g, off: (0, 0)),
            pl.BlockSpec((512, 512), lambda g, off: (0, 0)),
        ],
        out_specs=pl.BlockSpec((2, tile_rows, node_cols), lambda g, off: (0, g, 0)),
        scratch_shapes=[
            pltpu.VMEM((16, tile_rows, node_cols), jnp.float32),
            pltpu.VMEM((16, window, node_cols), jnp.float32),
            pltpu.VMEM((col_count // 128, window * 4, 128), jnp.float32),
            pltpu.VMEM((144, tile_rows, node_cols), jnp.float32),
            pltpu.VMEM((offset_count, tile_rows, node_cols), jnp.float32),
        ],
    )
    return pl.pallas_call(
        flow_kernel,
        grid_spec=grid_spec,
        out_shape=jax.ShapeDtypeStruct((2, node_rows, node_cols), jnp.float32),
        compiler_params=pltpu.CompilerParams(
            dimension_semantics=("arbitrary",), vmem_limit_bytes=48 * 1024 * 1024
        ),
    )(offsets, current, padded, lane_permutation())


def advance(
    positions,
    from_below,
    from_above,
    from_right,
    from_left,
    row_weight,
    weight_up,
    col_weight,
    weight_left,
    pull_term,
    pull_prior,
    diagonal,
):
    force = row_weight * (from_below - positions) + weight_up * (from_above - positions)
    force = force + col_weight * (from_right - positions) + weight_left * (from_left - positions)
    force = force + pull_term - pull_prior
    return positions + relax_rate * force / (1.0 + diagonal)


def tiles_with_halo(fields, halo):
    count = lax.axis_size("sec")
    fields = extended(fields, (("strip", 1),), halo)
    width = fields.shape[2] // count
    columns = jnp.pad(fields, ((0, 0), (0, 0), (halo, halo)))
    windows = jnp.stack([columns[:, :, j * width : (j + 1) * width + 2 * halo] for j in range(count)], axis=1)
    shape = windows.shape
    flat = windows.reshape(shape[0], shape[1], shape[2] * shape[3])
    return lax.all_to_all(flat, "sec", split_axis=1, concat_axis=1, tiled=True).reshape(shape)


def shards(images, offsets, springs, validity):
    pixels = images[0]
    half = pixels.shape[0] // 2
    sec_count = lax.axis_size("sec")
    strip_count = lax.axis_size("strip")
    successor_top = shifted_2(pixels[: half + RAD], "sec", -1)
    prior_bottom = shifted_2(pixels[half:], "sec", 1)
    corner = lax.ppermute(
        pixels[-RAD:],
        ("sec", "strip"),
        [((s + 1) * strip_count + p - 1, s * strip_count + p) for s in range(sec_count - 1) for p in range(1, strip_count)],
    )
    below = shifted_2(pixels[:RAD], "strip", -1)
    keep_mask = (lax.axis_index("sec") < sec_count - 1).astype(jnp.float32)
    springs, validity, below = lax.optimization_barrier((springs, validity, below))
    match_weight = validity[0].astype(jnp.float32) * keep_mask
    node_rows, node_cols = (springs.shape[2], springs.shape[3])
    global_rows = lax.axis_index("strip") * node_rows + jnp.arange(node_rows, dtype=jnp.int32)
    row_keep = (global_rows < node_rows * lax.axis_size("strip") - 1).astype(jnp.float32)
    col_keep = (jnp.arange(node_cols) < node_cols - 1).astype(jnp.float32)
    row_weight = 0.25 * springs[0, 0].astype(jnp.float32) * row_keep[:, None]
    col_weight = 0.25 * springs[1, 0].astype(jnp.float32) * col_keep[None, :]
    halo = ITERS
    weights = jnp.stack([row_weight, col_weight, match_weight]).astype(jnp.bfloat16)
    weights = tiles_with_halo(weights, halo)
    weights, successor_top, prior_bottom = lax.optimization_barrier((weights, successor_top, prior_bottom))
    weights = weights.astype(jnp.float32)
    flow_top = section_flow(pixels[:half], jnp.concatenate([corner, successor_top]), offsets) * keep_mask
    flow_bottom = section_flow(prior_bottom, jnp.concatenate([pixels[half - RAD :], below]), offsets)
    flow_field = jnp.concatenate([flow_top, flow_bottom], axis=1)
    tiled = tiles_with_halo(flow_field, halo)
    node_half = flow_field.shape[1] // 2
    following = jnp.concatenate([tiled[:, 1:], jnp.zeros_like(tiled[:, :1])], axis=1)
    row_ids = jnp.arange(tiled.shape[2], dtype=jnp.int32)[:, None]
    from_prior = (row_ids < halo) | ((row_ids >= halo + node_half) & (row_ids < halo + 2 * node_half))
    flow_tiles = jnp.where(from_prior, following, tiled)
    tile_row = weights[0]
    tile_col = weights[1]
    tile_match = weights[2]
    weight_up = jnp.pad(tile_row, ((0, 0), (1, 0), (0, 0)))[:, :-1, :]
    weight_left = jnp.pad(tile_col, ((0, 0), (0, 0), (1, 0)))[:, :, :-1]
    match_prior = jnp.pad(tile_match, ((1, 0), (0, 0), (0, 0)))[:-1]
    diagonal = tile_row + weight_up + tile_col + weight_left + tile_match + match_prior
    positions = jnp.zeros_like(flow_tiles)
    for iteration in range(ITERS):
        padded = jnp.pad(positions, ((0, 0), (0, 0), (1, 1), (1, 1)))
        following = jnp.pad(positions, ((0, 0), (0, 1), (0, 0), (0, 0)))[:, 1:]
        pull_term = tile_match * (following - positions - flow_tiles)
        pull_prior = jnp.pad(pull_term, ((0, 0), (1, 0), (0, 0), (0, 0)))[:, :-1]
        positions = advance(
            positions,
            padded[:, :, 2:, 1:-1],
            padded[:, :, :-2, 1:-1],
            padded[:, :, 1:-1, 2:],
            padded[:, :, 1:-1, :-2],
            tile_row,
            weight_up,
            tile_col,
            weight_left,
            pull_term,
            pull_prior,
            diagonal,
        )
    core = positions[:, :, halo:-halo, halo:-halo]
    shape = core.shape
    flat = core.reshape(shape[0], shape[1], shape[2] * shape[3])
    returned = lax.all_to_all(flat, "sec", split_axis=1, concat_axis=1, tiled=True).reshape(shape)
    return jnp.transpose(returned, (0, 2, 1, 3)).reshape(shape[0], 1, shape[2], shape[1] * shape[3])


def solution(mesh):
    in_specs = (
        P("sec", "strip", None),
        P(),
        P(None, "sec", "strip", None),
        P("sec", "strip", None),
    )
    out_specs = P(None, "sec", "strip", None)
    return jax.shard_map(shards, mesh=mesh, in_specs=in_specs, out_specs=out_specs, check_vma=False)
```

```python
import jax
import jax.numpy as jnp
from jax import lax
from jax.experimental import pallas as pl
from jax.experimental.pallas import tpu as pltpu
from jax.sharding import PartitionSpec as P

RAD = 3
ITERS = 8


sharpness = 0.5
relax_rate = 0.8


def shifted_2(shard, axis, by):
    size = lax.axis_size(axis)
    pairs = [(i, i + by) for i in range(size) if 0 <= i + by < size]
    return lax.ppermute(shard, axis, pairs)


def extended(cells, sides, width):
    for axis, dim in sides:
        count = lax.axis_size(axis)
        ends = count - 1
        head = lax.slice_in_dim(cells, 0, width, axis=dim)
        tail = lax.slice_in_dim(cells, cells.shape[dim] - width, cells.shape[dim], axis=dim)
        cells = jnp.concatenate(
            [
                lax.ppermute(tail, axis, [(i, (i + 1) % count) for i in range(ends)]),
                cells,
                lax.ppermute(head, axis, [((i + 1) % count, i) for i in range(ends)]),
            ],
            axis=dim,
        )
    return cells


def lane_permutation():
    source = jnp.arange(512, dtype=jnp.int32)[:, None]
    target = jnp.arange(512, dtype=jnp.int32)[None, :]
    return ((source % 4) * 128 + source // 4 == target).astype(jnp.bfloat16)


def split_phases(pixels, permute, lanes_ref, phase_ref, node_rows):
    chunks = pixels.shape[1] // 512
    for c in range(chunks):
        permuted = jnp.dot(pixels[:, c * 512 : (c + 1) * 512], permute, preferred_element_type=jnp.float32)
        for t in range(4):
            lanes_ref[c * 4 + t, 0 : pixels.shape[0], :] = permuted[:, t * 128 : (t + 1) * 128]
    for q in range(4):
        for t in range(4):
            parts = [lanes_ref[pl.ds(c * 4 + t, 1), pl.ds(q, node_rows, stride=4), :][0] for c in range(chunks)]
            phase_ref[q * 4 + t] = jnp.concatenate(parts, axis=1)


def flow_kernel(
    offsets_ref, current_ref, following_ref, permute_ref, flow_ref, current_ph, following_ph, lanes_ref, shifted_ref, scores_ref
):
    tile_rows = current_ph.shape[1]
    node_cols = current_ph.shape[2]
    window = following_ph.shape[1]
    base = pl.multiple_of(pl.program_id(0) * tile_rows * 4, 32)
    permute = permute_ref[...]
    split_phases(current_ref[...], permute, lanes_ref, current_ph, tile_rows)
    split_phases(following_ref[pl.ds(base, window * 4), :], permute, lanes_ref, following_ph, window)
    column = lax.broadcasted_iota(jnp.int32, (window, node_cols), 1)

    def reachable(shift, phase_of):
        if shift == 0:
            return phase_of != 0
        if shift == 2:
            return phase_of != 3
        return phase_of >= 0

    def build(phase, carry):
        row_phase = lax.shift_right_logical(phase, 2)
        col_phase = phase & 3
        for col_shift in range(3):

            @pl.when(reachable(col_shift, col_phase))
            def _():
                block = following_ph[phase]
                if col_shift == 1:
                    moved = block
                else:
                    moved = pltpu.roll(block, (1 - col_shift) % node_cols, 1)
                    inside = (column + col_shift - 1 >= 0) & (column + col_shift - 1 < node_cols)
                    moved = jnp.where(inside, moved, 0.0)
                for row_shift in range(3):

                    @pl.when(reachable(row_shift, row_phase))
                    def _():
                        rows = moved if row_shift == 0 else pltpu.roll(moved, window - row_shift, 0)
                        shifted_ref[(row_shift * 3 + col_shift) * 16 + phase] = rows[:tile_rows]

        return carry

    lax.fori_loop(0, 16, build, 0)
    chunks = tile_rows // 8
    offset_count = scores_ref.shape[0]

    def score(k, carry):
        row_off = offsets_ref[k, 0]
        col_off = offsets_ref[k, 1]
        sources = []
        for q in range(4):
            u = q + row_off + 4
            u_node, u_phase = lax.shift_right_logical(u, 2), u & 3
            for t in range(4):
                v = t + col_off + 4
                v_node, v_phase = lax.shift_right_logical(v, 2), v & 3
                sources.append((u_node * 3 + v_node) * 16 + u_phase * 4 + v_phase)
        for c in range(chunks):
            rows = pl.ds(c * 8, 8)
            acc = current_ph[0, rows, :] * shifted_ref[sources[0], rows, :]
            for p in range(1, 16):
                acc = acc + current_ph[p, rows, :] * shifted_ref[sources[p], rows, :]
            scores_ref[k, rows, :] = sharpness * acc
        return carry

    lax.fori_loop(0, offset_count, score, 0)
    for c in range(chunks):
        rows = pl.ds(c * 8, 8)
        highest = scores_ref[0, rows, :]
        for k in range(1, offset_count):
            highest = jnp.maximum(highest, scores_ref[k, rows, :])
        weight_sum = jnp.zeros_like(highest)
        row_sum = jnp.zeros_like(highest)
        col_sum = jnp.zeros_like(highest)
        for k in range(offset_count):
            weight = jnp.exp(scores_ref[k, rows, :] - highest)
            weight_sum = weight_sum + weight
            row_sum = row_sum + weight * offsets_ref[k, 0].astype(jnp.float32)
            col_sum = col_sum + weight * offsets_ref[k, 1].astype(jnp.float32)
        flow_ref[0, rows, :] = row_sum / weight_sum
        flow_ref[1, rows, :] = col_sum / weight_sum


def section_flow(current, following, offsets, tile_rows=64):
    row_count, col_count = current.shape
    node_rows, node_cols = row_count // 4, col_count // 4
    window = tile_rows + 8
    padded = jnp.pad(following, ((4 - RAD, (node_rows + 8) * 4 - following.shape[0] - (4 - RAD)), (0, 0)))
    offset_count = offsets.shape[0]
    grid_spec = pltpu.PrefetchScalarGridSpec(
        num_scalar_prefetch=1,
        grid=(node_rows // tile_rows,),
        in_specs=[
            pl.BlockSpec((tile_rows * 4, col_count), lambda g, off: (g, 0)),
            pl.BlockSpec(padded.shape, lambda g, off: (0, 0)),
            pl.BlockSpec((512, 512), lambda g, off: (0, 0)),
        ],
        out_specs=pl.BlockSpec((2, tile_rows, node_cols), lambda g, off: (0, g, 0)),
        scratch_shapes=[
            pltpu.VMEM((16, tile_rows, node_cols), jnp.float32),
            pltpu.VMEM((16, window, node_cols), jnp.float32),
            pltpu.VMEM((col_count // 128, window * 4, 128), jnp.float32),
            pltpu.VMEM((144, tile_rows, node_cols), jnp.float32),
            pltpu.VMEM((offset_count, tile_rows, node_cols), jnp.float32),
        ],
    )
    return pl.pallas_call(
        flow_kernel,
        grid_spec=grid_spec,
        out_shape=jax.ShapeDtypeStruct((2, node_rows, node_cols), jnp.float32),
        compiler_params=pltpu.CompilerParams(
            dimension_semantics=("arbitrary",), vmem_limit_bytes=48 * 1024 * 1024
        ),
    )(offsets, current, padded, lane_permutation())


def advance(
    positions,
    from_below,
    from_above,
    from_right,
    from_left,
    row_weight,
    weight_up,
    col_weight,
    weight_left,
    pull_term,
    pull_prior,
    diagonal,
):
    force = row_weight * (from_below - positions) + weight_up * (from_above - positions)
    force = force + col_weight * (from_right - positions) + weight_left * (from_left - positions)
    force = force + pull_term - pull_prior
    return positions + relax_rate * force / (1.0 + diagonal)


def tiles_with_halo(fields, halo):
    count = lax.axis_size("sec")
    fields = extended(fields, (("strip", 1),), halo)
    width = fields.shape[2] // count
    columns = jnp.pad(fields, ((0, 0), (0, 0), (halo, halo)))
    windows = jnp.stack([columns[:, :, j * width : (j + 1) * width + 2 * halo] for j in range(count)], axis=1)
    shape = windows.shape
    flat = windows.reshape(shape[0], shape[1], shape[2] * shape[3])
    return lax.all_to_all(flat, "sec", split_axis=1, concat_axis=1, tiled=True).reshape(shape)


def shards(images, offsets, springs, validity):
    pixels = images[0]
    half = pixels.shape[0] // 2
    sec_count = lax.axis_size("sec")
    strip_count = lax.axis_size("strip")
    successor_top = shifted_2(pixels[: half + RAD], "sec", -1)
    prior_bottom = shifted_2(pixels[half:], "sec", 1)
    corner = lax.ppermute(
        pixels[-RAD:],
        ("sec", "strip"),
        [((s + 1) * strip_count + p - 1, s * strip_count + p) for s in range(sec_count - 1) for p in range(1, strip_count)],
    )
    below = shifted_2(pixels[:RAD], "strip", -1)
    keep_mask = (lax.axis_index("sec") < sec_count - 1).astype(jnp.float32)
    springs, validity, below = lax.optimization_barrier((springs, validity, below))
    match_weight = validity[0].astype(jnp.float32) * keep_mask
    node_rows, node_cols = (springs.shape[2], springs.shape[3])
    global_rows = lax.axis_index("strip") * node_rows + jnp.arange(node_rows, dtype=jnp.int32)
    row_keep = (global_rows < node_rows * lax.axis_size("strip") - 1).astype(jnp.float32)
    col_keep = (jnp.arange(node_cols) < node_cols - 1).astype(jnp.float32)
    row_weight = 0.25 * springs[0, 0].astype(jnp.float32) * row_keep[:, None]
    col_weight = 0.25 * springs[1, 0].astype(jnp.float32) * col_keep[None, :]
    halo = ITERS
    weights = jnp.stack([row_weight, col_weight, match_weight]).astype(jnp.bfloat16)
    weights = tiles_with_halo(weights, halo)
    weights, successor_top, prior_bottom = lax.optimization_barrier((weights, successor_top, prior_bottom))
    weights = weights.astype(jnp.float32)
    flow_top = section_flow(pixels[:half], jnp.concatenate([corner, successor_top]), offsets) * keep_mask
    flow_bottom = section_flow(prior_bottom, jnp.concatenate([pixels[half - RAD :], below]), offsets)
    flow_field = jnp.concatenate([flow_top, flow_bottom], axis=1)
    tiled = tiles_with_halo(flow_field, halo)
    node_half = flow_field.shape[1] // 2
    following = jnp.concatenate([tiled[:, 1:], jnp.zeros_like(tiled[:, :1])], axis=1)
    row_ids = jnp.arange(tiled.shape[2], dtype=jnp.int32)[:, None]
    from_prior = (row_ids < halo) | ((row_ids >= halo + node_half) & (row_ids < halo + 2 * node_half))
    flow_tiles = jnp.where(from_prior, following, tiled)
    tile_row = weights[0]
    tile_col = weights[1]
    tile_match = weights[2]
    weight_up = jnp.pad(tile_row, ((0, 0), (1, 0), (0, 0)))[:, :-1, :]
    weight_left = jnp.pad(tile_col, ((0, 0), (0, 0), (1, 0)))[:, :, :-1]
    match_prior = jnp.pad(tile_match, ((1, 0), (0, 0), (0, 0)))[:-1]
    diagonal = tile_row + weight_up + tile_col + weight_left + tile_match + match_prior
    positions = jnp.zeros_like(flow_tiles)
    for iteration in range(ITERS):
        padded = jnp.pad(positions, ((0, 0), (0, 0), (1, 1), (1, 1)))
        following = jnp.pad(positions, ((0, 0), (0, 1), (0, 0), (0, 0)))[:, 1:]
        pull_term = tile_match * (following - positions - flow_tiles)
        pull_prior = jnp.pad(pull_term, ((0, 0), (1, 0), (0, 0), (0, 0)))[:, :-1]
        positions = advance(
            positions,
            padded[:, :, 2:, 1:-1],
            padded[:, :, :-2, 1:-1],
            padded[:, :, 1:-1, 2:],
            padded[:, :, 1:-1, :-2],
            tile_row,
            weight_up,
            tile_col,
            weight_left,
            pull_term,
            pull_prior,
            diagonal,
        )
    core = positions[:, :, halo:-halo, halo:-halo]
    shape = core.shape
    flat = core.reshape(shape[0], shape[1], shape[2] * shape[3])
    returned = lax.all_to_all(flat, "sec", split_axis=1, concat_axis=1, tiled=True).reshape(shape)
    return jnp.transpose(returned, (0, 2, 1, 3)).reshape(shape[0], 1, shape[2], shape[1] * shape[3])


def solution(mesh):
    in_specs = (
        P("sec", "strip", None),
        P(),
        P(None, "sec", "strip", None),
        P("sec", "strip", None),
    )
    out_specs = P(None, "sec", "strip", None)
    return jax.shard_map(shards, mesh=mesh, in_specs=in_specs, out_specs=out_specs, check_vma=False)
```

```python
import jax
import jax.numpy as jnp
from jax import lax
from jax.experimental import pallas as pl
from jax.experimental.pallas import tpu as pltpu
from jax.sharding import PartitionSpec as P

RAD = 3
ITERS = 8


sharpness = 0.5
relax_rate = 0.8


def shifted_2(shard, axis, by):
    size = lax.axis_size(axis)
    pairs = [(i, i + by) for i in range(size) if 0 <= i + by < size]
    return lax.ppermute(shard, axis, pairs)


def extended(cells, sides, width):
    for axis, dim in sides:
        count = lax.axis_size(axis)
        ends = count - 1
        head = lax.slice_in_dim(cells, 0, width, axis=dim)
        tail = lax.slice_in_dim(cells, cells.shape[dim] - width, cells.shape[dim], axis=dim)
        cells = jnp.concatenate(
            [
                lax.ppermute(tail, axis, [(i, (i + 1) % count) for i in range(ends)]),
                cells,
                lax.ppermute(head, axis, [((i + 1) % count, i) for i in range(ends)]),
            ],
            axis=dim,
        )
    return cells


def lane_permutation():
    source = jnp.arange(512, dtype=jnp.int32)[:, None]
    target = jnp.arange(512, dtype=jnp.int32)[None, :]
    return ((source % 4) * 128 + source // 4 == target).astype(jnp.bfloat16)


def split_phases(pixels, permute, lanes_ref, phase_ref, node_rows):
    chunks = pixels.shape[1] // 512
    for c in range(chunks):
        permuted = jnp.dot(pixels[:, c * 512 : (c + 1) * 512], permute, preferred_element_type=jnp.float32)
        for t in range(4):
            lanes_ref[c * 4 + t, 0 : pixels.shape[0], :] = permuted[:, t * 128 : (t + 1) * 128]
    for q in range(4):
        for t in range(4):
            parts = [lanes_ref[pl.ds(c * 4 + t, 1), pl.ds(q, node_rows, stride=4), :][0] for c in range(chunks)]
            phase_ref[q * 4 + t] = jnp.concatenate(parts, axis=1)


def flow_kernel(
    offsets_ref, current_ref, following_ref, permute_ref, flow_ref, current_ph, following_ph, lanes_ref, shifted_ref, scores_ref
):
    tile_rows = current_ph.shape[1]
    node_cols = current_ph.shape[2]
    window = following_ph.shape[1]
    base = pl.multiple_of(pl.program_id(0) * tile_rows * 4, 32)
    permute = permute_ref[...]
    split_phases(current_ref[...], permute, lanes_ref, current_ph, tile_rows)
    split_phases(following_ref[pl.ds(base, window * 4), :], permute, lanes_ref, following_ph, window)
    column = lax.broadcasted_iota(jnp.int32, (window, node_cols), 1)

    def build(phase, carry):
        block = following_ph[phase]
        for col_shift in range(3):
            if col_shift == 1:
                moved = block
            else:
                moved = pltpu.roll(block, (1 - col_shift) % node_cols, 1)
                inside = (column + col_shift - 1 >= 0) & (column + col_shift - 1 < node_cols)
                moved = jnp.where(inside, moved, 0.0)
            for row_shift in range(3):
                rows = moved if row_shift == 0 else pltpu.roll(moved, window - row_shift, 0)
                shifted_ref[(row_shift * 3 + col_shift) * 16 + phase] = rows[:tile_rows]
        return carry

    lax.fori_loop(0, 16, build, 0)
    chunks = tile_rows // 8
    offset_count = scores_ref.shape[0]

    def score(k, carry):
        row_off = offsets_ref[k, 0]
        col_off = offsets_ref[k, 1]
        sources = []
        for q in range(4):
            u = q + row_off + 4
            u_node, u_phase = lax.shift_right_logical(u, 2), u & 3
            for t in range(4):
                v = t + col_off + 4
                v_node, v_phase = lax.shift_right_logical(v, 2), v & 3
                sources.append((u_node * 3 + v_node) * 16 + u_phase * 4 + v_phase)
        for c in range(chunks):
            rows = pl.ds(c * 8, 8)
            acc = current_ph[0, rows, :] * shifted_ref[sources[0], rows, :]
            for p in range(1, 16):
                acc = acc + current_ph[p, rows, :] * shifted_ref[sources[p], rows, :]
            scores_ref[k, rows, :] = sharpness * acc
        return carry

    lax.fori_loop(0, offset_count, score, 0)
    for c in range(chunks):
        rows = pl.ds(c * 8, 8)
        highest = scores_ref[0, rows, :]
        for k in range(1, offset_count):
            highest = jnp.maximum(highest, scores_ref[k, rows, :])
        weight_sum = jnp.zeros_like(highest)
        row_sum = jnp.zeros_like(highest)
        col_sum = jnp.zeros_like(highest)
        for k in range(offset_count):
            weight = jnp.exp(scores_ref[k, rows, :] - highest)
            weight_sum = weight_sum + weight
            row_sum = row_sum + weight * offsets_ref[k, 0].astype(jnp.float32)
            col_sum = col_sum + weight * offsets_ref[k, 1].astype(jnp.float32)
        flow_ref[0, rows, :] = row_sum / weight_sum
        flow_ref[1, rows, :] = col_sum / weight_sum


def section_flow(current, following, offsets, tile_rows=64):
    row_count, col_count = current.shape
    node_rows, node_cols = row_count // 4, col_count // 4
    window = tile_rows + 8
    padded = jnp.pad(following, ((4 - RAD, (node_rows + 8) * 4 - following.shape[0] - (4 - RAD)), (0, 0)))
    offset_count = offsets.shape[0]
    grid_spec = pltpu.PrefetchScalarGridSpec(
        num_scalar_prefetch=1,
        grid=(node_rows // tile_rows,),
        in_specs=[
            pl.BlockSpec((tile_rows * 4, col_count), lambda g, off: (g, 0)),
            pl.BlockSpec(padded.shape, lambda g, off: (0, 0)),
            pl.BlockSpec((512, 512), lambda g, off: (0, 0)),
        ],
        out_specs=pl.BlockSpec((2, tile_rows, node_cols), lambda g, off: (0, g, 0)),
        scratch_shapes=[
            pltpu.VMEM((16, tile_rows, node_cols), jnp.float32),
            pltpu.VMEM((16, window, node_cols), jnp.float32),
            pltpu.VMEM((col_count // 128, window * 4, 128), jnp.float32),
            pltpu.VMEM((144, tile_rows, node_cols), jnp.float32),
            pltpu.VMEM((offset_count, tile_rows, node_cols), jnp.float32),
        ],
    )
    return pl.pallas_call(
        flow_kernel,
        grid_spec=grid_spec,
        out_shape=jax.ShapeDtypeStruct((2, node_rows, node_cols), jnp.float32),
        compiler_params=pltpu.CompilerParams(
            dimension_semantics=("arbitrary",), vmem_limit_bytes=48 * 1024 * 1024
        ),
    )(offsets, current, padded, lane_permutation())


def advance(
    positions,
    from_below,
    from_above,
    from_right,
    from_left,
    row_weight,
    weight_up,
    col_weight,
    weight_left,
    pull_term,
    pull_prior,
    diagonal,
):
    force = row_weight * (from_below - positions) + weight_up * (from_above - positions)
    force = force + col_weight * (from_right - positions) + weight_left * (from_left - positions)
    force = force + pull_term - pull_prior
    return positions + relax_rate * force / (1.0 + diagonal)


def tiles_with_halo(fields, halo):
    count = lax.axis_size("sec")
    fields = extended(fields, (("strip", 1),), halo)
    width = fields.shape[2] // count
    columns = jnp.pad(fields, ((0, 0), (0, 0), (halo, halo)))
    windows = jnp.stack([columns[:, :, j * width : (j + 1) * width + 2 * halo] for j in range(count)], axis=1)
    shape = windows.shape
    flat = windows.reshape(shape[0], shape[1], shape[2] * shape[3])
    return lax.all_to_all(flat, "sec", split_axis=1, concat_axis=1, tiled=True).reshape(shape)


def shards(images, offsets, springs, validity):
    pixels = images[0]
    half = pixels.shape[0] // 2
    sec_count = lax.axis_size("sec")
    strip_count = lax.axis_size("strip")
    successor_top = shifted_2(pixels[: half + RAD], "sec", -1)
    prior_bottom = shifted_2(pixels[half:], "sec", 1)
    corner = lax.ppermute(
        pixels[-RAD:],
        ("sec", "strip"),
        [((s + 1) * strip_count + p - 1, s * strip_count + p) for s in range(sec_count - 1) for p in range(1, strip_count)],
    )
    below = shifted_2(pixels[:RAD], "strip", -1)
    keep_mask = (lax.axis_index("sec") < sec_count - 1).astype(jnp.float32)
    springs, validity, below = lax.optimization_barrier((springs, validity, below))
    match_weight = validity[0].astype(jnp.float32) * keep_mask
    node_rows, node_cols = (springs.shape[2], springs.shape[3])
    global_rows = lax.axis_index("strip") * node_rows + jnp.arange(node_rows, dtype=jnp.int32)
    row_keep = (global_rows < node_rows * lax.axis_size("strip") - 1).astype(jnp.float32)
    col_keep = (jnp.arange(node_cols) < node_cols - 1).astype(jnp.float32)
    row_weight = 0.25 * springs[0, 0].astype(jnp.float32) * row_keep[:, None]
    col_weight = 0.25 * springs[1, 0].astype(jnp.float32) * col_keep[None, :]
    halo = ITERS
    weights = jnp.stack([row_weight, col_weight, match_weight]).astype(jnp.bfloat16)
    weights = tiles_with_halo(weights, halo)
    weights, successor_top, prior_bottom = lax.optimization_barrier((weights, successor_top, prior_bottom))
    weights = weights.astype(jnp.float32)
    flow_top = section_flow(pixels[:half], jnp.concatenate([corner, successor_top]), offsets) * keep_mask
    flow_bottom = section_flow(prior_bottom, jnp.concatenate([pixels[half - RAD :], below]), offsets)
    flow_field = jnp.concatenate([flow_top, flow_bottom], axis=1)
    node_half = flow_field.shape[1] // 2
    tile_row = weights[0]
    tile_col = weights[1]
    tile_match = weights[2]
    weight_up = jnp.pad(tile_row, ((0, 0), (1, 0), (0, 0)))[:, :-1, :]
    weight_left = jnp.pad(tile_col, ((0, 0), (0, 0), (1, 0)))[:, :, :-1]
    match_prior = jnp.pad(tile_match, ((1, 0), (0, 0), (0, 0)))[:-1]
    diagonal = tile_row + weight_up + tile_col + weight_left + tile_match + match_prior
    results = []
    for component in range(flow_field.shape[0]):
        tiled = tiles_with_halo(flow_field[component : component + 1], halo)
        following = jnp.concatenate([tiled[:, 1:], jnp.zeros_like(tiled[:, :1])], axis=1)
        row_ids = jnp.arange(tiled.shape[2], dtype=jnp.int32)[:, None]
        from_prior = (row_ids < halo) | ((row_ids >= halo + node_half) & (row_ids < halo + 2 * node_half))
        flow_tiles = jnp.where(from_prior, following, tiled)
        positions = jnp.zeros_like(flow_tiles)
        for iteration in range(ITERS):
            padded = jnp.pad(positions, ((0, 0), (0, 0), (1, 1), (1, 1)))
            following = jnp.pad(positions, ((0, 0), (0, 1), (0, 0), (0, 0)))[:, 1:]
            pull_term = tile_match * (following - positions - flow_tiles)
            pull_prior = jnp.pad(pull_term, ((0, 0), (1, 0), (0, 0), (0, 0)))[:, :-1]
            positions = advance(
                positions,
                padded[:, :, 2:, 1:-1],
                padded[:, :, :-2, 1:-1],
                padded[:, :, 1:-1, 2:],
                padded[:, :, 1:-1, :-2],
                tile_row,
                weight_up,
                tile_col,
                weight_left,
                pull_term,
                pull_prior,
                diagonal,
            )
        core = positions[:, :, halo:-halo, halo:-halo]
        shape = core.shape
        flat = core.reshape(shape[0], shape[1], shape[2] * shape[3])
        returned = lax.all_to_all(flat, "sec", split_axis=1, concat_axis=1, tiled=True).reshape(shape)
        results.append(jnp.transpose(returned, (0, 2, 1, 3)).reshape(shape[0], 1, shape[2], shape[1] * shape[3]))
    return jnp.concatenate(results)


def solution(mesh):
    in_specs = (
        P("sec", "strip", None),
        P(),
        P(None, "sec", "strip", None),
        P("sec", "strip", None),
    )
    out_specs = P(None, "sec", "strip", None)
    return jax.shard_map(shards, mesh=mesh, in_specs=in_specs, out_specs=out_specs, check_vma=False)
```

```python
import jax
import jax.numpy as jnp
from jax import lax
from jax.experimental import pallas as pl
from jax.experimental.pallas import tpu as pltpu
from jax.sharding import PartitionSpec as P

RAD = 3
ITERS = 8


sharpness = 0.5
relax_rate = 0.8


def shifted_2(shard, axis, by):
    size = lax.axis_size(axis)
    pairs = [(i, i + by) for i in range(size) if 0 <= i + by < size]
    return lax.ppermute(shard, axis, pairs)


def extended(cells, sides, width):
    for axis, dim in sides:
        count = lax.axis_size(axis)
        ends = count - 1
        head = lax.slice_in_dim(cells, 0, width, axis=dim)
        tail = lax.slice_in_dim(cells, cells.shape[dim] - width, cells.shape[dim], axis=dim)
        cells = jnp.concatenate(
            [
                lax.ppermute(tail, axis, [(i, (i + 1) % count) for i in range(ends)]),
                cells,
                lax.ppermute(head, axis, [((i + 1) % count, i) for i in range(ends)]),
            ],
            axis=dim,
        )
    return cells


def lane_permutation():
    source = jnp.arange(512, dtype=jnp.int32)[:, None]
    target = jnp.arange(512, dtype=jnp.int32)[None, :]
    return ((source % 4) * 128 + source // 4 == target).astype(jnp.bfloat16)


def split_phases(pixels, permute, lanes_ref, phase_ref, node_rows):
    chunks = pixels.shape[1] // 512
    for c in range(chunks):
        permuted = jnp.dot(pixels[:, c * 512 : (c + 1) * 512], permute, preferred_element_type=jnp.float32)
        for t in range(4):
            lanes_ref[c * 4 + t, 0 : pixels.shape[0], :] = permuted[:, t * 128 : (t + 1) * 128]
    for q in range(4):
        for t in range(4):
            parts = [lanes_ref[pl.ds(c * 4 + t, 1), pl.ds(q, node_rows, stride=4), :][0] for c in range(chunks)]
            phase_ref[q * 4 + t] = jnp.concatenate(parts, axis=1)


def flow_kernel(
    offsets_ref, current_ref, following_ref, permute_ref, flow_ref, current_ph, following_ph, lanes_ref, shifted_ref, scores_ref
):
    tile_rows = current_ph.shape[1]
    node_cols = current_ph.shape[2]
    window = following_ph.shape[1]
    base = pl.multiple_of(pl.program_id(0) * tile_rows * 4, 32)
    permute = permute_ref[...]
    split_phases(current_ref[...], permute, lanes_ref, current_ph, tile_rows)
    split_phases(following_ref[pl.ds(base, window * 4), :], permute, lanes_ref, following_ph, window)
    column = lax.broadcasted_iota(jnp.int32, (window, node_cols), 1)

    def build(phase, carry):
        block = following_ph[phase]
        for col_shift in range(3):
            if col_shift == 1:
                moved = block
            else:
                moved = pltpu.roll(block, (1 - col_shift) % node_cols, 1)
                inside = (column + col_shift - 1 >= 0) & (column + col_shift - 1 < node_cols)
                moved = jnp.where(inside, moved, 0.0)
            for row_shift in range(3):
                rows = moved if row_shift == 0 else pltpu.roll(moved, window - row_shift, 0)
                shifted_ref[(row_shift * 3 + col_shift) * 16 + phase] = rows[:tile_rows]
        return carry

    lax.fori_loop(0, 16, build, 0)
    chunks = tile_rows // 8
    offset_count = scores_ref.shape[0]

    def score(k, carry):
        row_off = offsets_ref[k, 0]
        col_off = offsets_ref[k, 1]
        sources = []
        for q in range(4):
            u = q + row_off + 4
            u_node, u_phase = lax.shift_right_logical(u, 2), u & 3
            for t in range(4):
                v = t + col_off + 4
                v_node, v_phase = lax.shift_right_logical(v, 2), v & 3
                sources.append((u_node * 3 + v_node) * 16 + u_phase * 4 + v_phase)
        for c in range(chunks):
            rows = pl.ds(c * 8, 8)
            acc = current_ph[0, rows, :] * shifted_ref[sources[0], rows, :]
            for p in range(1, 16):
                acc = acc + current_ph[p, rows, :] * shifted_ref[sources[p], rows, :]
            scores_ref[k, rows, :] = sharpness * acc
        return carry

    lax.fori_loop(0, offset_count, score, 0)
    for c in range(chunks):
        rows = pl.ds(c * 8, 8)
        highest = scores_ref[0, rows, :]
        for k in range(1, offset_count):
            highest = jnp.maximum(highest, scores_ref[k, rows, :])
        weight_sum = jnp.zeros_like(highest)
        row_sum = jnp.zeros_like(highest)
        col_sum = jnp.zeros_like(highest)
        for k in range(offset_count):
            weight = jnp.exp(scores_ref[k, rows, :] - highest)
            weight_sum = weight_sum + weight
            row_sum = row_sum + weight * offsets_ref[k, 0].astype(jnp.float32)
            col_sum = col_sum + weight * offsets_ref[k, 1].astype(jnp.float32)
        flow_ref[0, rows, :] = row_sum / weight_sum
        flow_ref[1, rows, :] = col_sum / weight_sum


def section_flow(current, following, offsets, tile_rows=64):
    row_count, col_count = current.shape
    node_rows, node_cols = row_count // 4, col_count // 4
    window = tile_rows + 8
    padded = jnp.pad(following, ((4 - RAD, (node_rows + 8) * 4 - following.shape[0] - (4 - RAD)), (0, 0)))
    offset_count = offsets.shape[0]
    grid_spec = pltpu.PrefetchScalarGridSpec(
        num_scalar_prefetch=1,
        grid=(node_rows // tile_rows,),
        in_specs=[
            pl.BlockSpec((tile_rows * 4, col_count), lambda g, off: (g, 0)),
            pl.BlockSpec(padded.shape, lambda g, off: (0, 0)),
            pl.BlockSpec((512, 512), lambda g, off: (0, 0)),
        ],
        out_specs=pl.BlockSpec((2, tile_rows, node_cols), lambda g, off: (0, g, 0)),
        scratch_shapes=[
            pltpu.VMEM((16, tile_rows, node_cols), jnp.float32),
            pltpu.VMEM((16, window, node_cols), jnp.float32),
            pltpu.VMEM((col_count // 128, window * 4, 128), jnp.float32),
            pltpu.VMEM((144, tile_rows, node_cols), jnp.float32),
            pltpu.VMEM((offset_count, tile_rows, node_cols), jnp.float32),
        ],
    )
    return pl.pallas_call(
        flow_kernel,
        grid_spec=grid_spec,
        out_shape=jax.ShapeDtypeStruct((2, node_rows, node_cols), jnp.float32),
        compiler_params=pltpu.CompilerParams(
            dimension_semantics=("arbitrary",), vmem_limit_bytes=48 * 1024 * 1024
        ),
    )(offsets, current, padded, lane_permutation())


def advance(
    positions,
    from_below,
    from_above,
    from_right,
    from_left,
    row_weight,
    weight_up,
    col_weight,
    weight_left,
    pull_term,
    pull_prior,
    diagonal,
):
    force = row_weight * (from_below - positions) + weight_up * (from_above - positions)
    force = force + col_weight * (from_right - positions) + weight_left * (from_left - positions)
    force = force + pull_term - pull_prior
    return positions + relax_rate * force / (1.0 + diagonal)


def tiles_with_halo(fields, halo):
    count = lax.axis_size("sec")
    fields = extended(fields, (("strip", 1),), halo)
    width = fields.shape[2] // count
    columns = jnp.pad(fields, ((0, 0), (0, 0), (halo, halo)))
    windows = jnp.stack([columns[:, :, j * width : (j + 1) * width + 2 * halo] for j in range(count)], axis=1)
    shape = windows.shape
    flat = windows.reshape(shape[0], shape[1], shape[2] * shape[3])
    return lax.all_to_all(flat, "sec", split_axis=1, concat_axis=1, tiled=True).reshape(shape)


def shards(images, offsets, springs, validity):
    pixels = images[0]
    half = pixels.shape[0] // 2
    sec_count = lax.axis_size("sec")
    strip_count = lax.axis_size("strip")
    successor_top = shifted_2(pixels[: half + RAD], "sec", -1)
    prior_bottom = shifted_2(pixels[half:], "sec", 1)
    corner = lax.ppermute(
        pixels[-RAD:],
        ("sec", "strip"),
        [((s + 1) * strip_count + p - 1, s * strip_count + p) for s in range(sec_count - 1) for p in range(1, strip_count)],
    )
    below = shifted_2(pixels[:RAD], "strip", -1)
    keep_mask = (lax.axis_index("sec") < sec_count - 1).astype(jnp.float32)
    springs, validity, below = lax.optimization_barrier((springs, validity, below))
    match_weight = validity[0].astype(jnp.float32) * keep_mask
    node_rows, node_cols = (springs.shape[2], springs.shape[3])
    global_rows = lax.axis_index("strip") * node_rows + jnp.arange(node_rows, dtype=jnp.int32)
    row_keep = (global_rows < node_rows * lax.axis_size("strip") - 1).astype(jnp.float32)
    col_keep = (jnp.arange(node_cols) < node_cols - 1).astype(jnp.float32)
    row_weight = 0.25 * springs[0, 0].astype(jnp.float32) * row_keep[:, None]
    col_weight = 0.25 * springs[1, 0].astype(jnp.float32) * col_keep[None, :]
    halo = ITERS
    weights = jnp.stack([row_weight, col_weight, match_weight]).astype(jnp.bfloat16)
    count = lax.axis_size("sec")
    weights = extended(weights, (("strip", 1),), halo)
    width = weights.shape[2] // count
    columns = jnp.pad(weights, ((0, 0), (0, 0), (halo, halo)))
    windows = jnp.stack([columns[:, :, j * width : (j + 1) * width + 2 * halo] for j in range(count)], axis=1)
    shape = windows.shape
    flat = windows.reshape(shape[0], shape[1], shape[2] * shape[3])
    flat = lax.all_to_all(flat, "sec", split_axis=1, concat_axis=1, tiled=True)
    flat, successor_top, prior_bottom = lax.optimization_barrier((flat, successor_top, prior_bottom))
    weights = flat.reshape(shape).astype(jnp.float32)
    flow_top = section_flow(pixels[:half], jnp.concatenate([corner, successor_top]), offsets) * keep_mask
    flow_bottom = section_flow(prior_bottom, jnp.concatenate([pixels[half - RAD :], below]), offsets)
    flow_field = jnp.concatenate([flow_top, flow_bottom], axis=1)
    tiled = tiles_with_halo(flow_field, halo)
    node_half = flow_field.shape[1] // 2
    following = jnp.concatenate([tiled[:, 1:], jnp.zeros_like(tiled[:, :1])], axis=1)
    row_ids = jnp.arange(tiled.shape[2], dtype=jnp.int32)[:, None]
    from_prior = (row_ids < halo) | ((row_ids >= halo + node_half) & (row_ids < halo + 2 * node_half))
    flow_tiles = jnp.where(from_prior, following, tiled)
    tile_row = weights[0]
    tile_col = weights[1]
    tile_match = weights[2]
    weight_up = jnp.pad(tile_row, ((0, 0), (1, 0), (0, 0)))[:, :-1, :]
    weight_left = jnp.pad(tile_col, ((0, 0), (0, 0), (1, 0)))[:, :, :-1]
    match_prior = jnp.pad(tile_match, ((1, 0), (0, 0), (0, 0)))[:-1]
    diagonal = tile_row + weight_up + tile_col + weight_left + tile_match + match_prior
    positions = jnp.zeros_like(flow_tiles)
    for iteration in range(ITERS):
        padded = jnp.pad(positions, ((0, 0), (0, 0), (1, 1), (1, 1)))
        following = jnp.pad(positions, ((0, 0), (0, 1), (0, 0), (0, 0)))[:, 1:]
        pull_term = tile_match * (following - positions - flow_tiles)
        pull_prior = jnp.pad(pull_term, ((0, 0), (1, 0), (0, 0), (0, 0)))[:, :-1]
        positions = advance(
            positions,
            padded[:, :, 2:, 1:-1],
            padded[:, :, :-2, 1:-1],
            padded[:, :, 1:-1, 2:],
            padded[:, :, 1:-1, :-2],
            tile_row,
            weight_up,
            tile_col,
            weight_left,
            pull_term,
            pull_prior,
            diagonal,
        )
    core = positions[:, :, halo:-halo, halo:-halo]
    shape = core.shape
    flat = core.reshape(shape[0], shape[1], shape[2] * shape[3])
    returned = lax.all_to_all(flat, "sec", split_axis=1, concat_axis=1, tiled=True).reshape(shape)
    return jnp.transpose(returned, (0, 2, 1, 3)).reshape(shape[0], 1, shape[2], shape[1] * shape[3])


def solution(mesh):
    in_specs = (
        P("sec", "strip", None),
        P(),
        P(None, "sec", "strip", None),
        P("sec", "strip", None),
    )
    out_specs = P(None, "sec", "strip", None)
    return jax.shard_map(shards, mesh=mesh, in_specs=in_specs, out_specs=out_specs, check_vma=False)
```

```python
import jax
import jax.numpy as jnp
import numpy as np
from jax import lax
from jax.experimental import pallas as pl
from jax.experimental.pallas import tpu as pltpu
from jax.sharding import PartitionSpec as P

RAD = 3
ITERS = 8


sharpness = 0.5
relax_rate = 0.8


def shifted_2(shard, axis, by):
    size = lax.axis_size(axis)
    pairs = [(i, i + by) for i in range(size) if 0 <= i + by < size]
    return lax.ppermute(shard, axis, pairs)


def extended(cells, sides, width):
    for axis, dim in sides:
        count = lax.axis_size(axis)
        ends = count - 1
        head = lax.slice_in_dim(cells, 0, width, axis=dim)
        tail = lax.slice_in_dim(cells, cells.shape[dim] - width, cells.shape[dim], axis=dim)
        cells = jnp.concatenate(
            [
                lax.ppermute(tail, axis, [(i, (i + 1) % count) for i in range(ends)]),
                cells,
                lax.ppermute(head, axis, [((i + 1) % count, i) for i in range(ends)]),
            ],
            axis=dim,
        )
    return cells


def lane_permutation():
    source = jnp.arange(512, dtype=jnp.int32)[:, None]
    target = jnp.arange(512, dtype=jnp.int32)[None, :]
    return ((source % 4) * 128 + source // 4 == target).astype(jnp.bfloat16)


def split_phases(pixels, permute, lanes_ref, phase_ref, node_rows):
    chunks = pixels.shape[1] // 512
    for c in range(chunks):
        permuted = jnp.dot(pixels[:, c * 512 : (c + 1) * 512], permute, preferred_element_type=jnp.float32)
        for t in range(4):
            lanes_ref[c * 4 + t, 0 : pixels.shape[0], :] = permuted[:, t * 128 : (t + 1) * 128]
    for q in range(4):
        for t in range(4):
            parts = [lanes_ref[pl.ds(c * 4 + t, 1), pl.ds(q, node_rows, stride=4), :][0] for c in range(chunks)]
            phase_ref[q * 4 + t] = jnp.concatenate(parts, axis=1)


def flow_kernel(
    offsets_ref, current_ref, following_ref, permute_ref, flow_ref, current_ph, following_ph, lanes_ref, shifted_ref, scores_ref
):
    tile_rows = current_ph.shape[1]
    node_cols = current_ph.shape[2]
    window = following_ph.shape[1]
    base = pl.multiple_of(pl.program_id(0) * tile_rows * 4, 32)
    permute = permute_ref[...]
    split_phases(current_ref[...], permute, lanes_ref, current_ph, tile_rows)
    split_phases(following_ref[pl.ds(base, window * 4), :], permute, lanes_ref, following_ph, window)
    column = lax.broadcasted_iota(jnp.int32, (window, node_cols), 1)

    def build(phase, carry):
        block = following_ph[phase]
        for col_shift in range(3):
            if col_shift == 1:
                moved = block
            else:
                moved = pltpu.roll(block, (1 - col_shift) % node_cols, 1)
                inside = (column + col_shift - 1 >= 0) & (column + col_shift - 1 < node_cols)
                moved = jnp.where(inside, moved, 0.0)
            for row_shift in range(3):
                rows = moved if row_shift == 0 else pltpu.roll(moved, window - row_shift, 0)
                shifted_ref[(row_shift * 3 + col_shift) * 16 + phase] = rows[:tile_rows]
        return carry

    lax.fori_loop(0, 16, build, 0)
    chunks = tile_rows // 8
    offset_count = scores_ref.shape[0]

    def score(k, carry):
        row_off = offsets_ref[k, 0]
        col_off = offsets_ref[k, 1]
        sources = []
        for q in range(4):
            u = q + row_off + 4
            u_node, u_phase = lax.shift_right_logical(u, 2), u & 3
            for t in range(4):
                v = t + col_off + 4
                v_node, v_phase = lax.shift_right_logical(v, 2), v & 3
                sources.append((u_node * 3 + v_node) * 16 + u_phase * 4 + v_phase)
        for c in range(chunks):
            rows = pl.ds(c * 8, 8)
            acc = current_ph[0, rows, :] * shifted_ref[sources[0], rows, :]
            for p in range(1, 16):
                acc = acc + current_ph[p, rows, :] * shifted_ref[sources[p], rows, :]
            scores_ref[k, rows, :] = sharpness * acc
        return carry

    lax.fori_loop(0, offset_count, score, 0)
    for c in range(chunks):
        rows = pl.ds(c * 8, 8)
        highest = scores_ref[0, rows, :]
        for k in range(1, offset_count):
            highest = jnp.maximum(highest, scores_ref[k, rows, :])
        weight_sum = jnp.zeros_like(highest)
        row_sum = jnp.zeros_like(highest)
        col_sum = jnp.zeros_like(highest)
        for k in range(offset_count):
            weight = jnp.exp(scores_ref[k, rows, :] - highest)
            weight_sum = weight_sum + weight
            row_sum = row_sum + weight * offsets_ref[k, 0].astype(jnp.float32)
            col_sum = col_sum + weight * offsets_ref[k, 1].astype(jnp.float32)
        flow_ref[0, rows, :] = row_sum / weight_sum
        flow_ref[1, rows, :] = col_sum / weight_sum


def section_flow(current, following, offsets, tile_rows=64):
    row_count, col_count = current.shape
    node_rows, node_cols = row_count // 4, col_count // 4
    window = tile_rows + 8
    padded = jnp.pad(following, ((4 - RAD, (node_rows + 8) * 4 - following.shape[0] - (4 - RAD)), (0, 0)))
    offset_count = offsets.shape[0]
    grid_spec = pltpu.PrefetchScalarGridSpec(
        num_scalar_prefetch=1,
        grid=(node_rows // tile_rows,),
        in_specs=[
            pl.BlockSpec((tile_rows * 4, col_count), lambda g, off: (g, 0)),
            pl.BlockSpec(padded.shape, lambda g, off: (0, 0)),
            pl.BlockSpec((512, 512), lambda g, off: (0, 0)),
        ],
        out_specs=pl.BlockSpec((2, tile_rows, node_cols), lambda g, off: (0, g, 0)),
        scratch_shapes=[
            pltpu.VMEM((16, tile_rows, node_cols), jnp.float32),
            pltpu.VMEM((16, window, node_cols), jnp.float32),
            pltpu.VMEM((col_count // 128, window * 4, 128), jnp.float32),
            pltpu.VMEM((144, tile_rows, node_cols), jnp.float32),
            pltpu.VMEM((offset_count, tile_rows, node_cols), jnp.float32),
        ],
    )
    return pl.pallas_call(
        flow_kernel,
        grid_spec=grid_spec,
        out_shape=jax.ShapeDtypeStruct((2, node_rows, node_cols), jnp.float32),
        compiler_params=pltpu.CompilerParams(
            dimension_semantics=("arbitrary",), vmem_limit_bytes=48 * 1024 * 1024
        ),
    )(offsets, current, padded, lane_permutation())


def advance(
    positions,
    from_below,
    from_above,
    from_right,
    from_left,
    row_weight,
    weight_up,
    col_weight,
    weight_left,
    pull_term,
    pull_prior,
    diagonal,
):
    force = row_weight * (from_below - positions) + weight_up * (from_above - positions)
    force = force + col_weight * (from_right - positions) + weight_left * (from_left - positions)
    force = force + pull_term - pull_prior
    return positions + relax_rate * force / (1.0 + diagonal)


def tiles_with_halo(fields, halo):
    count = lax.axis_size("sec")
    fields = extended(fields, (("strip", 1),), halo)
    width = fields.shape[2] // count
    columns = jnp.pad(fields, ((0, 0), (0, 0), (halo, halo)))
    index = np.arange(count)[:, None] * width + np.arange(width + 2 * halo)[None, :]
    windows = jnp.moveaxis(columns[:, :, index], 2, 1)
    shape = windows.shape
    flat = windows.reshape(shape[0], shape[1], shape[2] * shape[3])
    return lax.all_to_all(flat, "sec", split_axis=1, concat_axis=1, tiled=True).reshape(shape)


def shards(images, offsets, springs, validity):
    pixels = images[0]
    half = pixels.shape[0] // 2
    sec_count = lax.axis_size("sec")
    strip_count = lax.axis_size("strip")
    successor_top = shifted_2(pixels[: half + RAD], "sec", -1)
    prior_bottom = shifted_2(pixels[half:], "sec", 1)
    corner = lax.ppermute(
        pixels[-RAD:],
        ("sec", "strip"),
        [((s + 1) * strip_count + p - 1, s * strip_count + p) for s in range(sec_count - 1) for p in range(1, strip_count)],
    )
    below = shifted_2(pixels[:RAD], "strip", -1)
    keep_mask = (lax.axis_index("sec") < sec_count - 1).astype(jnp.float32)
    springs, validity, below = lax.optimization_barrier((springs, validity, below))
    match_weight = validity[0].astype(jnp.float32) * keep_mask
    node_rows, node_cols = (springs.shape[2], springs.shape[3])
    global_rows = lax.axis_index("strip") * node_rows + jnp.arange(node_rows, dtype=jnp.int32)
    row_keep = (global_rows < node_rows * lax.axis_size("strip") - 1).astype(jnp.float32)
    col_keep = (jnp.arange(node_cols) < node_cols - 1).astype(jnp.float32)
    row_weight = 0.25 * springs[0, 0].astype(jnp.float32) * row_keep[:, None]
    col_weight = 0.25 * springs[1, 0].astype(jnp.float32) * col_keep[None, :]
    halo = ITERS
    weights = jnp.stack([row_weight, col_weight, match_weight]).astype(jnp.bfloat16)
    count = lax.axis_size("sec")
    weights = extended(weights, (("strip", 1),), halo)
    width = weights.shape[2] // count
    columns = jnp.pad(weights, ((0, 0), (0, 0), (halo, halo)))
    windows = jnp.stack([columns[:, :, j * width : (j + 1) * width + 2 * halo] for j in range(count)], axis=1)
    shape = windows.shape
    flat = windows.reshape(shape[0], shape[1], shape[2] * shape[3])
    flat = lax.all_to_all(flat, "sec", split_axis=1, concat_axis=1, tiled=True)
    flat, successor_top, prior_bottom = lax.optimization_barrier((flat, successor_top, prior_bottom))
    weights = flat.reshape(shape).astype(jnp.float32)
    flow_top = section_flow(pixels[:half], jnp.concatenate([corner, successor_top]), offsets) * keep_mask
    flow_bottom = section_flow(prior_bottom, jnp.concatenate([pixels[half - RAD :], below]), offsets)
    flow_field = jnp.concatenate([flow_top, flow_bottom], axis=1)
    tiled = tiles_with_halo(flow_field, halo)
    node_half = flow_field.shape[1] // 2
    following = jnp.concatenate([tiled[:, 1:], jnp.zeros_like(tiled[:, :1])], axis=1)
    row_ids = jnp.arange(tiled.shape[2], dtype=jnp.int32)[:, None]
    from_prior = (row_ids < halo) | ((row_ids >= halo + node_half) & (row_ids < halo + 2 * node_half))
    flow_tiles = jnp.where(from_prior, following, tiled)
    tile_row = weights[0]
    tile_col = weights[1]
    tile_match = weights[2]
    weight_up = jnp.pad(tile_row, ((0, 0), (1, 0), (0, 0)))[:, :-1, :]
    weight_left = jnp.pad(tile_col, ((0, 0), (0, 0), (1, 0)))[:, :, :-1]
    match_prior = jnp.pad(tile_match, ((1, 0), (0, 0), (0, 0)))[:-1]
    diagonal = tile_row + weight_up + tile_col + weight_left + tile_match + match_prior
    positions = jnp.zeros_like(flow_tiles)
    for iteration in range(ITERS):
        padded = jnp.pad(positions, ((0, 0), (0, 0), (1, 1), (1, 1)))
        following = jnp.pad(positions, ((0, 0), (0, 1), (0, 0), (0, 0)))[:, 1:]
        pull_term = tile_match * (following - positions - flow_tiles)
        pull_prior = jnp.pad(pull_term, ((0, 0), (1, 0), (0, 0), (0, 0)))[:, :-1]
        positions = advance(
            positions,
            padded[:, :, 2:, 1:-1],
            padded[:, :, :-2, 1:-1],
            padded[:, :, 1:-1, 2:],
            padded[:, :, 1:-1, :-2],
            tile_row,
            weight_up,
            tile_col,
            weight_left,
            pull_term,
            pull_prior,
            diagonal,
        )
    core = positions[:, :, halo:-halo, halo:-halo]
    shape = core.shape
    flat = core.reshape(shape[0], shape[1], shape[2] * shape[3])
    returned = lax.all_to_all(flat, "sec", split_axis=1, concat_axis=1, tiled=True).reshape(shape)
    return jnp.transpose(returned, (0, 2, 1, 3)).reshape(shape[0], 1, shape[2], shape[1] * shape[3])


def solution(mesh):
    in_specs = (
        P("sec", "strip", None),
        P(),
        P(None, "sec", "strip", None),
        P("sec", "strip", None),
    )
    out_specs = P(None, "sec", "strip", None)
    return jax.shard_map(shards, mesh=mesh, in_specs=in_specs, out_specs=out_specs, check_vma=False)
```
